32 devices in a mesh: row: 4 (over z), col: 8 (over y, x, core).
Axes of the slice: x: 2, y: 2, z: 4, core: 2. Of those that a mesh axis runs over, the one named last changes fastest.
Arguments:
- layer_input: bfloat16 [8192, 2048], P(('col', 'row')), may hold values from -6 to 6
- w_query: bfloat16 [2048, 2048], P('col', 'row'), may hold values from -0.125 to 0.125
- w_key: bfloat16 [2048, 2048], P('col', 'row'), may hold values from -0.125 to 0.125
- w_value: bfloat16 [2048, 2048], P('col', 'row'), may hold values from -0.125 to 0.125
- w_output: bfloat16 [2048, 2048], P('row', 'col'), may hold values from -1.5 to 1.5
- w_gate: bfloat16 [2048, 8192], P('col', 'row'), may hold values from -0.125 to 0.125
- w_up: bfloat16 [2048, 8192], P('col', 'row'), may hold values from -0.125 to 0.125
- w_down: bfloat16 [8192, 2048], P('row', 'col'), may hold values from -0.0625 to 0.0625
- piece_starts: int32 [8, 2], P('col'), may hold values from 0 to 768, as said below
- cotangent: bfloat16 [8192, 2048], P(('col', 'row')), may hold values from -6 to 6
Outputs:
- output: bfloat16 [8192, 2048], P(('col', 'row'))
- input_grad: float32 [8192, 2048], P(('col', 'row'))
- grad_w_query: float32 [2048, 2048], P('col', 'row')
- grad_w_key: float32 [2048, 2048], P('col', 'row')
- grad_w_value: float32 [2048, 2048], P('col', 'row')
- grad_w_output: float32 [2048, 2048], P('row', 'col')
- grad_w_gate: float32 [2048, 8192], P('col', 'row')
- grad_w_up: float32 [2048, 8192], P('col', 'row')
- grad_w_down: float32 [8192, 2048], P('row', 'col')
The draws below stay inside these ranges and needn't reach their ends.
Inputs may be any that keep to these rules, and one draw needn't show every extreme that they name: `piece_starts`: piece p of a sequence starts at p * 512 or later and ends by (p + 1) * 512, so the pieces of one sequence do not intersect.
All inputs are finite; a program needn't handle non-finite values.
Results may differ from the reference program's by a relative error of at most 0.019.
Values may be sent and summed in bfloat16 or wider, within the bound.
No kernel may reach another device: no remote copies, remote signals or barrier semaphores. Data moves between devices by JAX's collectives and lax.ppermute only.
A program may use at most 256 MiB of HBM per device.

```python
import math
import jax
import jax.numpy as jnp
from jax import lax

D = 2048
HEADS = 16
HD = 128
FF = 8192
LENGTH = 1024
PIECE = 256
PIECES = 2
SEQS = 8
TOKENS = 8192


def draw_piece_starts(key, part):
    region = LENGTH // PIECES
    offsets = jax.random.randint(key, (SEQS, PIECES), 0, region - PIECE + 1, dtype=jnp.int32)
    offsets = offsets.at[0, 0].set(0)
    offsets = offsets.at[0, PIECES - 1].set(region - PIECE)
    bases = jnp.arange(PIECES, dtype=jnp.int32) * region
    return offsets + bases[None, :]


def block_levels(rng, dims, pieces, smallest, largest):
    gain = 1.0
    for position, shards_of in pieces:
        steps = jax.random.uniform(jax.random.fold_in(jax.random.fold_in(rng, 6), position), (shards_of,), jnp.float32, smallest / len(pieces), largest / len(pieces))
        gain = gain * jnp.repeat(jnp.exp(steps), dims[position] // shards_of).reshape((-1,) + (1,) * (len(dims) - 1 - position))
    return gain


def noise(stream_key, shape, width, bound, shards=(), kind=jnp.bfloat16):
    values = jax.random.normal(stream_key, shape, jnp.float32) * width
    if len(shards) > 0:
        values = block_levels(stream_key, shape, shards, -0.22, 0.18) * values
    return jnp.clip(values, min=-bound, max=bound).astype(kind)


def setup_inputs(seed: int = 0) -> dict:
    splits = jax.random.split(jax.random.key(seed), 11)
    layer_input = noise(splits[0], (TOKENS, D), 1.0, 6.0, ((0, 32),))
    w_query = noise(splits[1], (D, D), D ** -0.5, 0.125, ((0, 8), (1, 4)))
    w_key = noise(splits[2], (D, D), D ** -0.5, 0.125, ((0, 8), (1, 4)))
    w_value = noise(splits[3], (D, D), D ** -0.5, 0.125, ((0, 8), (1, 4)))
    w_output = noise(splits[4], (D, D), (D // 128) ** -0.5, 1.5, ((0, 4), (1, 8)))
    w_gate = noise(splits[5], (D, FF), D ** -0.5, 0.125, ((0, 8), (1, 4)))
    w_up = noise(splits[6], (D, FF), D ** -0.5, 0.125, ((0, 8), (1, 4)))
    w_down = noise(splits[7], (FF, D), FF ** -0.5, 0.0625, ((0, 4), (1, 8)))
    piece_starts = draw_piece_starts(jax.random.fold_in(splits[10], 71), 0)
    cotangent = noise(splits[9], (TOKENS, D), 1.0, 6.0, ((0, 32),))
    return dict(layer_input=layer_input, w_query=w_query, w_key=w_key, w_value=w_value, w_output=w_output, w_gate=w_gate, w_up=w_up, w_down=w_down, piece_starts=piece_starts, cotangent=cotangent)


@jax.custom_vjp
def low(v):
    return lax.optimization_barrier(v.astype(jnp.bfloat16)).astype(jnp.float32)

@jax.custom_vjp
def low_back(v):
    return v

def low_keep(v):
    return (low(v), None)

def low_pass(kept, grad):
    return (grad,)

def back_keep(v):
    return (v, None)

def back_low(kept, grad):
    return (low(grad),)
low.defvjp(low_keep, low_pass)
low_back.defvjp(back_keep, back_low)
EPSILON = 1e-05
NEGATIVE = -1e+30

def product(left, right):
    return jnp.dot(left, right, precision=lax.Precision.HIGHEST, preferred_element_type=jnp.float32)

def layer_norm(inputs):
    center = inputs - lax.optimization_barrier(jnp.mean(inputs, axis=-1, keepdims=True))
    spread = lax.optimization_barrier(jnp.mean(center * center, axis=-1, keepdims=True))
    return center * lax.rsqrt(spread + EPSILON)

def rope_tables():
    positions = jnp.arange(LENGTH, dtype=jnp.float32)
    freqs = jnp.power(jnp.float32(10000.0), -jnp.arange(HD // 2, dtype=jnp.float32) * (2.0 / HD))
    angles = positions[:, None] * freqs[None, :]
    return (jnp.cos(angles)[:, None, :], jnp.sin(angles)[:, None, :])

def rotate(field, cosine, sine):
    half_size = field.shape[-1] // 2
    first_half = field[..., :half_size]
    second_half = field[..., half_size:]
    return jnp.concatenate([first_half * cosine - second_half * sine, second_half * cosine + first_half * sine], axis=-1)

def piece_mask(starts):
    positions = jnp.arange(LENGTH, dtype=jnp.int32)
    inside = (positions[None, :] >= starts[:, None]) & (positions[None, :] < starts[:, None] + PIECE)
    shared = jnp.any(inside[:, :, None] & inside[:, None, :], axis=0)
    causal = positions[None, :] <= positions[:, None]
    return causal | shared

def attend(operands):
    queries, keys_rot, values, starts = operands
    scale = 1.0 / math.sqrt(HD)
    scores = jnp.einsum('qhd,khd->hqk', queries, keys_rot, precision=lax.Precision.HIGHEST) * scale
    scores = jnp.where(piece_mask(starts)[None], scores, NEGATIVE)
    scores = low_back(scores)
    probs = low(jax.nn.softmax(scores, axis=-1))
    mixed = jnp.einsum('hqk,khd->qhd', probs, values, precision=lax.Precision.HIGHEST)
    return low(low_back(mixed))

def forward(inputs, params, starts):
    w_query, w_key, w_value, w_output, w_gate, w_up, w_down = params
    seq_count = starts.shape[0]
    cosine, sine = rope_tables()
    normed_first = low(layer_norm(inputs))

    def split_heads(matrix):
        return matrix.reshape(seq_count, LENGTH, HEADS, HD)
    queries = low(rotate(split_heads(low_back(product(normed_first, w_query))), cosine, sine))
    keys_rot = low(rotate(split_heads(low_back(product(normed_first, w_key))), cosine, sine))
    values = low(split_heads(low_back(product(normed_first, w_value))))
    attended = lax.map(jax.checkpoint(attend), (queries, keys_rot, values, starts))
    attended = attended.reshape(inputs.shape[0], HEADS * HD)
    middle = inputs + low_back(product(attended, w_output))
    normed_second = low(layer_norm(middle))
    gate_lin = low_back(product(normed_second, w_gate))
    up_lin = low_back(product(normed_second, w_up))
    activation = low(jax.nn.silu(gate_lin) * up_lin)
    return middle + low_back(product(activation, w_down))

def reference(layer_input, w_query, w_key, w_value, w_output, w_gate, w_up, w_down, piece_starts, cotangent):
    params = tuple([matrix.astype(jnp.float32) for matrix in (w_query, w_key, w_value, w_output, w_gate, w_up, w_down)])
    group_seqs = 4 if SEQS % 4 == 0 else 1
    blocks = SEQS // group_seqs
    block_rows = group_seqs * LENGTH
    inputs = layer_input.astype(jnp.float32).reshape(blocks, block_rows, D)
    cot_blocks = cotangent.astype(jnp.float32).reshape(blocks, block_rows, D)
    start_blocks = piece_starts.reshape(blocks, group_seqs, PIECES)

    def one_block(totals, operands):
        block_input, block_starts, block_cot = operands

        def local_forward(values_in, weights):
            return forward(values_in, weights, block_starts)
        result, pullback = jax.vjp(local_forward, block_input, params)
        grad_input, grad_params = pullback(block_cot)
        totals = jax.tree.map(lambda total, grad: total + grad, totals, grad_params)
        return (totals, (result, grad_input))
    zeros = tuple([jnp.zeros_like(matrix) for matrix in params])
    totals, (results, grads_in) = lax.scan(one_block, zeros, (inputs, start_blocks, cot_blocks))
    return (results.reshape(TOKENS, D).astype(jnp.bfloat16), grads_in.reshape(TOKENS, D), totals[0], totals[1], totals[2], totals[3], totals[4], totals[5], totals[6])
```

```python
import math

import jax
import jax.numpy as jnp
from jax import lax
from jax.sharding import PartitionSpec as P

HD = 128
LENGTH = 1024
PIECE = 256


EPSILON = 1e-05
NEGATIVE = -1e30


def product(left, right):
    return jnp.dot(left, right, preferred_element_type=jnp.float32)


def contract_rows(left, right):
    return lax.dot_general(
        left, right, (((0,), (0,)), ((), ())), preferred_element_type=jnp.float32
    )


def times_transpose(left, right):
    return lax.dot_general(
        left, right, (((1,), (1,)), ((), ())), preferred_element_type=jnp.float32
    )


def line_all_gather(shard, axis):
    n = lax.psum(1, axis)
    if n == 1:
        return shard
    me = lax.axis_index(axis)
    rows = shard.shape[0]
    buf = jnp.zeros(((3 * n - 2) * rows,) + shard.shape[1:], shard.dtype)
    buf = lax.dynamic_update_slice_in_dim(buf, shard, (me + n - 1) * rows, 0)
    from_left = shard
    from_right = shard
    for step in range(1, n):
        right_pairs = [(j, j + 1) for j in range(step - 1, n - 1)]
        left_pairs = [(j, j - 1) for j in range(1, n - step + 1)]
        from_left = lax.ppermute(from_left, axis, right_pairs)
        from_right = lax.ppermute(from_right, axis, left_pairs)
        buf = lax.dynamic_update_slice_in_dim(buf, from_left, (me - step + n - 1) * rows, 0)
        buf = lax.dynamic_update_slice_in_dim(buf, from_right, (me + step + n - 1) * rows, 0)
    return buf[(n - 1) * rows : (2 * n - 1) * rows]


def line_reduce_scatter(partial, axis, send_dtype):
    n = lax.psum(1, axis)
    if n == 1:
        return partial
    me = lax.axis_index(axis)
    rows = partial.shape[0] // n

    def block(k):
        return lax.dynamic_slice_in_dim(partial, jnp.clip(k, 0, n - 1) * rows, rows, 0)

    recv_right = None
    recv_left = None
    for step in range(1, n):
        send_right = block(n - step + me)
        send_left = block(me + step - n)
        if recv_right is not None:
            send_right = send_right + recv_right
            send_left = send_left + recv_left
        recv_right = lax.ppermute(
            send_right.astype(send_dtype), axis, [(j, j + 1) for j in range(0, step)]
        ).astype(jnp.float32)
        recv_left = lax.ppermute(
            send_left.astype(send_dtype), axis, [(j, j - 1) for j in range(n - step, n)]
        ).astype(jnp.float32)
    return block(me) + recv_right + recv_left


def layer_norm(inputs):
    center = inputs - jnp.mean(inputs, axis=-1, keepdims=True)
    spread = jnp.mean(center * center, axis=-1, keepdims=True)
    return center * lax.rsqrt(spread + EPSILON)


def norm_back(inputs, grad):
    center = inputs - jnp.mean(inputs, axis=-1, keepdims=True)
    inverse = lax.rsqrt(jnp.mean(center * center, axis=-1, keepdims=True) + EPSILON)
    normed = center * inverse
    return inverse * (
        grad
        - jnp.mean(grad, axis=-1, keepdims=True)
        - normed * jnp.mean(grad * normed, axis=-1, keepdims=True)
    )


def rope_tables():
    positions = jnp.arange(LENGTH, dtype=jnp.float32)
    freqs = jnp.power(jnp.float32(10000.0), -jnp.arange(HD // 2, dtype=jnp.float32) * (2.0 / HD))
    angles = positions[:, None] * freqs[None, :]
    return (jnp.cos(angles)[:, None, :], jnp.sin(angles)[:, None, :])


def rotate(field, cosine, sine):
    half_size = field.shape[-1] // 2
    first_half = field[..., :half_size]
    second_half = field[..., half_size:]
    return jnp.concatenate(
        [first_half * cosine - second_half * sine, second_half * cosine + first_half * sine],
        axis=-1,
    )


def unrotate(field, cosine, sine):
    half_size = field.shape[-1] // 2
    first_half = field[..., :half_size]
    second_half = field[..., half_size:]
    return jnp.concatenate(
        [first_half * cosine + second_half * sine, second_half * cosine - first_half * sine],
        axis=-1,
    )


def piece_mask(starts):
    positions = jnp.arange(LENGTH, dtype=jnp.int32)
    inside = (positions[None, :] >= starts[:, None]) & (
        positions[None, :] < starts[:, None] + PIECE
    )
    shared = jnp.any(inside[:, :, None] & inside[:, None, :], axis=0)
    causal = positions[None, :] <= positions[:, None]
    return causal | shared


def masked_scores(queries, keys_rot, starts):
    scale = 1.0 / math.sqrt(HD)
    scores = (
        jnp.einsum("qhd,khd->hqk", queries, keys_rot, preferred_element_type=jnp.float32) * scale
    )
    return jnp.where(piece_mask(starts)[None], scores, NEGATIVE)


def attend_forward(operands):
    queries, keys_rot, values, starts = operands
    scores = masked_scores(queries, keys_rot, starts)
    row_top = jnp.max(scores, axis=-1, keepdims=True)
    shifted = jnp.exp(scores - row_top)
    row_total = jnp.sum(shifted, axis=-1, keepdims=True)
    probs = (shifted / row_total).astype(jnp.bfloat16)
    mixed = jnp.einsum("hqk,khd->qhd", probs, values, preferred_element_type=jnp.float32)
    return (mixed, row_top + jnp.log(row_total))


def attend_backward(operands):
    queries, keys_rot, values, starts, log_total, grad_mixed = operands
    scale = 1.0 / math.sqrt(HD)
    scores = masked_scores(queries, keys_rot, starts)
    probs = jnp.exp(scores - log_total)
    probs_low = probs.astype(jnp.bfloat16)
    grad_values = jnp.einsum(
        "hqk,qhd->khd", probs_low, grad_mixed, preferred_element_type=jnp.float32
    )
    grad_probs = jnp.einsum("qhd,khd->hqk", grad_mixed, values, preferred_element_type=jnp.float32)
    inner = jnp.sum(probs * grad_probs, axis=-1, keepdims=True)
    grad_scores = (probs * (grad_probs - inner)).astype(jnp.bfloat16)
    grad_queries = (
        jnp.einsum("hqk,khd->qhd", grad_scores, keys_rot, preferred_element_type=jnp.float32)
        * scale
    )
    grad_keys = (
        jnp.einsum("hqk,qhd->khd", grad_scores, queries, preferred_element_type=jnp.float32) * scale
    )
    return (grad_queries, grad_keys, grad_values)


def per_device(
    layer_input, w_query, w_key, w_value, w_output, w_gate, w_up, w_down, piece_starts, cotangent
):
    seq_count = piece_starts.shape[0]
    group_rows = seq_count * LENGTH
    heads_local = w_query.shape[1] // HD
    gathered = (
        lax.all_gather(w_query, "col", axis=0, tiled=True),
        lax.all_gather(w_key, "col", axis=0, tiled=True),
        lax.all_gather(w_value, "col", axis=0, tiled=True),
        lax.all_gather(w_output, "col", axis=1, tiled=True),
        lax.all_gather(w_gate, "col", axis=0, tiled=True),
        lax.all_gather(w_up, "col", axis=0, tiled=True),
        lax.all_gather(w_down, "col", axis=1, tiled=True),
    )
    full_query, full_key, full_value, full_output, full_gate, full_up, full_down = gathered
    cosine, sine = rope_tables()
    inputs = layer_input.astype(jnp.float32)
    normed_first = layer_norm(inputs).astype(jnp.bfloat16)
    first_rows = line_all_gather(normed_first, "row")

    def split_heads(matrix):
        return matrix.reshape(seq_count, LENGTH, heads_local, HD)

    def merge_heads(field):
        return field.reshape(group_rows, heads_local * HD)

    queries = rotate(split_heads(product(first_rows, full_query)), cosine, sine).astype(
        jnp.bfloat16
    )
    keys_rot = rotate(split_heads(product(first_rows, full_key)), cosine, sine).astype(jnp.bfloat16)
    values = split_heads(product(first_rows, full_value)).astype(jnp.bfloat16)
    mixed, log_total = lax.map(attend_forward, (queries, keys_rot, values, piece_starts))
    attended = merge_heads(mixed.astype(jnp.bfloat16))
    attention_sum = line_reduce_scatter(product(attended, full_output), "row", jnp.float32)
    middle = inputs + attention_sum
    normed_second = layer_norm(middle).astype(jnp.bfloat16)
    second_rows = line_all_gather(normed_second, "row")
    gate_lin = product(second_rows, full_gate)
    up_lin = product(second_rows, full_up)
    activation = (jax.nn.silu(gate_lin) * up_lin).astype(jnp.bfloat16)
    ffn_sum = line_reduce_scatter(product(activation, full_down), "row", jnp.bfloat16)
    output = (middle + ffn_sum).astype(jnp.bfloat16)
    back_query, back_key, back_value, back_output = (full_query, full_key, full_value, full_output)
    back_gate, back_up, back_down = (full_gate, full_up, full_down)
    grad_rows = line_all_gather(cotangent, "row")
    grad_activation = times_transpose(grad_rows, back_down)
    sigma = jax.nn.sigmoid(gate_lin)
    grad_gate = (grad_activation * up_lin * sigma * (1.0 + gate_lin * (1.0 - sigma))).astype(
        jnp.bfloat16
    )
    grad_up = (grad_activation * gate_lin * sigma).astype(jnp.bfloat16)
    grad_second = line_reduce_scatter(
        times_transpose(grad_gate, back_gate) + times_transpose(grad_up, back_up),
        "row",
        jnp.bfloat16,
    )
    grad_middle = cotangent.astype(jnp.float32) + norm_back(middle, grad_second)
    grad_branch = line_all_gather(grad_middle.astype(jnp.bfloat16), "row")
    grad_mixed = split_heads(times_transpose(grad_branch, back_output).astype(jnp.bfloat16))
    grad_q_rot, grad_k_rot, grad_values = lax.map(
        attend_backward, (queries, keys_rot, values, piece_starts, log_total, grad_mixed)
    )
    grad_query = merge_heads(unrotate(grad_q_rot, cosine, sine)).astype(jnp.bfloat16)
    grad_key = merge_heads(unrotate(grad_k_rot, cosine, sine)).astype(jnp.bfloat16)
    grad_value = merge_heads(grad_values).astype(jnp.bfloat16)
    grad_first = line_reduce_scatter(
        times_transpose(grad_query, back_query)
        + times_transpose(grad_key, back_key)
        + times_transpose(grad_value, back_value),
        "row",
        jnp.bfloat16,
    )
    grad_input = grad_middle + norm_back(inputs, grad_first)
    grad_query_w = contract_rows(first_rows, grad_query)
    grad_key_w = contract_rows(first_rows, grad_key)
    grad_value_w = contract_rows(first_rows, grad_value)
    grad_output_w = contract_rows(attended, grad_branch)
    grad_gate_w = contract_rows(second_rows, grad_gate)
    grad_up_w = contract_rows(second_rows, grad_up)
    grad_down_w = contract_rows(activation, grad_rows)
    summed = (
        lax.psum_scatter(
            grad_query_w.astype(jnp.bfloat16), "col", scatter_dimension=0, tiled=True
        ).astype(jnp.float32),
        lax.psum_scatter(
            grad_key_w.astype(jnp.bfloat16), "col", scatter_dimension=0, tiled=True
        ).astype(jnp.float32),
        lax.psum_scatter(
            grad_value_w.astype(jnp.bfloat16), "col", scatter_dimension=0, tiled=True
        ).astype(jnp.float32),
        lax.psum_scatter(
            grad_output_w.astype(jnp.bfloat16), "col", scatter_dimension=1, tiled=True
        ).astype(jnp.float32),
        lax.psum_scatter(
            grad_gate_w.astype(jnp.bfloat16), "col", scatter_dimension=0, tiled=True
        ).astype(jnp.float32),
        lax.psum_scatter(
            grad_up_w.astype(jnp.bfloat16), "col", scatter_dimension=0, tiled=True
        ).astype(jnp.float32),
        lax.psum_scatter(
            grad_down_w.astype(jnp.bfloat16), "col", scatter_dimension=1, tiled=True
        ).astype(jnp.float32),
    )
    results = tuple(summed)
    return (
        output,
        grad_input,
        results[0],
        results[1],
        results[2],
        results[3],
        results[4],
        results[5],
        results[6],
    )


def solution(mesh):
    in_specs = (
        P(("col", "row"), None),
        P("col", "row"),
        P("col", "row"),
        P("col", "row"),
        P("row", "col"),
        P("col", "row"),
        P("col", "row"),
        P("row", "col"),
        P("col", None),
        P(("col", "row"), None),
    )
    out_specs = (
        P(("col", "row"), None),
        P(("col", "row"), None),
        P("col", "row"),
        P("col", "row"),
        P("col", "row"),
        P("row", "col"),
        P("col", "row"),
        P("col", "row"),
        P("row", "col"),
    )
    return jax.shard_map(
        per_device, mesh=mesh, in_specs=in_specs, out_specs=out_specs, check_vma=False
    )
```

```python
import math

import jax
import jax.numpy as jnp
from jax import lax
from jax.sharding import Mesh, PartitionSpec as P

HD = 128
LENGTH = 1024
PIECE = 256


EPSILON = 1e-05
NEGATIVE = -1e30


def product(left, right):
    return jnp.dot(left, right, preferred_element_type=jnp.float32)


def contract_rows(left, right):
    return lax.dot_general(
        left, right, (((0,), (0,)), ((), ())), preferred_element_type=jnp.float32
    )


def times_transpose(left, right):
    return lax.dot_general(
        left, right, (((1,), (1,)), ((), ())), preferred_element_type=jnp.float32
    )


def line_all_gather(shard, axis):
    n = lax.psum(1, axis)
    if n == 1:
        return shard
    me = lax.axis_index(axis)
    rows = shard.shape[0]
    buf = jnp.zeros(((3 * n - 2) * rows,) + shard.shape[1:], shard.dtype)
    buf = lax.dynamic_update_slice_in_dim(buf, shard, (me + n - 1) * rows, 0)
    from_left = shard
    from_right = shard
    for step in range(1, n):
        right_pairs = [(j, j + 1) for j in range(step - 1, n - 1)]
        left_pairs = [(j, j - 1) for j in range(1, n - step + 1)]
        from_left = lax.ppermute(from_left, axis, right_pairs)
        from_right = lax.ppermute(from_right, axis, left_pairs)
        buf = lax.dynamic_update_slice_in_dim(buf, from_left, (me - step + n - 1) * rows, 0)
        buf = lax.dynamic_update_slice_in_dim(buf, from_right, (me + step + n - 1) * rows, 0)
    return buf[(n - 1) * rows : (2 * n - 1) * rows]


def line_reduce_scatter(partial, axis, send_dtype):
    n = lax.psum(1, axis)
    if n == 1:
        return partial
    me = lax.axis_index(axis)
    rows = partial.shape[0] // n

    def block(k):
        return lax.dynamic_slice_in_dim(partial, jnp.clip(k, 0, n - 1) * rows, rows, 0)

    recv_right = None
    recv_left = None
    for step in range(1, n):
        send_right = block(n - step + me)
        send_left = block(me + step - n)
        if recv_right is not None:
            send_right = send_right + recv_right
            send_left = send_left + recv_left
        recv_right = lax.ppermute(
            send_right.astype(send_dtype), axis, [(j, j + 1) for j in range(0, step)]
        ).astype(jnp.float32)
        recv_left = lax.ppermute(
            send_left.astype(send_dtype), axis, [(j, j - 1) for j in range(n - step, n)]
        ).astype(jnp.float32)
    return block(me) + recv_right + recv_left


COL = ("chip", "core")


def col_gather(block, axis):
    part = lax.all_gather(block, "chip", axis=axis, tiled=True)
    both = lax.all_gather(part, "core", axis=axis, tiled=False)
    shape = both.shape
    chips = lax.psum(1, "chip")
    size = block.shape[axis]
    split = shape[:axis] + (2, chips, size) + shape[axis + 2 :]
    order = list(range(len(split)))
    order[axis], order[axis + 1] = axis + 1, axis
    merged = shape[:axis] + (2 * chips * size,) + shape[axis + 2 :]
    return both.reshape(split).transpose(order).reshape(merged)


def col_scatter(partial, axis):
    chips = lax.psum(1, "chip")
    shape = partial.shape
    size = shape[axis] // (2 * chips)
    split = shape[:axis] + (chips, 2, size) + shape[axis + 1 :]
    order = list(range(len(split)))
    order[axis], order[axis + 1] = axis + 1, axis
    low_part = partial.reshape(split).transpose(order).reshape(shape).astype(jnp.bfloat16)
    half = lax.psum_scatter(low_part, "core", scatter_dimension=axis, tiled=True)
    return lax.psum_scatter(half, "chip", scatter_dimension=axis, tiled=True).astype(jnp.float32)


def layer_norm(inputs):
    center = inputs - jnp.mean(inputs, axis=-1, keepdims=True)
    spread = jnp.mean(center * center, axis=-1, keepdims=True)
    return center * lax.rsqrt(spread + EPSILON)


def norm_back(inputs, grad):
    center = inputs - jnp.mean(inputs, axis=-1, keepdims=True)
    inverse = lax.rsqrt(jnp.mean(center * center, axis=-1, keepdims=True) + EPSILON)
    normed = center * inverse
    return inverse * (
        grad
        - jnp.mean(grad, axis=-1, keepdims=True)
        - normed * jnp.mean(grad * normed, axis=-1, keepdims=True)
    )


def rope_tables():
    positions = jnp.arange(LENGTH, dtype=jnp.float32)
    freqs = jnp.power(jnp.float32(10000.0), -jnp.arange(HD // 2, dtype=jnp.float32) * (2.0 / HD))
    angles = positions[:, None] * freqs[None, :]
    return (jnp.cos(angles)[:, None, :], jnp.sin(angles)[:, None, :])


def rotate(field, cosine, sine):
    half_size = field.shape[-1] // 2
    first_half = field[..., :half_size]
    second_half = field[..., half_size:]
    return jnp.concatenate(
        [first_half * cosine - second_half * sine, second_half * cosine + first_half * sine],
        axis=-1,
    )


def unrotate(field, cosine, sine):
    half_size = field.shape[-1] // 2
    first_half = field[..., :half_size]
    second_half = field[..., half_size:]
    return jnp.concatenate(
        [first_half * cosine + second_half * sine, second_half * cosine - first_half * sine],
        axis=-1,
    )


def piece_mask(starts):
    positions = jnp.arange(LENGTH, dtype=jnp.int32)
    inside = (positions[None, :] >= starts[:, None]) & (
        positions[None, :] < starts[:, None] + PIECE
    )
    shared = jnp.any(inside[:, :, None] & inside[:, None, :], axis=0)
    causal = positions[None, :] <= positions[:, None]
    return causal | shared


def masked_scores(queries, keys_rot, starts):
    scale = 1.0 / math.sqrt(HD)
    scores = (
        jnp.einsum("qhd,khd->hqk", queries, keys_rot, preferred_element_type=jnp.float32) * scale
    )
    return jnp.where(piece_mask(starts)[None], scores, NEGATIVE)


def attend_forward(operands):
    queries, keys_rot, values, starts = operands
    scores = masked_scores(queries, keys_rot, starts)
    row_top = jnp.max(scores, axis=-1, keepdims=True)
    shifted = jnp.exp(scores - row_top)
    row_total = jnp.sum(shifted, axis=-1, keepdims=True)
    probs = (shifted / row_total).astype(jnp.bfloat16)
    mixed = jnp.einsum("hqk,khd->qhd", probs, values, preferred_element_type=jnp.float32)
    return (mixed, row_top + jnp.log(row_total))


def attend_backward(operands):
    queries, keys_rot, values, starts, log_total, grad_mixed = operands
    scale = 1.0 / math.sqrt(HD)
    scores = masked_scores(queries, keys_rot, starts)
    probs = jnp.exp(scores - log_total)
    probs_low = probs.astype(jnp.bfloat16)
    grad_values = jnp.einsum(
        "hqk,qhd->khd", probs_low, grad_mixed, preferred_element_type=jnp.float32
    )
    grad_probs = jnp.einsum("qhd,khd->hqk", grad_mixed, values, preferred_element_type=jnp.float32)
    inner = jnp.sum(probs * grad_probs, axis=-1, keepdims=True)
    grad_scores = (probs * (grad_probs - inner)).astype(jnp.bfloat16)
    grad_queries = (
        jnp.einsum("hqk,khd->qhd", grad_scores, keys_rot, preferred_element_type=jnp.float32)
        * scale
    )
    grad_keys = (
        jnp.einsum("hqk,qhd->khd", grad_scores, queries, preferred_element_type=jnp.float32) * scale
    )
    return (grad_queries, grad_keys, grad_values)


def per_device(
    layer_input, w_query, w_key, w_value, w_output, w_gate, w_up, w_down, piece_starts, cotangent
):
    seq_count = piece_starts.shape[0]
    group_rows = seq_count * LENGTH
    heads_local = w_query.shape[1] // HD
    gathered = (
        col_gather(w_query, 0),
        col_gather(w_key, 0),
        col_gather(w_value, 0),
        col_gather(w_output, 1),
        col_gather(w_gate, 0),
        col_gather(w_up, 0),
        col_gather(w_down, 1),
    )
    full_query, full_key, full_value, full_output, full_gate, full_up, full_down = gathered
    cosine, sine = rope_tables()
    inputs = layer_input.astype(jnp.float32)
    normed_first = layer_norm(inputs).astype(jnp.bfloat16)
    first_rows = line_all_gather(normed_first, "row")

    def split_heads(matrix):
        return matrix.reshape(seq_count, LENGTH, heads_local, HD)

    def merge_heads(field):
        return field.reshape(group_rows, heads_local * HD)

    queries = rotate(split_heads(product(first_rows, full_query)), cosine, sine).astype(
        jnp.bfloat16
    )
    keys_rot = rotate(split_heads(product(first_rows, full_key)), cosine, sine).astype(jnp.bfloat16)
    values = split_heads(product(first_rows, full_value)).astype(jnp.bfloat16)
    mixed, log_total = lax.map(attend_forward, (queries, keys_rot, values, piece_starts))
    attended = merge_heads(mixed.astype(jnp.bfloat16))
    attention_sum = line_reduce_scatter(product(attended, full_output), "row", jnp.bfloat16)
    middle = inputs + attention_sum
    normed_second = layer_norm(middle).astype(jnp.bfloat16)
    second_rows = line_all_gather(normed_second, "row")
    gate_lin = product(second_rows, full_gate)
    up_lin = product(second_rows, full_up)
    activation = (jax.nn.silu(gate_lin) * up_lin).astype(jnp.bfloat16)
    ffn_sum = line_reduce_scatter(product(activation, full_down), "row", jnp.bfloat16)
    output = (middle + ffn_sum).astype(jnp.bfloat16)
    back_query, back_key, back_value, back_output = (full_query, full_key, full_value, full_output)
    back_gate, back_up, back_down = (full_gate, full_up, full_down)
    grad_rows = line_all_gather(cotangent, "row")
    grad_activation = times_transpose(grad_rows, back_down)
    sigma = jax.nn.sigmoid(gate_lin)
    grad_gate = (grad_activation * up_lin * sigma * (1.0 + gate_lin * (1.0 - sigma))).astype(
        jnp.bfloat16
    )
    grad_up = (grad_activation * gate_lin * sigma).astype(jnp.bfloat16)
    grad_second = line_reduce_scatter(
        times_transpose(grad_gate, back_gate) + times_transpose(grad_up, back_up),
        "row",
        jnp.bfloat16,
    )
    grad_middle = cotangent.astype(jnp.float32) + norm_back(middle, grad_second)
    grad_branch = line_all_gather(grad_middle.astype(jnp.bfloat16), "row")
    grad_mixed = split_heads(times_transpose(grad_branch, back_output).astype(jnp.bfloat16))
    grad_q_rot, grad_k_rot, grad_values = lax.map(
        attend_backward, (queries, keys_rot, values, piece_starts, log_total, grad_mixed)
    )
    grad_query = merge_heads(unrotate(grad_q_rot, cosine, sine)).astype(jnp.bfloat16)
    grad_key = merge_heads(unrotate(grad_k_rot, cosine, sine)).astype(jnp.bfloat16)
    grad_value = merge_heads(grad_values).astype(jnp.bfloat16)
    grad_first = line_reduce_scatter(
        times_transpose(grad_query, back_query)
        + times_transpose(grad_key, back_key)
        + times_transpose(grad_value, back_value),
        "row",
        jnp.bfloat16,
    )
    grad_input = grad_middle + norm_back(inputs, grad_first)
    grad_query_w = contract_rows(first_rows, grad_query)
    grad_key_w = contract_rows(first_rows, grad_key)
    grad_value_w = contract_rows(first_rows, grad_value)
    grad_output_w = contract_rows(attended, grad_branch)
    grad_gate_w = contract_rows(second_rows, grad_gate)
    grad_up_w = contract_rows(second_rows, grad_up)
    grad_down_w = contract_rows(activation, grad_rows)
    summed = (
        col_scatter(grad_query_w, 0),
        col_scatter(grad_key_w, 0),
        col_scatter(grad_value_w, 0),
        col_scatter(grad_output_w, 1),
        col_scatter(grad_gate_w, 0),
        col_scatter(grad_up_w, 0),
        col_scatter(grad_down_w, 1),
    )
    results = tuple(summed)
    return (
        output,
        grad_input,
        results[0],
        results[1],
        results[2],
        results[3],
        results[4],
        results[5],
        results[6],
    )


def solution(mesh):
    in_specs = (
        P(("chip", "core", "row"), None),
        P(COL, "row"),
        P(COL, "row"),
        P(COL, "row"),
        P("row", COL),
        P(COL, "row"),
        P(COL, "row"),
        P("row", COL),
        P(COL, None),
        P(("chip", "core", "row"), None),
    )
    out_specs = (
        P(("chip", "core", "row"), None),
        P(("chip", "core", "row"), None),
        P(COL, "row"),
        P(COL, "row"),
        P(COL, "row"),
        P("row", COL),
        P(COL, "row"),
        P(COL, "row"),
        P("row", COL),
    )
    devices = mesh.devices
    sub_mesh = Mesh(
        devices.reshape(devices.shape[0], devices.shape[1] // 2, 2), ("row", "chip", "core")
    )
    return jax.shard_map(
        per_device, mesh=sub_mesh, in_specs=in_specs, out_specs=out_specs, check_vma=False
    )
```

```python
import math

import jax
import jax.numpy as jnp
from jax import lax
from jax.sharding import Mesh, PartitionSpec as P


HD = 128
LENGTH = 1024
PIECE = 256


EPSILON = 1e-05
NEGATIVE = -1e30


def product(left, right):
    return jnp.dot(left, right, preferred_element_type=jnp.float32)


def contract_rows(left, right):
    return lax.dot_general(
        left, right, (((0,), (0,)), ((), ())), preferred_element_type=jnp.float32
    )


def times_transpose(left, right):
    return lax.dot_general(
        left, right, (((1,), (1,)), ((), ())), preferred_element_type=jnp.float32
    )


def line_all_gather(shard, axis):
    n = lax.psum(1, axis)
    if n == 1:
        return shard
    me = lax.axis_index(axis)
    rows = shard.shape[0]
    buf = jnp.zeros(((3 * n - 2) * rows,) + shard.shape[1:], shard.dtype)
    buf = lax.dynamic_update_slice_in_dim(buf, shard, (me + n - 1) * rows, 0)
    from_left = shard
    from_right = shard
    for step in range(1, n):
        right_pairs = [(j, j + 1) for j in range(step - 1, n - 1)]
        left_pairs = [(j, j - 1) for j in range(1, n - step + 1)]
        from_left = lax.ppermute(from_left, axis, right_pairs)
        from_right = lax.ppermute(from_right, axis, left_pairs)
        buf = lax.dynamic_update_slice_in_dim(buf, from_left, (me - step + n - 1) * rows, 0)
        buf = lax.dynamic_update_slice_in_dim(buf, from_right, (me + step + n - 1) * rows, 0)
    return buf[(n - 1) * rows : (2 * n - 1) * rows]


def line_reduce_scatter(partial, axis, send_dtype):
    n = lax.psum(1, axis)
    if n == 1:
        return partial
    me = lax.axis_index(axis)
    rows = partial.shape[0] // n

    def block(k):
        return lax.dynamic_slice_in_dim(partial, jnp.clip(k, 0, n - 1) * rows, rows, 0)

    recv_right = None
    recv_left = None
    for step in range(1, n):
        send_right = block(n - step + me)
        send_left = block(me + step - n)
        if recv_right is not None:
            send_right = send_right + recv_right
            send_left = send_left + recv_left
        recv_right = lax.ppermute(
            send_right.astype(send_dtype), axis, [(j, j + 1) for j in range(0, step)]
        ).astype(jnp.float32)
        recv_left = lax.ppermute(
            send_left.astype(send_dtype), axis, [(j, j - 1) for j in range(n - step, n)]
        ).astype(jnp.float32)
    return block(me) + recv_right + recv_left


COL = ("chip", "core")


def col_gather(block, axis):
    return lax.all_gather(block, COL, axis=axis, tiled=True)


def col_scatter(partial, axis):
    low_part = partial.astype(jnp.bfloat16)
    return lax.psum_scatter(low_part, COL, scatter_dimension=axis, tiled=True).astype(jnp.float32)


def layer_norm(inputs):
    center = inputs - jnp.mean(inputs, axis=-1, keepdims=True)
    spread = jnp.mean(center * center, axis=-1, keepdims=True)
    return center * lax.rsqrt(spread + EPSILON)


def norm_back(inputs, grad):
    center = inputs - jnp.mean(inputs, axis=-1, keepdims=True)
    inverse = lax.rsqrt(jnp.mean(center * center, axis=-1, keepdims=True) + EPSILON)
    normed = center * inverse
    return inverse * (
        grad
        - jnp.mean(grad, axis=-1, keepdims=True)
        - normed * jnp.mean(grad * normed, axis=-1, keepdims=True)
    )


def rope_tables():
    positions = jnp.arange(LENGTH, dtype=jnp.float32)
    freqs = jnp.power(jnp.float32(10000.0), -jnp.arange(HD // 2, dtype=jnp.float32) * (2.0 / HD))
    angles = positions[:, None] * freqs[None, :]
    return (jnp.cos(angles)[:, None, :], jnp.sin(angles)[:, None, :])


def rotate(field, cosine, sine):
    half_size = field.shape[-1] // 2
    first_half = field[..., :half_size]
    second_half = field[..., half_size:]
    return jnp.concatenate(
        [first_half * cosine - second_half * sine, second_half * cosine + first_half * sine],
        axis=-1,
    )


def unrotate(field, cosine, sine):
    half_size = field.shape[-1] // 2
    first_half = field[..., :half_size]
    second_half = field[..., half_size:]
    return jnp.concatenate(
        [first_half * cosine + second_half * sine, second_half * cosine - first_half * sine],
        axis=-1,
    )


def piece_mask(starts):
    positions = jnp.arange(LENGTH, dtype=jnp.int32)
    inside = (positions[None, :] >= starts[:, None]) & (
        positions[None, :] < starts[:, None] + PIECE
    )
    shared = jnp.any(inside[:, :, None] & inside[:, None, :], axis=0)
    causal = positions[None, :] <= positions[:, None]
    return causal | shared


def masked_scores(queries, keys_rot, starts):
    scale = 1.0 / math.sqrt(HD)
    scores = (
        jnp.einsum("qhd,khd->hqk", queries, keys_rot, preferred_element_type=jnp.float32) * scale
    )
    return jnp.where(piece_mask(starts)[None], scores, NEGATIVE)


def attend_forward(operands):
    queries, keys_rot, values, starts = operands
    scores = masked_scores(queries, keys_rot, starts)
    row_top = jnp.max(scores, axis=-1, keepdims=True)
    shifted = jnp.exp(scores - row_top)
    row_total = jnp.sum(shifted, axis=-1, keepdims=True)
    probs = (shifted / row_total).astype(jnp.bfloat16)
    mixed = jnp.einsum("hqk,khd->qhd", probs, values, preferred_element_type=jnp.float32)
    return (mixed, row_top + jnp.log(row_total))


def attend_backward(operands):
    queries, keys_rot, values, starts, log_total, grad_mixed = operands
    scale = 1.0 / math.sqrt(HD)
    scores = masked_scores(queries, keys_rot, starts)
    probs = jnp.exp(scores - log_total)
    probs_low = probs.astype(jnp.bfloat16)
    grad_values = jnp.einsum(
        "hqk,qhd->khd", probs_low, grad_mixed, preferred_element_type=jnp.float32
    )
    grad_probs = jnp.einsum("qhd,khd->hqk", grad_mixed, values, preferred_element_type=jnp.float32)
    inner = jnp.sum(probs * grad_probs, axis=-1, keepdims=True)
    grad_scores = (probs * (grad_probs - inner)).astype(jnp.bfloat16)
    grad_queries = (
        jnp.einsum("hqk,khd->qhd", grad_scores, keys_rot, preferred_element_type=jnp.float32)
        * scale
    )
    grad_keys = (
        jnp.einsum("hqk,qhd->khd", grad_scores, queries, preferred_element_type=jnp.float32) * scale
    )
    return (grad_queries, grad_keys, grad_values)


def per_device_body(
    layer_input, w_query, w_key, w_value, w_output, w_gate, w_up, w_down, piece_starts, cotangent
):
    seq_count = piece_starts.shape[0]
    group_rows = seq_count * LENGTH
    heads_local = w_query.shape[1] // HD
    gathered = (
        col_gather(w_query, 0),
        col_gather(w_key, 0),
        col_gather(w_value, 0),
        col_gather(w_output, 1),
        col_gather(w_gate, 0),
        col_gather(w_up, 0),
        col_gather(w_down, 1),
    )
    full_query, full_key, full_value, full_output, full_gate, full_up, full_down = gathered
    cosine, sine = rope_tables()
    inputs = layer_input.astype(jnp.float32)
    normed_first = layer_norm(inputs).astype(jnp.bfloat16)
    first_rows = line_all_gather(normed_first, "row")

    def split_heads(matrix):
        return matrix.reshape(seq_count, LENGTH, heads_local, HD)

    def merge_heads(field):
        return field.reshape(group_rows, heads_local * HD)

    queries = rotate(split_heads(product(first_rows, full_query)), cosine, sine).astype(
        jnp.bfloat16
    )
    keys_rot = rotate(split_heads(product(first_rows, full_key)), cosine, sine).astype(jnp.bfloat16)
    values = split_heads(product(first_rows, full_value)).astype(jnp.bfloat16)
    mixed, log_total = lax.map(attend_forward, (queries, keys_rot, values, piece_starts))
    attended = merge_heads(mixed.astype(jnp.bfloat16))
    attention_sum = line_reduce_scatter(product(attended, full_output), "row", jnp.bfloat16)
    middle = inputs + attention_sum
    normed_second = layer_norm(middle).astype(jnp.bfloat16)
    second_rows = line_all_gather(normed_second, "row")
    gate_lin = product(second_rows, full_gate)
    up_lin = product(second_rows, full_up)
    activation = (jax.nn.silu(gate_lin) * up_lin).astype(jnp.bfloat16)
    ffn_sum = line_reduce_scatter(product(activation, full_down), "row", jnp.bfloat16)
    output = (middle + ffn_sum).astype(jnp.bfloat16)
    back_query, back_key, back_value, back_output = (full_query, full_key, full_value, full_output)
    back_gate, back_up, back_down = (full_gate, full_up, full_down)
    grad_rows = line_all_gather(cotangent, "row")
    grad_activation = times_transpose(grad_rows, back_down)
    sigma = jax.nn.sigmoid(gate_lin)
    grad_gate = (grad_activation * up_lin * sigma * (1.0 + gate_lin * (1.0 - sigma))).astype(
        jnp.bfloat16
    )
    grad_up = (grad_activation * gate_lin * sigma).astype(jnp.bfloat16)
    grad_second = line_reduce_scatter(
        times_transpose(grad_gate, back_gate) + times_transpose(grad_up, back_up),
        "row",
        jnp.bfloat16,
    )
    grad_middle = cotangent.astype(jnp.float32) + norm_back(middle, grad_second)
    grad_branch = line_all_gather(grad_middle.astype(jnp.bfloat16), "row")
    grad_mixed = split_heads(times_transpose(grad_branch, back_output).astype(jnp.bfloat16))
    grad_q_rot, grad_k_rot, grad_values = lax.map(
        attend_backward, (queries, keys_rot, values, piece_starts, log_total, grad_mixed)
    )
    grad_query = merge_heads(unrotate(grad_q_rot, cosine, sine)).astype(jnp.bfloat16)
    grad_key = merge_heads(unrotate(grad_k_rot, cosine, sine)).astype(jnp.bfloat16)
    grad_value = merge_heads(grad_values).astype(jnp.bfloat16)
    grad_first = line_reduce_scatter(
        times_transpose(grad_query, back_query)
        + times_transpose(grad_key, back_key)
        + times_transpose(grad_value, back_value),
        "row",
        jnp.bfloat16,
    )
    grad_input = grad_middle + norm_back(inputs, grad_first)
    grad_query_w = contract_rows(first_rows, grad_query)
    grad_key_w = contract_rows(first_rows, grad_key)
    grad_value_w = contract_rows(first_rows, grad_value)
    grad_output_w = contract_rows(attended, grad_branch)
    grad_gate_w = contract_rows(second_rows, grad_gate)
    grad_up_w = contract_rows(second_rows, grad_up)
    grad_down_w = contract_rows(activation, grad_rows)
    summed = (
        col_scatter(grad_query_w, 0),
        col_scatter(grad_key_w, 0),
        col_scatter(grad_value_w, 0),
        col_scatter(grad_output_w, 1),
        col_scatter(grad_gate_w, 0),
        col_scatter(grad_up_w, 0),
        col_scatter(grad_down_w, 1),
    )
    results = tuple(summed)
    return (
        output,
        grad_input,
        results[0],
        results[1],
        results[2],
        results[3],
        results[4],
        results[5],
        results[6],
    )


def solution(mesh):
    in_specs = (
        P(("chip", "core", "row"), None),
        P(COL, "row"),
        P(COL, "row"),
        P(COL, "row"),
        P("row", COL),
        P(COL, "row"),
        P(COL, "row"),
        P("row", COL),
        P(COL, None),
        P(("chip", "core", "row"), None),
    )
    out_specs = (
        P(("chip", "core", "row"), None),
        P(("chip", "core", "row"), None),
        P(COL, "row"),
        P(COL, "row"),
        P(COL, "row"),
        P("row", COL),
        P(COL, "row"),
        P(COL, "row"),
        P("row", COL),
    )
    devices = mesh.devices
    sub_mesh = Mesh(
        devices.reshape(devices.shape[0], devices.shape[1] // 2, 2), ("row", "chip", "core")
    )
    return jax.shard_map(
        per_device_body, mesh=sub_mesh, in_specs=in_specs, out_specs=out_specs, check_vma=False
    )
```

```python
import math

import jax
import jax.numpy as jnp
from jax import lax
from jax.sharding import Mesh, PartitionSpec as P


HD = 128
LENGTH = 1024
PIECE = 256


EPSILON = 1e-05
NEGATIVE = -1e30


def product(left, right):
    return jnp.dot(left, right, preferred_element_type=jnp.float32)


def contract_rows(left, right):
    return lax.dot_general(
        left, right, (((0,), (0,)), ((), ())), preferred_element_type=jnp.float32
    )


def times_transpose(left, right):
    return lax.dot_general(
        left, right, (((1,), (1,)), ((), ())), preferred_element_type=jnp.float32
    )


def line_all_gather(shard, axis):
    n = lax.psum(1, axis)
    if n == 1:
        return shard
    me = lax.axis_index(axis)
    rows = shard.shape[0]
    buf = jnp.zeros(((3 * n - 2) * rows,) + shard.shape[1:], shard.dtype)
    buf = lax.dynamic_update_slice_in_dim(buf, shard, (me + n - 1) * rows, 0)
    from_left = shard
    from_right = shard
    for step in range(1, n):
        right_pairs = [(j, j + 1) for j in range(step - 1, n - 1)]
        left_pairs = [(j, j - 1) for j in range(1, n - step + 1)]
        from_left = lax.ppermute(from_left, axis, right_pairs)
        from_right = lax.ppermute(from_right, axis, left_pairs)
        buf = lax.dynamic_update_slice_in_dim(buf, from_left, (me - step + n - 1) * rows, 0)
        buf = lax.dynamic_update_slice_in_dim(buf, from_right, (me + step + n - 1) * rows, 0)
    return buf[(n - 1) * rows : (2 * n - 1) * rows]


def line_reduce_scatter(partial, axis, send_dtype):
    n = lax.psum(1, axis)
    if n == 1:
        return partial
    me = lax.axis_index(axis)
    rows = partial.shape[0] // n

    def block(k):
        return lax.dynamic_slice_in_dim(partial, jnp.clip(k, 0, n - 1) * rows, rows, 0)

    recv_right = None
    recv_left = None
    for step in range(1, n):
        send_right = block(n - step + me)
        send_left = block(me + step - n)
        if recv_right is not None:
            send_right = send_right + recv_right
            send_left = send_left + recv_left
        recv_right = lax.ppermute(
            send_right.astype(send_dtype), axis, [(j, j + 1) for j in range(0, step)]
        ).astype(jnp.float32)
        recv_left = lax.ppermute(
            send_left.astype(send_dtype), axis, [(j, j - 1) for j in range(n - step, n)]
        ).astype(jnp.float32)
    return block(me) + recv_right + recv_left


class GatherSteps:
    def __init__(self, shard, axis):
        self.axis = axis
        self.n = lax.psum(1, axis)
        self.me = lax.axis_index(axis)
        self.rows = shard.shape[0]
        buf = jnp.zeros(((3 * self.n - 2) * self.rows,) + shard.shape[1:], shard.dtype)
        self.buf = lax.dynamic_update_slice_in_dim(buf, shard, (self.me + self.n - 1) * self.rows, 0)
        self.pending = (shard, shard)
        self.step = 0

    def steps(self):
        return self.n - 1

    def send(self):
        n, step = self.n, self.step + 1
        from_left, from_right = self.pending
        from_left = lax.ppermute(from_left, self.axis, [(j, j + 1) for j in range(step - 1, n - 1)])
        from_right = lax.ppermute(from_right, self.axis, [(j, j - 1) for j in range(1, n - step + 1)])
        self.pending = (from_left, from_right)
        self.step = step

    def land(self):
        n, step, rows = self.n, self.step, self.rows
        from_left, from_right = self.pending
        self.buf = lax.dynamic_update_slice_in_dim(self.buf, from_left, (self.me - step + n - 1) * rows, 0)
        self.buf = lax.dynamic_update_slice_in_dim(self.buf, from_right, (self.me + step + n - 1) * rows, 0)

    def result(self):
        return self.buf[(self.n - 1) * self.rows : (2 * self.n - 1) * self.rows]


class ScatterSteps:
    def __init__(self, partial, axis, send_dtype):
        self.axis = axis
        self.n = lax.psum(1, axis)
        self.me = lax.axis_index(axis)
        self.rows = partial.shape[0] // self.n
        self.partial = partial
        self.send_dtype = send_dtype
        self.pending = None
        self.step = 0

    def steps(self):
        return self.n - 1

    def block(self, k):
        return lax.dynamic_slice_in_dim(
            self.partial, jnp.clip(k, 0, self.n - 1) * self.rows, self.rows, 0
        )

    def send(self):
        n, me, step = self.n, self.me, self.step + 1
        send_right = self.block(n - step + me)
        send_left = self.block(me + step - n)
        if self.pending is not None:
            send_right = send_right + self.pending[0].astype(jnp.float32)
            send_left = send_left + self.pending[1].astype(jnp.float32)
        recv_right = lax.ppermute(
            send_right.astype(self.send_dtype), self.axis, [(j, j + 1) for j in range(0, step)]
        )
        recv_left = lax.ppermute(
            send_left.astype(self.send_dtype), self.axis, [(j, j - 1) for j in range(n - step, n)]
        )
        self.pending = (recv_right, recv_left)
        self.step = step

    def land(self):
        pass

    def result(self):
        return (
            self.block(self.me)
            + self.pending[0].astype(jnp.float32)
            + self.pending[1].astype(jnp.float32)
        )


def overlap(chain, pieces):
    value = ()
    count = chain.steps()
    for index in range(count):
        chain.send()
        if index < len(pieces):
            value = pieces[index](value)
        chain.pending, value = lax.optimization_barrier((chain.pending, value))
        chain.land()
    for piece in pieces[count:]:
        value = piece(value)
    return value


COL = ("chip", "core")


def col_gather(block, axis):
    return lax.all_gather(block, COL, axis=axis, tiled=True)


def col_scatter(partial, axis):
    low_part = partial.astype(jnp.bfloat16)
    return lax.psum_scatter(low_part, COL, scatter_dimension=axis, tiled=True).astype(jnp.float32)


def layer_norm(inputs):
    center = inputs - jnp.mean(inputs, axis=-1, keepdims=True)
    spread = jnp.mean(center * center, axis=-1, keepdims=True)
    return center * lax.rsqrt(spread + EPSILON)


def norm_back(inputs, grad):
    center = inputs - jnp.mean(inputs, axis=-1, keepdims=True)
    inverse = lax.rsqrt(jnp.mean(center * center, axis=-1, keepdims=True) + EPSILON)
    normed = center * inverse
    return inverse * (
        grad
        - jnp.mean(grad, axis=-1, keepdims=True)
        - normed * jnp.mean(grad * normed, axis=-1, keepdims=True)
    )


def rope_tables():
    positions = jnp.arange(LENGTH, dtype=jnp.float32)
    freqs = jnp.power(jnp.float32(10000.0), -jnp.arange(HD // 2, dtype=jnp.float32) * (2.0 / HD))
    angles = positions[:, None] * freqs[None, :]
    return (jnp.cos(angles)[:, None, :], jnp.sin(angles)[:, None, :])


def rotate(field, cosine, sine):
    half_size = field.shape[-1] // 2
    first_half = field[..., :half_size]
    second_half = field[..., half_size:]
    return jnp.concatenate(
        [first_half * cosine - second_half * sine, second_half * cosine + first_half * sine],
        axis=-1,
    )


def unrotate(field, cosine, sine):
    half_size = field.shape[-1] // 2
    first_half = field[..., :half_size]
    second_half = field[..., half_size:]
    return jnp.concatenate(
        [first_half * cosine + second_half * sine, second_half * cosine - first_half * sine],
        axis=-1,
    )


def piece_mask(starts):
    positions = jnp.arange(LENGTH, dtype=jnp.int32)
    inside = (positions[None, :] >= starts[:, None]) & (
        positions[None, :] < starts[:, None] + PIECE
    )
    shared = jnp.any(inside[:, :, None] & inside[:, None, :], axis=0)
    causal = positions[None, :] <= positions[:, None]
    return causal | shared


def masked_scores(queries, keys_rot, starts):
    scale = 1.0 / math.sqrt(HD)
    scores = (
        jnp.einsum("qhd,khd->hqk", queries, keys_rot, preferred_element_type=jnp.float32) * scale
    )
    return jnp.where(piece_mask(starts)[None], scores, NEGATIVE)


def attend_forward(operands):
    queries, keys_rot, values, starts = operands
    scores = masked_scores(queries, keys_rot, starts)
    row_top = jnp.max(scores, axis=-1, keepdims=True)
    shifted = jnp.exp(scores - row_top)
    row_total = jnp.sum(shifted, axis=-1, keepdims=True)
    probs = (shifted / row_total).astype(jnp.bfloat16)
    mixed = jnp.einsum("hqk,khd->qhd", probs, values, preferred_element_type=jnp.float32)
    return (mixed, row_top + jnp.log(row_total))


def attend_backward(operands):
    queries, keys_rot, values, starts, log_total, grad_mixed = operands
    scale = 1.0 / math.sqrt(HD)
    scores = masked_scores(queries, keys_rot, starts)
    probs = jnp.exp(scores - log_total)
    probs_low = probs.astype(jnp.bfloat16)
    grad_values = jnp.einsum(
        "hqk,qhd->khd", probs_low, grad_mixed, preferred_element_type=jnp.float32
    )
    grad_probs = jnp.einsum("qhd,khd->hqk", grad_mixed, values, preferred_element_type=jnp.float32)
    inner = jnp.sum(probs * grad_probs, axis=-1, keepdims=True)
    grad_scores = (probs * (grad_probs - inner)).astype(jnp.bfloat16)
    grad_queries = (
        jnp.einsum("hqk,khd->qhd", grad_scores, keys_rot, preferred_element_type=jnp.float32)
        * scale
    )
    grad_keys = (
        jnp.einsum("hqk,qhd->khd", grad_scores, queries, preferred_element_type=jnp.float32) * scale
    )
    return (grad_queries, grad_keys, grad_values)


def per_device_body(
    layer_input, w_query, w_key, w_value, w_output, w_gate, w_up, w_down, piece_starts, cotangent
):
    seq_count = piece_starts.shape[0]
    group_rows = seq_count * LENGTH
    width = w_query.shape[1]
    hidden = w_gate.shape[1]
    heads_local = width // HD
    full_qkv = col_gather(jnp.concatenate([w_query, w_key, w_value], axis=1), 0)
    full_output = col_gather(w_output, 1)
    full_gu = col_gather(jnp.concatenate([w_gate, w_up], axis=1), 0)
    full_down = col_gather(w_down, 1)
    cosine, sine = rope_tables()
    inputs = layer_input.astype(jnp.float32)
    normed_first = layer_norm(inputs).astype(jnp.bfloat16)
    first_rows = line_all_gather(normed_first, "row")

    def split_heads(matrix):
        return matrix.reshape(seq_count, LENGTH, heads_local, HD)

    def merge_heads(field):
        return field.reshape(group_rows, heads_local * HD)

    def project(_):
        qkv_lin = product(first_rows, full_qkv)
        queries = rotate(split_heads(qkv_lin[:, :width]), cosine, sine).astype(jnp.bfloat16)
        keys_rot = rotate(split_heads(qkv_lin[:, width : 2 * width]), cosine, sine).astype(
            jnp.bfloat16
        )
        values = split_heads(qkv_lin[:, 2 * width :]).astype(jnp.bfloat16)
        return dict(queries=queries, keys_rot=keys_rot, values=values)

    def attend(state):
        mixed, log_total = lax.map(
            attend_forward, (state["queries"], state["keys_rot"], state["values"], piece_starts)
        )
        return dict(state, mixed=mixed, log_total=log_total)

    def out_project(state):
        attended = merge_heads(state.pop("mixed").astype(jnp.bfloat16))
        return dict(state, attended=attended, attn_partial=product(attended, full_output))

    cot_chain = GatherSteps(cotangent, "row")
    fwd = overlap(cot_chain, [project, attend, out_project])
    grad_rows = cot_chain.result()
    queries, keys_rot, values = fwd["queries"], fwd["keys_rot"], fwd["values"]
    log_total, attended = fwd["log_total"], fwd["attended"]
    attention_sum = line_reduce_scatter(fwd["attn_partial"], "row", jnp.bfloat16)
    middle = inputs + attention_sum
    normed_second = layer_norm(middle).astype(jnp.bfloat16)
    second_rows = line_all_gather(normed_second, "row")
    gu_lin = product(second_rows, full_gu)
    gate_lin = gu_lin[:, :hidden]
    up_lin = gu_lin[:, hidden:]
    activation = (jax.nn.silu(gate_lin) * up_lin).astype(jnp.bfloat16)
    ffn_chain = ScatterSteps(product(activation, full_down), "row", jnp.bfloat16)

    def gate_up_grads(_):
        grad_activation = times_transpose(grad_rows, full_down)
        sigma = jax.nn.sigmoid(gate_lin)
        grad_gate = grad_activation * up_lin * sigma * (1.0 + gate_lin * (1.0 - sigma))
        grad_up = grad_activation * gate_lin * sigma
        return dict(grad_gu=jnp.concatenate([grad_gate, grad_up], axis=1).astype(jnp.bfloat16))

    def second_partial(state):
        return dict(state, second_partial=times_transpose(state["grad_gu"], full_gu))

    def down_weight_grad(state):
        return dict(state, grad_down_w=contract_rows(activation, grad_rows))

    bwd = overlap(ffn_chain, [gate_up_grads, second_partial, down_weight_grad])
    ffn_sum = ffn_chain.result()
    output = (middle + ffn_sum).astype(jnp.bfloat16)
    grad_gu = bwd["grad_gu"]
    down_sum = col_scatter(bwd["grad_down_w"], 1)
    second_chain = ScatterSteps(bwd["second_partial"], "row", jnp.bfloat16)

    def gate_up_weight_grad(_):
        return contract_rows(second_rows, grad_gu)

    grad_gu_w = overlap(second_chain, [gate_up_weight_grad])
    grad_second = second_chain.result()
    gu_sum = col_scatter(grad_gu_w, 0)
    grad_middle = cotangent.astype(jnp.float32) + norm_back(middle, grad_second)
    grad_branch = line_all_gather(grad_middle.astype(jnp.bfloat16), "row")
    output_sum = col_scatter(contract_rows(attended, grad_branch), 1)
    grad_mixed = split_heads(times_transpose(grad_branch, full_output).astype(jnp.bfloat16))
    grad_q_rot, grad_k_rot, grad_values = lax.map(
        attend_backward, (queries, keys_rot, values, piece_starts, log_total, grad_mixed)
    )
    grad_qkv = jnp.concatenate(
        [
            merge_heads(unrotate(grad_q_rot, cosine, sine)),
            merge_heads(unrotate(grad_k_rot, cosine, sine)),
            merge_heads(grad_values),
        ],
        axis=1,
    ).astype(jnp.bfloat16)
    qkv_sum = col_scatter(contract_rows(first_rows, grad_qkv), 0)
    grad_first = line_reduce_scatter(times_transpose(grad_qkv, full_qkv), "row", jnp.bfloat16)
    grad_input = grad_middle + norm_back(inputs, grad_first)
    return (
        output,
        grad_input,
        qkv_sum[:, :width],
        qkv_sum[:, width : 2 * width],
        qkv_sum[:, 2 * width :],
        output_sum,
        gu_sum[:, :hidden],
        gu_sum[:, hidden:],
        down_sum,
    )


def solution(mesh):
    in_specs = (
        P(("chip", "core", "row"), None),
        P(COL, "row"),
        P(COL, "row"),
        P(COL, "row"),
        P("row", COL),
        P(COL, "row"),
        P(COL, "row"),
        P("row", COL),
        P(COL, None),
        P(("chip", "core", "row"), None),
    )
    out_specs = (
        P(("chip", "core", "row"), None),
        P(("chip", "core", "row"), None),
        P(COL, "row"),
        P(COL, "row"),
        P(COL, "row"),
        P("row", COL),
        P(COL, "row"),
        P(COL, "row"),
        P("row", COL),
    )
    devices = mesh.devices
    sub_mesh = Mesh(
        devices.reshape(devices.shape[0], devices.shape[1] // 2, 2), ("row", "chip", "core")
    )
    return jax.shard_map(
        per_device_body, mesh=sub_mesh, in_specs=in_specs, out_specs=out_specs, check_vma=False
    )
```

```python
import math

import jax
import jax.numpy as jnp
from jax import lax
from jax.sharding import Mesh, PartitionSpec as P


HD = 128
LENGTH = 1024
PIECE = 256


EPSILON = 1e-05
NEGATIVE = -1e30


def product(left, right):
    return jnp.dot(left, right, preferred_element_type=jnp.float32)


def contract_rows(left, right):
    return lax.dot_general(
        left, right, (((0,), (0,)), ((), ())), preferred_element_type=jnp.float32
    )


def times_transpose(left, right):
    return lax.dot_general(
        left, right, (((1,), (1,)), ((), ())), preferred_element_type=jnp.float32
    )


def line_all_gather(shard, axis):
    n = lax.psum(1, axis)
    if n == 1:
        return shard
    me = lax.axis_index(axis)
    rows = shard.shape[0]
    buf = jnp.zeros(((3 * n - 2) * rows,) + shard.shape[1:], shard.dtype)
    buf = lax.dynamic_update_slice_in_dim(buf, shard, (me + n - 1) * rows, 0)
    from_left = shard
    from_right = shard
    for step in range(1, n):
        right_pairs = [(j, j + 1) for j in range(step - 1, n - 1)]
        left_pairs = [(j, j - 1) for j in range(1, n - step + 1)]
        from_left = lax.ppermute(from_left, axis, right_pairs)
        from_right = lax.ppermute(from_right, axis, left_pairs)
        buf = lax.dynamic_update_slice_in_dim(buf, from_left, (me - step + n - 1) * rows, 0)
        buf = lax.dynamic_update_slice_in_dim(buf, from_right, (me + step + n - 1) * rows, 0)
    return buf[(n - 1) * rows : (2 * n - 1) * rows]


def line_reduce_scatter(partial, axis, send_dtype):
    n = lax.psum(1, axis)
    if n == 1:
        return partial
    me = lax.axis_index(axis)
    rows = partial.shape[0] // n

    def block(k):
        return lax.dynamic_slice_in_dim(partial, jnp.clip(k, 0, n - 1) * rows, rows, 0)

    recv_right = None
    recv_left = None
    for step in range(1, n):
        send_right = block(n - step + me)
        send_left = block(me + step - n)
        if recv_right is not None:
            send_right = send_right + recv_right
            send_left = send_left + recv_left
        recv_right = lax.ppermute(
            send_right.astype(send_dtype), axis, [(j, j + 1) for j in range(0, step)]
        ).astype(jnp.float32)
        recv_left = lax.ppermute(
            send_left.astype(send_dtype), axis, [(j, j - 1) for j in range(n - step, n)]
        ).astype(jnp.float32)
    return block(me) + recv_right + recv_left


class GatherSteps:
    def __init__(self, shard, axis):
        self.axis = axis
        self.n = lax.psum(1, axis)
        self.me = lax.axis_index(axis)
        self.rows = shard.shape[0]
        buf = jnp.zeros(((3 * self.n - 2) * self.rows,) + shard.shape[1:], shard.dtype)
        self.buf = lax.dynamic_update_slice_in_dim(buf, shard, (self.me + self.n - 1) * self.rows, 0)
        self.pending = (shard, shard)
        self.step = 0

    def steps(self):
        return self.n - 1

    def send(self):
        n, step = self.n, self.step + 1
        from_left, from_right = self.pending
        from_left = lax.ppermute(from_left, self.axis, [(j, j + 1) for j in range(step - 1, n - 1)])
        from_right = lax.ppermute(from_right, self.axis, [(j, j - 1) for j in range(1, n - step + 1)])
        self.pending = (from_left, from_right)
        self.step = step

    def land(self):
        n, step, rows = self.n, self.step, self.rows
        from_left, from_right = self.pending
        self.buf = lax.dynamic_update_slice_in_dim(self.buf, from_left, (self.me - step + n - 1) * rows, 0)
        self.buf = lax.dynamic_update_slice_in_dim(self.buf, from_right, (self.me + step + n - 1) * rows, 0)

    def result(self):
        return self.buf[(self.n - 1) * self.rows : (2 * self.n - 1) * self.rows]


class ScatterSteps:
    def __init__(self, partial, axis, send_dtype):
        self.axis = axis
        self.n = lax.psum(1, axis)
        self.me = lax.axis_index(axis)
        self.rows = partial.shape[0] // self.n
        self.partial = partial
        self.send_dtype = send_dtype
        self.pending = None
        self.step = 0

    def steps(self):
        return self.n - 1

    def block(self, k):
        return lax.dynamic_slice_in_dim(
            self.partial, jnp.clip(k, 0, self.n - 1) * self.rows, self.rows, 0
        )

    def send(self):
        n, me, step = self.n, self.me, self.step + 1
        send_right = self.block(n - step + me)
        send_left = self.block(me + step - n)
        if self.pending is not None:
            send_right = send_right + self.pending[0].astype(jnp.float32)
            send_left = send_left + self.pending[1].astype(jnp.float32)
        recv_right = lax.ppermute(
            send_right.astype(self.send_dtype), self.axis, [(j, j + 1) for j in range(0, step)]
        )
        recv_left = lax.ppermute(
            send_left.astype(self.send_dtype), self.axis, [(j, j - 1) for j in range(n - step, n)]
        )
        self.pending = (recv_right, recv_left)
        self.step = step

    def land(self):
        pass

    def result(self):
        return (
            self.block(self.me)
            + self.pending[0].astype(jnp.float32)
            + self.pending[1].astype(jnp.float32)
        )


def overlap(chain, pieces):
    value = ()
    count = chain.steps()
    for index in range(count):
        chain.send()
        if index < len(pieces):
            value = pieces[index](value)
        chain.pending, value = lax.optimization_barrier((chain.pending, value))
        chain.land()
    for piece in pieces[count:]:
        value = piece(value)
    return value


COL = ("chip", "core")


def col_gather(block, axis):
    return lax.all_gather(block, COL, axis=axis, tiled=True)


def col_scatter(partial, axis):
    low_part = partial.astype(jnp.bfloat16)
    return lax.psum_scatter(low_part, COL, scatter_dimension=axis, tiled=True).astype(jnp.float32)


def layer_norm(inputs):
    center = inputs - jnp.mean(inputs, axis=-1, keepdims=True)
    spread = jnp.mean(center * center, axis=-1, keepdims=True)
    return center * lax.rsqrt(spread + EPSILON)


def norm_back(inputs, grad):
    center = inputs - jnp.mean(inputs, axis=-1, keepdims=True)
    inverse = lax.rsqrt(jnp.mean(center * center, axis=-1, keepdims=True) + EPSILON)
    normed = center * inverse
    return inverse * (
        grad
        - jnp.mean(grad, axis=-1, keepdims=True)
        - normed * jnp.mean(grad * normed, axis=-1, keepdims=True)
    )


def rope_tables():
    positions = jnp.arange(LENGTH, dtype=jnp.float32)
    freqs = jnp.power(jnp.float32(10000.0), -jnp.arange(HD // 2, dtype=jnp.float32) * (2.0 / HD))
    angles = positions[:, None] * freqs[None, :]
    return (jnp.cos(angles)[:, None, :], jnp.sin(angles)[:, None, :])


def rotate(field, cosine, sine):
    half_size = field.shape[-1] // 2
    first_half = field[..., :half_size]
    second_half = field[..., half_size:]
    return jnp.concatenate(
        [first_half * cosine - second_half * sine, second_half * cosine + first_half * sine],
        axis=-1,
    )


def unrotate(field, cosine, sine):
    half_size = field.shape[-1] // 2
    first_half = field[..., :half_size]
    second_half = field[..., half_size:]
    return jnp.concatenate(
        [first_half * cosine + second_half * sine, second_half * cosine - first_half * sine],
        axis=-1,
    )


def piece_mask(starts):
    positions = jnp.arange(LENGTH, dtype=jnp.int32)
    inside = (positions[None, :] >= starts[:, None]) & (
        positions[None, :] < starts[:, None] + PIECE
    )
    shared = jnp.any(inside[:, :, None] & inside[:, None, :], axis=0)
    causal = positions[None, :] <= positions[:, None]
    return causal | shared


def masked_scores(queries, keys_rot, starts):
    scale = 1.0 / math.sqrt(HD)
    scores = (
        jnp.einsum("qhd,khd->hqk", queries, keys_rot, preferred_element_type=jnp.float32) * scale
    )
    return jnp.where(piece_mask(starts)[None], scores, NEGATIVE)


def attend_forward(operands):
    queries, keys_rot, values, starts = operands
    scores = masked_scores(queries, keys_rot, starts)
    row_top = jnp.max(scores, axis=-1, keepdims=True)
    shifted = jnp.exp(scores - row_top)
    row_total = jnp.sum(shifted, axis=-1, keepdims=True)
    probs = (shifted / row_total).astype(jnp.bfloat16)
    mixed = jnp.einsum("hqk,khd->qhd", probs, values, preferred_element_type=jnp.float32)
    return (mixed, row_top + jnp.log(row_total))


def attend_backward(operands):
    queries, keys_rot, values, starts, log_total, grad_mixed = operands
    scale = 1.0 / math.sqrt(HD)
    scores = masked_scores(queries, keys_rot, starts)
    probs = jnp.exp(scores - log_total)
    probs_low = probs.astype(jnp.bfloat16)
    grad_values = jnp.einsum(
        "hqk,qhd->khd", probs_low, grad_mixed, preferred_element_type=jnp.float32
    )
    grad_probs = jnp.einsum("qhd,khd->hqk", grad_mixed, values, preferred_element_type=jnp.float32)
    inner = jnp.sum(probs * grad_probs, axis=-1, keepdims=True)
    grad_scores = (probs * (grad_probs - inner)).astype(jnp.bfloat16)
    grad_queries = (
        jnp.einsum("hqk,khd->qhd", grad_scores, keys_rot, preferred_element_type=jnp.float32)
        * scale
    )
    grad_keys = (
        jnp.einsum("hqk,qhd->khd", grad_scores, queries, preferred_element_type=jnp.float32) * scale
    )
    return (grad_queries, grad_keys, grad_values)


def per_device_body(
    layer_input, w_query, w_key, w_value, w_output, w_gate, w_up, w_down, piece_starts, cotangent
):
    seq_count = piece_starts.shape[0]
    group_rows = seq_count * LENGTH
    width = w_query.shape[1]
    hidden = w_gate.shape[1]
    heads_local = width // HD
    full_qkv = col_gather(jnp.concatenate([w_query, w_key, w_value], axis=1), 0)
    full_output = col_gather(w_output, 1)
    full_gu = col_gather(jnp.concatenate([w_gate, w_up], axis=1), 0)
    full_down = col_gather(w_down, 1)
    cosine, sine = rope_tables()
    inputs = layer_input.astype(jnp.float32)
    normed_first = layer_norm(inputs).astype(jnp.bfloat16)
    first_rows = line_all_gather(normed_first, "row")

    def split_heads(matrix):
        return matrix.reshape(seq_count, LENGTH, heads_local, HD)

    def merge_heads(field):
        return field.reshape(group_rows, heads_local * HD)

    def project(_):
        qkv_lin = product(first_rows, full_qkv)
        queries = rotate(split_heads(qkv_lin[:, :width]), cosine, sine).astype(jnp.bfloat16)
        keys_rot = rotate(split_heads(qkv_lin[:, width : 2 * width]), cosine, sine).astype(
            jnp.bfloat16
        )
        values = split_heads(qkv_lin[:, 2 * width :]).astype(jnp.bfloat16)
        return dict(queries=queries, keys_rot=keys_rot, values=values)

    def attend(state):
        mixed, log_total = lax.map(
            attend_forward, (state["queries"], state["keys_rot"], state["values"], piece_starts)
        )
        return dict(state, mixed=mixed, log_total=log_total)

    def out_project(state):
        attended = merge_heads(state.pop("mixed").astype(jnp.bfloat16))
        return dict(state, attended=attended, attn_partial=product(attended, full_output))

    cot_later, first_rows = lax.optimization_barrier((cotangent, first_rows))
    cot_chain = GatherSteps(cot_later, "row")
    fwd = overlap(cot_chain, [project, attend, out_project])
    grad_rows = cot_chain.result()
    queries, keys_rot, values = fwd["queries"], fwd["keys_rot"], fwd["values"]
    log_total, attended = fwd["log_total"], fwd["attended"]
    attention_sum = line_reduce_scatter(fwd["attn_partial"], "row", jnp.bfloat16)
    middle = inputs + attention_sum
    normed_second = layer_norm(middle).astype(jnp.bfloat16)
    second_rows = line_all_gather(normed_second, "row")
    gu_lin = product(second_rows, full_gu)
    gate_lin = gu_lin[:, :hidden]
    up_lin = gu_lin[:, hidden:]
    activation = (jax.nn.silu(gate_lin) * up_lin).astype(jnp.bfloat16)
    ffn_chain = ScatterSteps(product(activation, full_down), "row", jnp.bfloat16)

    def gate_up_grads(_):
        grad_activation = times_transpose(grad_rows, full_down)
        sigma = jax.nn.sigmoid(gate_lin)
        grad_gate = grad_activation * up_lin * sigma * (1.0 + gate_lin * (1.0 - sigma))
        grad_up = grad_activation * gate_lin * sigma
        return dict(grad_gu=jnp.concatenate([grad_gate, grad_up], axis=1).astype(jnp.bfloat16))

    def second_partial(state):
        return dict(state, second_partial=times_transpose(state["grad_gu"], full_gu))

    def down_weight_grad(state):
        return dict(state, grad_down_w=contract_rows(activation, grad_rows))

    bwd = overlap(ffn_chain, [gate_up_grads, second_partial, down_weight_grad])
    ffn_sum = ffn_chain.result()
    output = (middle + ffn_sum).astype(jnp.bfloat16)
    grad_gu = bwd["grad_gu"]
    down_sum = col_scatter(bwd["grad_down_w"], 1)
    second_chain = ScatterSteps(bwd["second_partial"], "row", jnp.bfloat16)

    def gate_up_weight_grad(_):
        return contract_rows(second_rows, grad_gu)

    def keep_down_sum(grad_gu_w):
        return (grad_gu_w, down_sum)

    grad_gu_w, down_sum = overlap(
        second_chain, [gate_up_weight_grad, lambda value: value, keep_down_sum]
    )
    grad_second = second_chain.result()
    gu_sum = col_scatter(grad_gu_w, 0)
    grad_middle = cotangent.astype(jnp.float32) + norm_back(middle, grad_second)
    grad_branch = line_all_gather(grad_middle.astype(jnp.bfloat16), "row")
    output_sum = col_scatter(contract_rows(attended, grad_branch), 1)
    grad_mixed = split_heads(times_transpose(grad_branch, full_output).astype(jnp.bfloat16))
    grad_q_rot, grad_k_rot, grad_values = lax.map(
        attend_backward, (queries, keys_rot, values, piece_starts, log_total, grad_mixed)
    )
    grad_qkv = jnp.concatenate(
        [
            merge_heads(unrotate(grad_q_rot, cosine, sine)),
            merge_heads(unrotate(grad_k_rot, cosine, sine)),
            merge_heads(grad_values),
        ],
        axis=1,
    ).astype(jnp.bfloat16)
    qkv_sum = col_scatter(contract_rows(first_rows, grad_qkv), 0)
    grad_first = line_reduce_scatter(times_transpose(grad_qkv, full_qkv), "row", jnp.bfloat16)
    grad_input = grad_middle + norm_back(inputs, grad_first)
    return (
        output,
        grad_input,
        qkv_sum[:, :width],
        qkv_sum[:, width : 2 * width],
        qkv_sum[:, 2 * width :],
        output_sum,
        gu_sum[:, :hidden],
        gu_sum[:, hidden:],
        down_sum,
    )


def solution(mesh):
    in_specs = (
        P(("chip", "core", "row"), None),
        P(COL, "row"),
        P(COL, "row"),
        P(COL, "row"),
        P("row", COL),
        P(COL, "row"),
        P(COL, "row"),
        P("row", COL),
        P(COL, None),
        P(("chip", "core", "row"), None),
    )
    out_specs = (
        P(("chip", "core", "row"), None),
        P(("chip", "core", "row"), None),
        P(COL, "row"),
        P(COL, "row"),
        P(COL, "row"),
        P("row", COL),
        P(COL, "row"),
        P(COL, "row"),
        P("row", COL),
    )
    devices = mesh.devices
    sub_mesh = Mesh(
        devices.reshape(devices.shape[0], devices.shape[1] // 2, 2), ("row", "chip", "core")
    )
    return jax.shard_map(
        per_device_body, mesh=sub_mesh, in_specs=in_specs, out_specs=out_specs, check_vma=False
    )
```

```python
import math

import jax
import jax.numpy as jnp
from jax import lax
from jax.sharding import Mesh, PartitionSpec as P


HD = 128
LENGTH = 1024
PIECE = 256


EPSILON = 1e-05
NEGATIVE = -1e30


def product(left, right):
    return jnp.dot(left, right, preferred_element_type=jnp.float32)


def contract_rows(left, right):
    return lax.dot_general(
        left, right, (((0,), (0,)), ((), ())), preferred_element_type=jnp.float32
    )


def times_transpose(left, right):
    return lax.dot_general(
        left, right, (((1,), (1,)), ((), ())), preferred_element_type=jnp.float32
    )


def line_all_gather(shard, axis):
    n = lax.psum(1, axis)
    if n == 1:
        return shard
    me = lax.axis_index(axis)
    rows = shard.shape[0]
    buf = jnp.zeros(((3 * n - 2) * rows,) + shard.shape[1:], shard.dtype)
    buf = lax.dynamic_update_slice_in_dim(buf, shard, (me + n - 1) * rows, 0)
    from_left = shard
    from_right = shard
    for step in range(1, n):
        right_pairs = [(j, j + 1) for j in range(step - 1, n - 1)]
        left_pairs = [(j, j - 1) for j in range(1, n - step + 1)]
        from_left = lax.ppermute(from_left, axis, right_pairs)
        from_right = lax.ppermute(from_right, axis, left_pairs)
        buf = lax.dynamic_update_slice_in_dim(buf, from_left, (me - step + n - 1) * rows, 0)
        buf = lax.dynamic_update_slice_in_dim(buf, from_right, (me + step + n - 1) * rows, 0)
    return buf[(n - 1) * rows : (2 * n - 1) * rows]


def line_reduce_scatter(partial, axis, send_dtype):
    n = lax.psum(1, axis)
    if n == 1:
        return partial
    me = lax.axis_index(axis)
    rows = partial.shape[0] // n

    def block(k):
        return lax.dynamic_slice_in_dim(partial, jnp.clip(k, 0, n - 1) * rows, rows, 0)

    recv_right = None
    recv_left = None
    for step in range(1, n):
        send_right = block(n - step + me)
        send_left = block(me + step - n)
        if recv_right is not None:
            send_right = send_right + recv_right
            send_left = send_left + recv_left
        recv_right = lax.ppermute(
            send_right.astype(send_dtype), axis, [(j, j + 1) for j in range(0, step)]
        ).astype(jnp.float32)
        recv_left = lax.ppermute(
            send_left.astype(send_dtype), axis, [(j, j - 1) for j in range(n - step, n)]
        ).astype(jnp.float32)
    return block(me) + recv_right + recv_left


class GatherSteps:
    def __init__(self, shard, axis):
        self.axis = axis
        self.n = lax.psum(1, axis)
        self.me = lax.axis_index(axis)
        self.rows = shard.shape[0]
        buf = jnp.zeros(((3 * self.n - 2) * self.rows,) + shard.shape[1:], shard.dtype)
        self.buf = lax.dynamic_update_slice_in_dim(buf, shard, (self.me + self.n - 1) * self.rows, 0)
        self.pending = (shard, shard)
        self.step = 0

    def steps(self):
        return self.n - 1

    def send(self):
        n, step = self.n, self.step + 1
        from_left, from_right = self.pending
        from_left = lax.ppermute(from_left, self.axis, [(j, j + 1) for j in range(step - 1, n - 1)])
        from_right = lax.ppermute(from_right, self.axis, [(j, j - 1) for j in range(1, n - step + 1)])
        self.pending = (from_left, from_right)
        self.step = step

    def land(self):
        n, step, rows = self.n, self.step, self.rows
        from_left, from_right = self.pending
        self.buf = lax.dynamic_update_slice_in_dim(self.buf, from_left, (self.me - step + n - 1) * rows, 0)
        self.buf = lax.dynamic_update_slice_in_dim(self.buf, from_right, (self.me + step + n - 1) * rows, 0)

    def result(self):
        return self.buf[(self.n - 1) * self.rows : (2 * self.n - 1) * self.rows]


class ScatterSteps:
    def __init__(self, partial, axis, send_dtype):
        self.axis = axis
        self.n = lax.psum(1, axis)
        self.me = lax.axis_index(axis)
        self.rows = partial.shape[0] // self.n
        self.partial = partial
        self.send_dtype = send_dtype
        self.pending = None
        self.step = 0

    def steps(self):
        return self.n - 1

    def block(self, k):
        return lax.dynamic_slice_in_dim(
            self.partial, jnp.clip(k, 0, self.n - 1) * self.rows, self.rows, 0
        )

    def send(self):
        n, me, step = self.n, self.me, self.step + 1
        send_right = self.block(n - step + me)
        send_left = self.block(me + step - n)
        if self.pending is not None:
            send_right = send_right + self.pending[0].astype(jnp.float32)
            send_left = send_left + self.pending[1].astype(jnp.float32)
        recv_right = lax.ppermute(
            send_right.astype(self.send_dtype), self.axis, [(j, j + 1) for j in range(0, step)]
        )
        recv_left = lax.ppermute(
            send_left.astype(self.send_dtype), self.axis, [(j, j - 1) for j in range(n - step, n)]
        )
        self.pending = (recv_right, recv_left)
        self.step = step

    def land(self):
        pass

    def result(self):
        return (
            self.block(self.me)
            + self.pending[0].astype(jnp.float32)
            + self.pending[1].astype(jnp.float32)
        )


class RingGather:
    def __init__(self, shard, axis):
        self.axis = axis
        self.n = lax.psum(1, axis)
        self.slots = [shard]
        self.pending = shard

    def steps(self):
        return self.n - 1

    def send(self):
        n = self.n
        self.pending = lax.ppermute(self.pending, self.axis, [(j, (j + 1) % n) for j in range(n)])

    def land(self):
        self.slots.append(self.pending)


class RingScatter:
    def __init__(self, slots, axis, send_dtype):
        self.axis = axis
        self.n = lax.psum(1, axis)
        self.slots = slots
        self.send_dtype = send_dtype
        self.pending = None
        self.step = 0

    def steps(self):
        return self.n - 1

    def send(self):
        n, step = self.n, self.step + 1
        value = self.slots[step]
        if self.pending is not None:
            value = value + self.pending.astype(jnp.float32)
        self.pending = lax.ppermute(
            value.astype(self.send_dtype), self.axis, [(j, (j + 1) % n) for j in range(n)]
        )
        self.step = step

    def land(self):
        pass

    def result(self):
        return self.slots[0] + self.pending.astype(jnp.float32)


def overlap(chain, pieces):
    value = ()
    count = chain.steps()
    for index in range(count):
        chain.send()
        if index < len(pieces):
            value = pieces[index](value)
        chain.pending, value = lax.optimization_barrier((chain.pending, value))
        chain.land()
    for piece in pieces[count:]:
        value = piece(value)
    return value


COL = ("chip", "core")


def col_gather(block, axis):
    return lax.all_gather(block, COL, axis=axis, tiled=True)


def col_scatter(partial, axis):
    low_part = partial.astype(jnp.bfloat16)
    return lax.psum_scatter(low_part, COL, scatter_dimension=axis, tiled=True).astype(jnp.float32)


def layer_norm(inputs):
    center = inputs - jnp.mean(inputs, axis=-1, keepdims=True)
    spread = jnp.mean(center * center, axis=-1, keepdims=True)
    return center * lax.rsqrt(spread + EPSILON)


def norm_back(inputs, grad):
    center = inputs - jnp.mean(inputs, axis=-1, keepdims=True)
    inverse = lax.rsqrt(jnp.mean(center * center, axis=-1, keepdims=True) + EPSILON)
    normed = center * inverse
    return inverse * (
        grad
        - jnp.mean(grad, axis=-1, keepdims=True)
        - normed * jnp.mean(grad * normed, axis=-1, keepdims=True)
    )


def rope_tables():
    positions = jnp.arange(LENGTH, dtype=jnp.float32)
    freqs = jnp.power(jnp.float32(10000.0), -jnp.arange(HD // 2, dtype=jnp.float32) * (2.0 / HD))
    angles = positions[:, None] * freqs[None, :]
    return (jnp.cos(angles)[:, None, :], jnp.sin(angles)[:, None, :])


def rotate(field, cosine, sine):
    half_size = field.shape[-1] // 2
    first_half = field[..., :half_size]
    second_half = field[..., half_size:]
    return jnp.concatenate(
        [first_half * cosine - second_half * sine, second_half * cosine + first_half * sine],
        axis=-1,
    )


def unrotate(field, cosine, sine):
    half_size = field.shape[-1] // 2
    first_half = field[..., :half_size]
    second_half = field[..., half_size:]
    return jnp.concatenate(
        [first_half * cosine + second_half * sine, second_half * cosine - first_half * sine],
        axis=-1,
    )


def piece_mask(starts):
    positions = jnp.arange(LENGTH, dtype=jnp.int32)
    inside = (positions[None, :] >= starts[:, None]) & (
        positions[None, :] < starts[:, None] + PIECE
    )
    shared = jnp.any(inside[:, :, None] & inside[:, None, :], axis=0)
    causal = positions[None, :] <= positions[:, None]
    return causal | shared


def masked_scores(queries, keys_rot, starts):
    scale = 1.0 / math.sqrt(HD)
    scores = (
        jnp.einsum("qhd,khd->hqk", queries, keys_rot, preferred_element_type=jnp.float32) * scale
    )
    return jnp.where(piece_mask(starts)[None], scores, NEGATIVE)


def attend_forward(operands):
    queries, keys_rot, values, starts = operands
    scores = masked_scores(queries, keys_rot, starts)
    row_top = jnp.max(scores, axis=-1, keepdims=True)
    shifted = jnp.exp(scores - row_top)
    row_total = jnp.sum(shifted, axis=-1, keepdims=True)
    probs = (shifted / row_total).astype(jnp.bfloat16)
    mixed = jnp.einsum("hqk,khd->qhd", probs, values, preferred_element_type=jnp.float32)
    return (mixed, row_top + jnp.log(row_total))


def attend_backward(operands):
    queries, keys_rot, values, starts, log_total, grad_mixed = operands
    scale = 1.0 / math.sqrt(HD)
    scores = masked_scores(queries, keys_rot, starts)
    probs = jnp.exp(scores - log_total)
    probs_low = probs.astype(jnp.bfloat16)
    grad_values = jnp.einsum(
        "hqk,qhd->khd", probs_low, grad_mixed, preferred_element_type=jnp.float32
    )
    grad_probs = jnp.einsum("qhd,khd->hqk", grad_mixed, values, preferred_element_type=jnp.float32)
    inner = jnp.sum(probs * grad_probs, axis=-1, keepdims=True)
    grad_scores = (probs * (grad_probs - inner)).astype(jnp.bfloat16)
    grad_queries = (
        jnp.einsum("hqk,khd->qhd", grad_scores, keys_rot, preferred_element_type=jnp.float32)
        * scale
    )
    grad_keys = (
        jnp.einsum("hqk,qhd->khd", grad_scores, queries, preferred_element_type=jnp.float32) * scale
    )
    return (grad_queries, grad_keys, grad_values)


def per_device_body(
    layer_input, w_query, w_key, w_value, w_output, w_gate, w_up, w_down, piece_starts, cotangent
):
    seq_count = piece_starts.shape[0]
    group_rows = seq_count * LENGTH
    width = w_query.shape[1]
    hidden = w_gate.shape[1]
    heads_local = width // HD
    full_qkv = col_gather(jnp.concatenate([w_query, w_key, w_value], axis=1), 0)
    full_output = col_gather(w_output, 1)
    full_gu = col_gather(jnp.concatenate([w_gate, w_up], axis=1), 0)
    full_down = col_gather(w_down, 1)
    cosine, sine = rope_tables()
    inputs = layer_input.astype(jnp.float32)
    normed_first = layer_norm(inputs).astype(jnp.bfloat16)
    first_rows = line_all_gather(normed_first, "row")

    def split_heads(matrix):
        return matrix.reshape(seq_count, LENGTH, heads_local, HD)

    def merge_heads(field):
        return field.reshape(group_rows, heads_local * HD)

    def project(_):
        qkv_lin = product(first_rows, full_qkv)
        queries = rotate(split_heads(qkv_lin[:, :width]), cosine, sine).astype(jnp.bfloat16)
        keys_rot = rotate(split_heads(qkv_lin[:, width : 2 * width]), cosine, sine).astype(
            jnp.bfloat16
        )
        values = split_heads(qkv_lin[:, 2 * width :]).astype(jnp.bfloat16)
        return dict(queries=queries, keys_rot=keys_rot, values=values)

    def attend(state):
        mixed, log_total = lax.map(
            attend_forward, (state["queries"], state["keys_rot"], state["values"], piece_starts)
        )
        return dict(state, mixed=mixed, log_total=log_total)

    def out_project(state):
        attended = merge_heads(state.pop("mixed").astype(jnp.bfloat16))
        return dict(state, attended=attended, attn_partial=product(attended, full_output))

    cot_later, first_rows = lax.optimization_barrier((cotangent, first_rows))
    cot_ring = RingGather(cot_later, "row")
    fwd = overlap(cot_ring, [project, attend, out_project])
    cot_slots = cot_ring.slots
    queries, keys_rot, values = fwd["queries"], fwd["keys_rot"], fwd["values"]
    log_total, attended = fwd["log_total"], fwd["attended"]
    attention_sum = line_reduce_scatter(fwd["attn_partial"], "row", jnp.bfloat16)
    middle = inputs + attention_sum
    normed_second = layer_norm(middle).astype(jnp.bfloat16)
    second_ring = RingGather(normed_second, "row")
    slots = second_ring.n

    def ffn_forward(slot):
        def piece(done):
            gu_lin = product(second_ring.slots[slot], full_gu)
            gate_lin = gu_lin[:, :hidden]
            up_lin = gu_lin[:, hidden:]
            activation = (jax.nn.silu(gate_lin) * up_lin).astype(jnp.bfloat16)
            part = product(activation, full_down)
            return done + ((gate_lin, up_lin, activation, part),)

        return piece

    ffn = overlap(second_ring, [ffn_forward(slot) for slot in range(slots)])
    second_slots = second_ring.slots
    gate_slots = [item[0] for item in ffn]
    up_slots = [item[1] for item in ffn]
    act_slots = [item[2] for item in ffn]
    ffn_ring = RingScatter([item[3] for item in ffn], "row", jnp.bfloat16)

    def ffn_backward(slot):
        def piece(done):
            gate_lin, up_lin = gate_slots[slot], up_slots[slot]
            grad_activation = times_transpose(cot_slots[slot], full_down)
            sigma = jax.nn.sigmoid(gate_lin)
            grad_gate = grad_activation * up_lin * sigma * (1.0 + gate_lin * (1.0 - sigma))
            grad_up = grad_activation * gate_lin * sigma
            grad_gu = jnp.concatenate([grad_gate, grad_up], axis=1).astype(jnp.bfloat16)
            return done + ((grad_gu, times_transpose(grad_gu, full_gu)),)

        return piece

    order = list(range(1, slots)) + [0]
    bwd = overlap(ffn_ring, [ffn_backward(slot) for slot in order])
    ffn_sum = ffn_ring.result()
    output = (middle + ffn_sum).astype(jnp.bfloat16)
    by_slot = dict(zip(order, bwd))
    grad_gu = jnp.concatenate([by_slot[slot][0] for slot in range(slots)], axis=0)
    second_ring_back = RingScatter([by_slot[slot][1] for slot in range(slots)], "row", jnp.bfloat16)
    rows_second = jnp.concatenate(second_slots, axis=0)

    def down_weight_grad(_):
        return contract_rows(jnp.concatenate(act_slots, axis=0), jnp.concatenate(cot_slots, axis=0))

    def gate_up_weight_grad(grad_down_w):
        return (grad_down_w, contract_rows(rows_second, grad_gu))

    grad_down_w, grad_gu_w = overlap(second_ring_back, [down_weight_grad, gate_up_weight_grad])
    grad_second = second_ring_back.result()
    down_sum = col_scatter(grad_down_w, 1)
    gu_sum = col_scatter(grad_gu_w, 0)
    grad_middle = cotangent.astype(jnp.float32) + norm_back(middle, grad_second)
    branch_chain = GatherSteps(grad_middle.astype(jnp.bfloat16), "row")
    down_sum = overlap(branch_chain, [lambda value: value] * (branch_chain.steps() - 1) + [lambda value: down_sum])
    grad_branch = branch_chain.result()
    output_sum = col_scatter(contract_rows(attended, grad_branch), 1)
    grad_mixed = split_heads(times_transpose(grad_branch, full_output).astype(jnp.bfloat16))
    grad_q_rot, grad_k_rot, grad_values = lax.map(
        attend_backward, (queries, keys_rot, values, piece_starts, log_total, grad_mixed)
    )
    grad_qkv = jnp.concatenate(
        [
            merge_heads(unrotate(grad_q_rot, cosine, sine)),
            merge_heads(unrotate(grad_k_rot, cosine, sine)),
            merge_heads(grad_values),
        ],
        axis=1,
    ).astype(jnp.bfloat16)
    qkv_sum = col_scatter(contract_rows(first_rows, grad_qkv), 0)
    grad_first = line_reduce_scatter(times_transpose(grad_qkv, full_qkv), "row", jnp.bfloat16)
    grad_input = grad_middle + norm_back(inputs, grad_first)
    return (
        output,
        grad_input,
        qkv_sum[:, :width],
        qkv_sum[:, width : 2 * width],
        qkv_sum[:, 2 * width :],
        output_sum,
        gu_sum[:, :hidden],
        gu_sum[:, hidden:],
        down_sum,
    )


def solution(mesh):
    in_specs = (
        P(("chip", "core", "row"), None),
        P(COL, "row"),
        P(COL, "row"),
        P(COL, "row"),
        P("row", COL),
        P(COL, "row"),
        P(COL, "row"),
        P("row", COL),
        P(COL, None),
        P(("chip", "core", "row"), None),
    )
    out_specs = (
        P(("chip", "core", "row"), None),
        P(("chip", "core", "row"), None),
        P(COL, "row"),
        P(COL, "row"),
        P(COL, "row"),
        P("row", COL),
        P(COL, "row"),
        P(COL, "row"),
        P("row", COL),
    )
    devices = mesh.devices
    sub_mesh = Mesh(
        devices.reshape(devices.shape[0], devices.shape[1] // 2, 2), ("row", "chip", "core")
    )
    return jax.shard_map(
        per_device_body, mesh=sub_mesh, in_specs=in_specs, out_specs=out_specs, check_vma=False
    )
```

```python
import math

import jax
import jax.numpy as jnp
from jax import lax
from jax.sharding import Mesh, PartitionSpec as P


HD = 128
LENGTH = 1024
PIECE = 256


EPSILON = 1e-05
NEGATIVE = -1e30


def product(left, right):
    return jnp.dot(left, right, preferred_element_type=jnp.float32)


def contract_rows(left, right):
    return lax.dot_general(
        left, right, (((0,), (0,)), ((), ())), preferred_element_type=jnp.float32
    )


def times_transpose(left, right):
    return lax.dot_general(
        left, right, (((1,), (1,)), ((), ())), preferred_element_type=jnp.float32
    )


class GatherSteps:
    def __init__(self, shard, axis):
        self.axis = axis
        self.n = lax.psum(1, axis)
        self.me = lax.axis_index(axis)
        self.rows = shard.shape[0]
        buf = jnp.zeros(((3 * self.n - 2) * self.rows,) + shard.shape[1:], shard.dtype)
        self.buf = lax.dynamic_update_slice_in_dim(buf, shard, (self.me + self.n - 1) * self.rows, 0)
        self.pending = (shard, shard)
        self.step = 0

    def steps(self):
        return self.n - 1

    def send(self):
        n, step = self.n, self.step + 1
        from_left, from_right = self.pending
        from_left = lax.ppermute(from_left, self.axis, [(j, j + 1) for j in range(step - 1, n - 1)])
        from_right = lax.ppermute(from_right, self.axis, [(j, j - 1) for j in range(1, n - step + 1)])
        self.pending = (from_left, from_right)
        self.step = step

    def land(self):
        n, step, rows = self.n, self.step, self.rows
        from_left, from_right = self.pending
        self.buf = lax.dynamic_update_slice_in_dim(self.buf, from_left, (self.me - step + n - 1) * rows, 0)
        self.buf = lax.dynamic_update_slice_in_dim(self.buf, from_right, (self.me + step + n - 1) * rows, 0)

    def result(self):
        return self.buf[(self.n - 1) * self.rows : (2 * self.n - 1) * self.rows]


class ScatterSteps:
    def __init__(self, partial, axis, send_dtype):
        self.axis = axis
        self.n = lax.psum(1, axis)
        self.me = lax.axis_index(axis)
        self.rows = partial.shape[0] // self.n
        self.partial = partial
        self.send_dtype = send_dtype
        self.pending = None
        self.step = 0

    def steps(self):
        return self.n - 1

    def block(self, k):
        return lax.dynamic_slice_in_dim(
            self.partial, jnp.clip(k, 0, self.n - 1) * self.rows, self.rows, 0
        )

    def send(self):
        n, me, step = self.n, self.me, self.step + 1
        send_right = self.block(n - step + me)
        send_left = self.block(me + step - n)
        if self.pending is not None:
            send_right = send_right + self.pending[0].astype(jnp.float32)
            send_left = send_left + self.pending[1].astype(jnp.float32)
        recv_right = lax.ppermute(
            send_right.astype(self.send_dtype), self.axis, [(j, j + 1) for j in range(0, step)]
        )
        recv_left = lax.ppermute(
            send_left.astype(self.send_dtype), self.axis, [(j, j - 1) for j in range(n - step, n)]
        )
        self.pending = (recv_right, recv_left)
        self.step = step

    def land(self):
        pass

    def result(self):
        return (
            self.block(self.me)
            + self.pending[0].astype(jnp.float32)
            + self.pending[1].astype(jnp.float32)
        )


class RingGather:
    def __init__(self, shard, axis, absolute=False):
        self.axis = axis
        self.n = lax.psum(1, axis)
        self.me = lax.axis_index(axis)
        self.rows = shard.shape[0]
        self.slots = [shard]
        self.pending = shard
        self.buf = None
        if absolute:
            buf = jnp.zeros((self.n * self.rows,) + shard.shape[1:], shard.dtype)
            self.buf = self.place(buf, shard, 0)

    def place(self, buf, block, slot):
        start = lax.rem(self.me - slot + self.n, self.n) * self.rows
        return lax.dynamic_update_slice_in_dim(buf, block, start, 0)

    def steps(self):
        return self.n - 1

    def send(self):
        n = self.n
        self.pending = lax.ppermute(self.pending, self.axis, [(j, (j + 1) % n) for j in range(n)])

    def land(self):
        self.slots.append(self.pending)
        if self.buf is not None:
            self.buf = self.place(self.buf, self.pending, len(self.slots) - 1)

    def result(self):
        return self.buf


class RingScatter:
    def __init__(self, slots, axis, send_dtype):
        self.axis = axis
        self.n = lax.psum(1, axis)
        self.slots = slots
        self.send_dtype = send_dtype
        self.pending = None
        self.step = 0

    def steps(self):
        return self.n - 1

    def send(self):
        n, step = self.n, self.step + 1
        value = self.slots[step]
        if self.pending is not None:
            value = value + self.pending.astype(jnp.float32)
        self.pending = lax.ppermute(
            value.astype(self.send_dtype), self.axis, [(j, (j + 1) % n) for j in range(n)]
        )
        self.step = step

    def land(self):
        pass

    def result(self):
        return self.slots[0] + self.pending.astype(jnp.float32)


def ring_slots(partial, axis):
    n = lax.psum(1, axis)
    me = lax.axis_index(axis)
    rows = partial.shape[0] // n
    return [
        lax.dynamic_slice_in_dim(partial, lax.rem(me - slot + n, n) * rows, rows, 0)
        for slot in range(n)
    ]


def ring_all_gather(shard, axis):
    chain = RingGather(shard, axis, absolute=True)
    overlap(chain, [])
    return chain.result()


def ring_reduce_scatter(partial, axis, send_dtype):
    chain = RingScatter(ring_slots(partial, axis), axis, send_dtype)
    overlap(chain, [])
    return chain.result()


def overlap(chain, pieces):
    outputs = []
    count = chain.steps()
    for index in range(count):
        chain.send()
        if index < len(pieces):
            value = pieces[index](tuple(outputs))
            chain.pending, value = lax.optimization_barrier((chain.pending, value))
            outputs.append(value)
        else:
            chain.pending = lax.optimization_barrier(chain.pending)
        chain.land()
    for piece in pieces[count:]:
        outputs.append(piece(tuple(outputs)))
    return tuple(outputs)


COL = ("chip", "core")


def col_gather(block, axis):
    return lax.all_gather(block, COL, axis=axis, tiled=True)


def col_scatter(partial, axis):
    low_part = partial.astype(jnp.bfloat16)
    return lax.psum_scatter(low_part, COL, scatter_dimension=axis, tiled=True).astype(jnp.float32)


def layer_norm(inputs):
    center = inputs - jnp.mean(inputs, axis=-1, keepdims=True)
    spread = jnp.mean(center * center, axis=-1, keepdims=True)
    return center * lax.rsqrt(spread + EPSILON)


def norm_back(inputs, grad):
    center = inputs - jnp.mean(inputs, axis=-1, keepdims=True)
    inverse = lax.rsqrt(jnp.mean(center * center, axis=-1, keepdims=True) + EPSILON)
    normed = center * inverse
    return inverse * (
        grad
        - jnp.mean(grad, axis=-1, keepdims=True)
        - normed * jnp.mean(grad * normed, axis=-1, keepdims=True)
    )


def rope_tables():
    positions = jnp.arange(LENGTH, dtype=jnp.float32)
    freqs = jnp.power(jnp.float32(10000.0), -jnp.arange(HD // 2, dtype=jnp.float32) * (2.0 / HD))
    angles = positions[:, None] * freqs[None, :]
    return (jnp.cos(angles)[:, None, :], jnp.sin(angles)[:, None, :])


def rotate(field, cosine, sine):
    half_size = field.shape[-1] // 2
    first_half = field[..., :half_size]
    second_half = field[..., half_size:]
    return jnp.concatenate(
        [first_half * cosine - second_half * sine, second_half * cosine + first_half * sine],
        axis=-1,
    )


def unrotate(field, cosine, sine):
    half_size = field.shape[-1] // 2
    first_half = field[..., :half_size]
    second_half = field[..., half_size:]
    return jnp.concatenate(
        [first_half * cosine + second_half * sine, second_half * cosine - first_half * sine],
        axis=-1,
    )


def piece_mask(starts):
    positions = jnp.arange(LENGTH, dtype=jnp.int32)
    inside = (positions[None, :] >= starts[:, None]) & (
        positions[None, :] < starts[:, None] + PIECE
    )
    shared = jnp.any(inside[:, :, None] & inside[:, None, :], axis=0)
    causal = positions[None, :] <= positions[:, None]
    return causal | shared


def masked_scores(queries, keys_rot, starts):
    scale = 1.0 / math.sqrt(HD)
    scores = (
        jnp.einsum("qhd,khd->hqk", queries, keys_rot, preferred_element_type=jnp.float32) * scale
    )
    return jnp.where(piece_mask(starts)[None], scores, NEGATIVE)


def attend_forward(operands):
    queries, keys_rot, values, starts = operands
    scores = masked_scores(queries, keys_rot, starts)
    row_top = jnp.max(scores, axis=-1, keepdims=True)
    shifted = jnp.exp(scores - row_top)
    row_total = jnp.sum(shifted, axis=-1, keepdims=True)
    probs = (shifted / row_total).astype(jnp.bfloat16)
    mixed = jnp.einsum("hqk,khd->qhd", probs, values, preferred_element_type=jnp.float32)
    return (mixed, row_top + jnp.log(row_total))


def attend_backward(operands):
    queries, keys_rot, values, starts, log_total, grad_mixed = operands
    scale = 1.0 / math.sqrt(HD)
    scores = masked_scores(queries, keys_rot, starts)
    probs = jnp.exp(scores - log_total)
    probs_low = probs.astype(jnp.bfloat16)
    grad_values = jnp.einsum(
        "hqk,qhd->khd", probs_low, grad_mixed, preferred_element_type=jnp.float32
    )
    grad_probs = jnp.einsum("qhd,khd->hqk", grad_mixed, values, preferred_element_type=jnp.float32)
    inner = jnp.sum(probs * grad_probs, axis=-1, keepdims=True)
    grad_scores = (probs * (grad_probs - inner)).astype(jnp.bfloat16)
    grad_queries = (
        jnp.einsum("hqk,khd->qhd", grad_scores, keys_rot, preferred_element_type=jnp.float32)
        * scale
    )
    grad_keys = (
        jnp.einsum("hqk,qhd->khd", grad_scores, queries, preferred_element_type=jnp.float32) * scale
    )
    return (grad_queries, grad_keys, grad_values)


def per_device_body(
    layer_input, w_query, w_key, w_value, w_output, w_gate, w_up, w_down, piece_starts, cotangent
):
    seq_count = piece_starts.shape[0]
    group_rows = seq_count * LENGTH
    width = w_query.shape[1]
    hidden = w_gate.shape[1]
    heads_local = width // HD
    full_qkv = col_gather(jnp.concatenate([w_query, w_key, w_value], axis=1), 0)
    full_output = col_gather(w_output, 1)
    full_gu = col_gather(jnp.concatenate([w_gate, w_up], axis=1), 0)
    full_down = col_gather(w_down, 1)
    cosine, sine = rope_tables()
    inputs = layer_input.astype(jnp.float32)
    normed_first = layer_norm(inputs).astype(jnp.bfloat16)
    first_rows = ring_all_gather(normed_first, "row")

    def split_heads(matrix):
        return matrix.reshape(seq_count, LENGTH, heads_local, HD)

    def merge_heads(field):
        return field.reshape(group_rows, heads_local * HD)

    def project(_):
        qkv_lin = product(first_rows, full_qkv)
        queries = rotate(split_heads(qkv_lin[:, :width]), cosine, sine).astype(jnp.bfloat16)
        keys_rot = rotate(split_heads(qkv_lin[:, width : 2 * width]), cosine, sine).astype(
            jnp.bfloat16
        )
        values = split_heads(qkv_lin[:, 2 * width :]).astype(jnp.bfloat16)
        return dict(queries=queries, keys_rot=keys_rot, values=values)

    def attend(done):
        state = done[0]
        mixed, log_total = lax.map(
            attend_forward, (state["queries"], state["keys_rot"], state["values"], piece_starts)
        )
        return dict(mixed=mixed, log_total=log_total)

    def out_project(done):
        attended = merge_heads(done[1]["mixed"].astype(jnp.bfloat16))
        return dict(attended=attended, attn_partial=product(attended, full_output))

    cot_later, first_rows = lax.optimization_barrier((cotangent, first_rows))
    cot_ring = RingGather(cot_later, "row")
    projected, attention, mixed_out = overlap(cot_ring, [project, attend, out_project])
    cot_slots = cot_ring.slots
    queries, keys_rot = projected["queries"], projected["keys_rot"]
    values = projected["values"]
    log_total, attended = attention["log_total"], mixed_out["attended"]
    attention_sum = ring_reduce_scatter(mixed_out["attn_partial"], "row", jnp.bfloat16)
    middle = inputs + attention_sum
    normed_second = layer_norm(middle).astype(jnp.bfloat16)
    second_ring = RingGather(normed_second, "row")
    slots = second_ring.n

    def ffn_forward(slot):
        def piece(done):
            gu_lin = product(second_ring.slots[slot], full_gu)
            gate_lin = gu_lin[:, :hidden]
            up_lin = gu_lin[:, hidden:]
            activation = (jax.nn.silu(gate_lin) * up_lin).astype(jnp.bfloat16)
            part = product(activation, full_down)
            return (gate_lin, up_lin, activation, part)

        return piece

    ffn = overlap(second_ring, [ffn_forward(slot) for slot in range(slots)])
    second_slots = second_ring.slots
    gate_slots = [item[0] for item in ffn]
    up_slots = [item[1] for item in ffn]
    act_slots = [item[2] for item in ffn]
    ffn_ring = RingScatter([item[3] for item in ffn], "row", jnp.bfloat16)

    def ffn_backward(slot):
        def piece(done):
            gate_lin, up_lin = gate_slots[slot], up_slots[slot]
            grad_activation = times_transpose(cot_slots[slot], full_down)
            sigma = jax.nn.sigmoid(gate_lin)
            grad_gate = grad_activation * up_lin * sigma * (1.0 + gate_lin * (1.0 - sigma))
            grad_up = grad_activation * gate_lin * sigma
            grad_gu = jnp.concatenate([grad_gate, grad_up], axis=1).astype(jnp.bfloat16)
            return (grad_gu, times_transpose(grad_gu, full_gu))

        return piece

    order = list(range(1, slots)) + [0]
    bwd = overlap(ffn_ring, [ffn_backward(slot) for slot in order])
    ffn_sum = ffn_ring.result()
    output = (middle + ffn_sum).astype(jnp.bfloat16)
    by_slot = dict(zip(order, bwd))
    grad_gu = jnp.concatenate([by_slot[slot][0] for slot in range(slots)], axis=0)
    second_ring_back = RingScatter([by_slot[slot][1] for slot in range(slots)], "row", jnp.bfloat16)
    rows_second = jnp.concatenate(second_slots, axis=0)

    def down_weight_grad(_):
        return contract_rows(jnp.concatenate(act_slots, axis=0), jnp.concatenate(cot_slots, axis=0))

    def gate_up_weight_grad(_):
        return contract_rows(rows_second, grad_gu)

    grad_down_w, grad_gu_w = overlap(second_ring_back, [down_weight_grad, gate_up_weight_grad])
    grad_second = second_ring_back.result()
    down_sum = col_scatter(grad_down_w, 1)
    gu_sum = col_scatter(grad_gu_w, 0)
    grad_middle = cotangent.astype(jnp.float32) + norm_back(middle, grad_second)
    branch_chain = RingGather(grad_middle.astype(jnp.bfloat16), "row", absolute=True)
    steps = branch_chain.steps()
    down_sum = overlap(branch_chain, [lambda done: ()] * (steps - 1) + [lambda done: down_sum])[-1]
    grad_branch = branch_chain.result()
    output_sum = col_scatter(contract_rows(attended, grad_branch), 1)
    grad_mixed = split_heads(times_transpose(grad_branch, full_output).astype(jnp.bfloat16))
    grad_q_rot, grad_k_rot, grad_values = lax.map(
        attend_backward, (queries, keys_rot, values, piece_starts, log_total, grad_mixed)
    )
    grad_qkv = jnp.concatenate(
        [
            merge_heads(unrotate(grad_q_rot, cosine, sine)),
            merge_heads(unrotate(grad_k_rot, cosine, sine)),
            merge_heads(grad_values),
        ],
        axis=1,
    ).astype(jnp.bfloat16)
    qkv_sum = col_scatter(contract_rows(first_rows, grad_qkv), 0)
    grad_first = ring_reduce_scatter(times_transpose(grad_qkv, full_qkv), "row", jnp.bfloat16)
    grad_input = grad_middle + norm_back(inputs, grad_first)
    return (
        output,
        grad_input,
        qkv_sum[:, :width],
        qkv_sum[:, width : 2 * width],
        qkv_sum[:, 2 * width :],
        output_sum,
        gu_sum[:, :hidden],
        gu_sum[:, hidden:],
        down_sum,
    )


def solution(mesh):
    in_specs = (
        P(("chip", "core", "row"), None),
        P(COL, "row"),
        P(COL, "row"),
        P(COL, "row"),
        P("row", COL),
        P(COL, "row"),
        P(COL, "row"),
        P("row", COL),
        P(COL, None),
        P(("chip", "core", "row"), None),
    )
    out_specs = (
        P(("chip", "core", "row"), None),
        P(("chip", "core", "row"), None),
        P(COL, "row"),
        P(COL, "row"),
        P(COL, "row"),
        P("row", COL),
        P(COL, "row"),
        P(COL, "row"),
        P("row", COL),
    )
    devices = mesh.devices
    sub_mesh = Mesh(
        devices.reshape(devices.shape[0], devices.shape[1] // 2, 2), ("row", "chip", "core")
    )
    return jax.shard_map(
        per_device_body, mesh=sub_mesh, in_specs=in_specs, out_specs=out_specs, check_vma=False
    )
```

```python
import math

import jax
import jax.numpy as jnp
from jax import lax
from jax.sharding import Mesh, PartitionSpec as P


HD = 128
LENGTH = 1024
PIECE = 256


EPSILON = 1e-05
NEGATIVE = -1e30


def product(left, right):
    return jnp.dot(left, right, preferred_element_type=jnp.float32)


def contract_rows(left, right):
    return lax.dot_general(
        left, right, (((0,), (0,)), ((), ())), preferred_element_type=jnp.float32
    )


def times_transpose(left, right):
    return lax.dot_general(
        left, right, (((1,), (1,)), ((), ())), preferred_element_type=jnp.float32
    )


class GatherSteps:
    def __init__(self, shard, axis):
        self.axis = axis
        self.n = lax.psum(1, axis)
        self.me = lax.axis_index(axis)
        self.rows = shard.shape[0]
        buf = jnp.zeros(((3 * self.n - 2) * self.rows,) + shard.shape[1:], shard.dtype)
        self.buf = lax.dynamic_update_slice_in_dim(buf, shard, (self.me + self.n - 1) * self.rows, 0)
        self.pending = (shard, shard)
        self.step = 0

    def steps(self):
        return self.n - 1

    def send(self):
        n, step = self.n, self.step + 1
        from_left, from_right = self.pending
        from_left = lax.ppermute(from_left, self.axis, [(j, j + 1) for j in range(step - 1, n - 1)])
        from_right = lax.ppermute(from_right, self.axis, [(j, j - 1) for j in range(1, n - step + 1)])
        self.pending = (from_left, from_right)
        self.step = step

    def land(self):
        n, step, rows = self.n, self.step, self.rows
        from_left, from_right = self.pending
        self.buf = lax.dynamic_update_slice_in_dim(self.buf, from_left, (self.me - step + n - 1) * rows, 0)
        self.buf = lax.dynamic_update_slice_in_dim(self.buf, from_right, (self.me + step + n - 1) * rows, 0)

    def result(self):
        return self.buf[(self.n - 1) * self.rows : (2 * self.n - 1) * self.rows]


class ScatterSteps:
    def __init__(self, partial, axis, send_dtype):
        self.axis = axis
        self.n = lax.psum(1, axis)
        self.me = lax.axis_index(axis)
        self.rows = partial.shape[0] // self.n
        self.partial = partial
        self.send_dtype = send_dtype
        self.pending = None
        self.step = 0

    def steps(self):
        return self.n - 1

    def block(self, k):
        return lax.dynamic_slice_in_dim(
            self.partial, jnp.clip(k, 0, self.n - 1) * self.rows, self.rows, 0
        )

    def send(self):
        n, me, step = self.n, self.me, self.step + 1
        send_right = self.block(n - step + me)
        send_left = self.block(me + step - n)
        if self.pending is not None:
            send_right = send_right + self.pending[0].astype(jnp.float32)
            send_left = send_left + self.pending[1].astype(jnp.float32)
        recv_right = lax.ppermute(
            send_right.astype(self.send_dtype), self.axis, [(j, j + 1) for j in range(0, step)]
        )
        recv_left = lax.ppermute(
            send_left.astype(self.send_dtype), self.axis, [(j, j - 1) for j in range(n - step, n)]
        )
        self.pending = (recv_right, recv_left)
        self.step = step

    def land(self):
        pass

    def result(self):
        return (
            self.block(self.me)
            + self.pending[0].astype(jnp.float32)
            + self.pending[1].astype(jnp.float32)
        )


class RingGather:
    def __init__(self, shard, axis, absolute=False):
        self.axis = axis
        self.n = lax.psum(1, axis)
        self.me = lax.axis_index(axis)
        self.rows = shard.shape[0]
        self.slots = [shard]
        self.pending = shard
        self.buf = None
        if absolute:
            buf = jnp.zeros((self.n * self.rows,) + shard.shape[1:], shard.dtype)
            self.buf = self.place(buf, shard, 0)

    def place(self, buf, block, slot):
        start = lax.rem(self.me - slot + self.n, self.n) * self.rows
        return lax.dynamic_update_slice_in_dim(buf, block, start, 0)

    def steps(self):
        return self.n - 1

    def send(self):
        n = self.n
        self.pending = lax.ppermute(self.pending, self.axis, [(j, (j + 1) % n) for j in range(n)])

    def land(self):
        self.slots.append(self.pending)
        if self.buf is not None:
            self.buf = self.place(self.buf, self.pending, len(self.slots) - 1)

    def result(self):
        return self.buf


class RingScatter:
    def __init__(self, slots, axis, send_dtype):
        self.axis = axis
        self.n = lax.psum(1, axis)
        self.slots = slots
        self.send_dtype = send_dtype
        self.pending = None
        self.step = 0

    def steps(self):
        return self.n - 1

    def send(self):
        n, step = self.n, self.step + 1
        value = self.slots[step]
        if self.pending is not None:
            value = value + self.pending.astype(jnp.float32)
        self.pending = lax.ppermute(
            value.astype(self.send_dtype), self.axis, [(j, (j + 1) % n) for j in range(n)]
        )
        self.step = step

    def land(self):
        pass

    def result(self):
        return self.slots[0] + self.pending.astype(jnp.float32)


def ring_slots(partial, axis):
    n = lax.psum(1, axis)
    me = lax.axis_index(axis)
    rows = partial.shape[0] // n
    return [
        lax.dynamic_slice_in_dim(partial, lax.rem(me - slot + n, n) * rows, rows, 0)
        for slot in range(n)
    ]


def ring_all_gather(shard, axis):
    chain = RingGather(shard, axis, absolute=True)
    overlap(chain, [])
    return chain.result()


def ring_reduce_scatter(partial, axis, send_dtype):
    chain = RingScatter(ring_slots(partial, axis), axis, send_dtype)
    overlap(chain, [])
    return chain.result()


def overlap(chain, pieces):
    outputs = []
    count = chain.steps()
    for index in range(count):
        chain.send()
        if index < len(pieces):
            value = pieces[index](tuple(outputs))
            chain.pending, value = lax.optimization_barrier((chain.pending, value))
            outputs.append(value)
        else:
            chain.pending = lax.optimization_barrier(chain.pending)
        chain.land()
    for piece in pieces[count:]:
        outputs.append(piece(tuple(outputs)))
    return tuple(outputs)


COL = ("chip", "core")


def col_gather(block, axis):
    return lax.all_gather(block, COL, axis=axis, tiled=True)


def col_scatter(partial, axis):
    low_part = partial.astype(jnp.bfloat16)
    return lax.psum_scatter(low_part, COL, scatter_dimension=axis, tiled=True).astype(jnp.float32)


def layer_norm(inputs):
    center = inputs - jnp.mean(inputs, axis=-1, keepdims=True)
    spread = jnp.mean(center * center, axis=-1, keepdims=True)
    return center * lax.rsqrt(spread + EPSILON)


def norm_back(inputs, grad):
    center = inputs - jnp.mean(inputs, axis=-1, keepdims=True)
    inverse = lax.rsqrt(jnp.mean(center * center, axis=-1, keepdims=True) + EPSILON)
    normed = center * inverse
    return inverse * (
        grad
        - jnp.mean(grad, axis=-1, keepdims=True)
        - normed * jnp.mean(grad * normed, axis=-1, keepdims=True)
    )


def rope_tables():
    positions = jnp.arange(LENGTH, dtype=jnp.float32)
    freqs = jnp.power(jnp.float32(10000.0), -jnp.arange(HD // 2, dtype=jnp.float32) * (2.0 / HD))
    angles = positions[:, None] * freqs[None, :]
    return (jnp.cos(angles)[:, None, :], jnp.sin(angles)[:, None, :])


def rotate(field, cosine, sine):
    half_size = field.shape[-1] // 2
    first_half = field[..., :half_size]
    second_half = field[..., half_size:]
    return jnp.concatenate(
        [first_half * cosine - second_half * sine, second_half * cosine + first_half * sine],
        axis=-1,
    )


def unrotate(field, cosine, sine):
    half_size = field.shape[-1] // 2
    first_half = field[..., :half_size]
    second_half = field[..., half_size:]
    return jnp.concatenate(
        [first_half * cosine + second_half * sine, second_half * cosine - first_half * sine],
        axis=-1,
    )


def piece_mask(starts):
    positions = jnp.arange(LENGTH, dtype=jnp.int32)
    inside = (positions[None, :] >= starts[:, None]) & (
        positions[None, :] < starts[:, None] + PIECE
    )
    shared = jnp.any(inside[:, :, None] & inside[:, None, :], axis=0)
    causal = positions[None, :] <= positions[:, None]
    return causal | shared


def masked_scores(queries, keys_rot, starts):
    scale = 1.0 / math.sqrt(HD)
    scores = (
        jnp.einsum("qhd,khd->hqk", queries, keys_rot, preferred_element_type=jnp.float32) * scale
    )
    return jnp.where(piece_mask(starts)[None], scores, NEGATIVE)


def attend_forward(operands):
    queries, keys_rot, values, starts = operands
    scores = masked_scores(queries, keys_rot, starts)
    row_top = jnp.max(scores, axis=-1, keepdims=True)
    shifted = jnp.exp(scores - row_top)
    row_total = jnp.sum(shifted, axis=-1, keepdims=True)
    probs = (shifted / row_total).astype(jnp.bfloat16)
    mixed = jnp.einsum("hqk,khd->qhd", probs, values, preferred_element_type=jnp.float32)
    return (mixed, row_top + jnp.log(row_total))


def attend_backward(operands):
    queries, keys_rot, values, starts, log_total, grad_mixed = operands
    scale = 1.0 / math.sqrt(HD)
    scores = masked_scores(queries, keys_rot, starts)
    probs = jnp.exp(scores - log_total)
    probs_low = probs.astype(jnp.bfloat16)
    grad_values = jnp.einsum(
        "hqk,qhd->khd", probs_low, grad_mixed, preferred_element_type=jnp.float32
    )
    grad_probs = jnp.einsum("qhd,khd->hqk", grad_mixed, values, preferred_element_type=jnp.float32)
    inner = jnp.sum(probs * grad_probs, axis=-1, keepdims=True)
    grad_scores = (probs * (grad_probs - inner)).astype(jnp.bfloat16)
    grad_queries = (
        jnp.einsum("hqk,khd->qhd", grad_scores, keys_rot, preferred_element_type=jnp.float32)
        * scale
    )
    grad_keys = (
        jnp.einsum("hqk,qhd->khd", grad_scores, queries, preferred_element_type=jnp.float32) * scale
    )
    return (grad_queries, grad_keys, grad_values)


def per_device_body(
    layer_input, w_query, w_key, w_value, w_output, w_gate, w_up, w_down, piece_starts, cotangent
):
    seq_count = piece_starts.shape[0]
    group_rows = seq_count * LENGTH
    width = w_query.shape[1]
    hidden = w_gate.shape[1]
    heads_local = width // HD
    full_qkv = col_gather(jnp.concatenate([w_query, w_key, w_value], axis=1), 0)
    full_output = col_gather(w_output, 1)
    full_gu = col_gather(jnp.concatenate([w_gate, w_up], axis=1), 0)
    full_down = col_gather(w_down, 1)
    cosine, sine = rope_tables()
    inputs = layer_input.astype(jnp.float32)
    normed_first = layer_norm(inputs).astype(jnp.bfloat16)
    first_rows = ring_all_gather(normed_first, "row")

    def split_heads(matrix):
        return matrix.reshape(seq_count, LENGTH, heads_local, HD)

    def merge_heads(field):
        return field.reshape(group_rows, heads_local * HD)

    def project(_):
        qkv_lin = product(first_rows, full_qkv)
        queries = rotate(split_heads(qkv_lin[:, :width]), cosine, sine).astype(jnp.bfloat16)
        keys_rot = rotate(split_heads(qkv_lin[:, width : 2 * width]), cosine, sine).astype(
            jnp.bfloat16
        )
        values = split_heads(qkv_lin[:, 2 * width :]).astype(jnp.bfloat16)
        return dict(queries=queries, keys_rot=keys_rot, values=values)

    def attend(done):
        state = done[0]
        mixed, log_total = lax.map(
            attend_forward, (state["queries"], state["keys_rot"], state["values"], piece_starts)
        )
        return dict(mixed=mixed, log_total=log_total)

    def out_project(done):
        attended = merge_heads(done[1]["mixed"].astype(jnp.bfloat16))
        return dict(attended=attended, attn_partial=product(attended, full_output))

    cot_later, first_rows = lax.optimization_barrier((cotangent, first_rows))
    cot_ring = RingGather(cot_later, "row")
    projected, attention, mixed_out = overlap(cot_ring, [project, attend, out_project])
    cot_slots = cot_ring.slots
    queries, keys_rot = projected["queries"], projected["keys_rot"]
    values = projected["values"]
    log_total, attended = attention["log_total"], mixed_out["attended"]
    attention_sum = ring_reduce_scatter(mixed_out["attn_partial"], "row", jnp.bfloat16)
    middle = inputs + attention_sum
    normed_second = layer_norm(middle).astype(jnp.bfloat16)
    second_ring = RingGather(normed_second, "row")
    slots = second_ring.n

    def ffn_forward(slot):
        def piece(done):
            gu_lin = product(second_ring.slots[slot], full_gu)
            gate_lin = gu_lin[:, :hidden]
            up_lin = gu_lin[:, hidden:]
            activation = (jax.nn.silu(gate_lin) * up_lin).astype(jnp.bfloat16)
            part = product(activation, full_down)
            return (gate_lin, up_lin, activation, part)

        return piece

    ffn = overlap(second_ring, [ffn_forward(slot) for slot in range(slots)])
    second_slots = second_ring.slots
    gate_slots = [item[0] for item in ffn]
    up_slots = [item[1] for item in ffn]
    act_slots = [item[2] for item in ffn]
    ffn_ring = RingScatter([item[3] for item in ffn], "row", jnp.bfloat16)

    def ffn_backward(slot):
        def piece(done):
            gate_lin, up_lin = gate_slots[slot], up_slots[slot]
            grad_activation = times_transpose(cot_slots[slot], full_down)
            sigma = jax.nn.sigmoid(gate_lin)
            grad_gate = grad_activation * up_lin * sigma * (1.0 + gate_lin * (1.0 - sigma))
            grad_up = grad_activation * gate_lin * sigma
            grad_gu = jnp.concatenate([grad_gate, grad_up], axis=1).astype(jnp.bfloat16)
            return (grad_gu, times_transpose(grad_gu, full_gu))

        return piece

    order = list(range(1, slots)) + [0]

    def first_backward(done):
        grad_down_w = contract_rows(
            jnp.concatenate(act_slots, axis=0), jnp.concatenate(cot_slots, axis=0)
        )
        return (ffn_backward(order[0])(done), grad_down_w)

    bwd = overlap(ffn_ring, [first_backward] + [ffn_backward(slot) for slot in order[1:]])
    grad_down_w = bwd[0][1]
    bwd = (bwd[0][0],) + bwd[1:]
    ffn_sum = ffn_ring.result()
    output = (middle + ffn_sum).astype(jnp.bfloat16)
    by_slot = dict(zip(order, bwd))
    grad_gu = jnp.concatenate([by_slot[slot][0] for slot in range(slots)], axis=0)
    second_ring_back = RingScatter([by_slot[slot][1] for slot in range(slots)], "row", jnp.bfloat16)
    rows_second = jnp.concatenate(second_slots, axis=0)

    def gate_up_weight_grad(_):
        return contract_rows(rows_second, grad_gu)

    (grad_gu_w,) = overlap(second_ring_back, [gate_up_weight_grad])
    grad_second = second_ring_back.result()
    down_sum = col_scatter(grad_down_w, 1)
    gu_sum = col_scatter(grad_gu_w, 0)
    grad_middle = cotangent.astype(jnp.float32) + norm_back(middle, grad_second)
    branch_chain = RingGather(grad_middle.astype(jnp.bfloat16), "row", absolute=True)
    steps = branch_chain.steps()
    down_sum = overlap(branch_chain, [lambda done: ()] * (steps - 1) + [lambda done: down_sum])[-1]
    grad_branch = branch_chain.result()
    grad_output_t = contract_rows(grad_branch, attended)
    grad_mixed = split_heads(times_transpose(grad_branch, full_output).astype(jnp.bfloat16))
    grad_q_rot, grad_k_rot, grad_values = lax.map(
        attend_backward, (queries, keys_rot, values, piece_starts, log_total, grad_mixed)
    )
    grad_qkv = jnp.concatenate(
        [
            merge_heads(unrotate(grad_q_rot, cosine, sine)),
            merge_heads(unrotate(grad_k_rot, cosine, sine)),
            merge_heads(grad_values),
        ],
        axis=1,
    ).astype(jnp.bfloat16)
    attn_sum = col_scatter(
        jnp.concatenate([contract_rows(first_rows, grad_qkv), grad_output_t], axis=1), 0
    )
    qkv_sum = attn_sum[:, : 3 * width]
    output_sum = attn_sum[:, 3 * width :].T
    grad_first = ring_reduce_scatter(times_transpose(grad_qkv, full_qkv), "row", jnp.bfloat16)
    grad_input = grad_middle + norm_back(inputs, grad_first)
    return (
        output,
        grad_input,
        qkv_sum[:, :width],
        qkv_sum[:, width : 2 * width],
        qkv_sum[:, 2 * width :],
        output_sum,
        gu_sum[:, :hidden],
        gu_sum[:, hidden:],
        down_sum,
    )


def solution(mesh):
    in_specs = (
        P(("chip", "core", "row"), None),
        P(COL, "row"),
        P(COL, "row"),
        P(COL, "row"),
        P("row", COL),
        P(COL, "row"),
        P(COL, "row"),
        P("row", COL),
        P(COL, None),
        P(("chip", "core", "row"), None),
    )
    out_specs = (
        P(("chip", "core", "row"), None),
        P(("chip", "core", "row"), None),
        P(COL, "row"),
        P(COL, "row"),
        P(COL, "row"),
        P("row", COL),
        P(COL, "row"),
        P(COL, "row"),
        P("row", COL),
    )
    devices = mesh.devices
    sub_mesh = Mesh(
        devices.reshape(devices.shape[0], devices.shape[1] // 2, 2), ("row", "chip", "core")
    )
    return jax.shard_map(
        per_device_body, mesh=sub_mesh, in_specs=in_specs, out_specs=out_specs, check_vma=False
    )
```

```python
import math

import jax
import jax.numpy as jnp
from jax import lax
from jax.sharding import Mesh, PartitionSpec as P


HD = 128
LENGTH = 1024
PIECE = 256


EPSILON = 1e-05
NEGATIVE = -1e30


def product(left, right):
    return jnp.dot(left, right, preferred_element_type=jnp.float32)


def contract_rows(left, right):
    return lax.dot_general(
        left, right, (((0,), (0,)), ((), ())), preferred_element_type=jnp.float32
    )


def times_transpose(left, right):
    return lax.dot_general(
        left, right, (((1,), (1,)), ((), ())), preferred_element_type=jnp.float32
    )


class GatherSteps:
    def __init__(self, shard, axis):
        self.axis = axis
        self.n = lax.psum(1, axis)
        self.me = lax.axis_index(axis)
        self.rows = shard.shape[0]
        buf = jnp.zeros(((3 * self.n - 2) * self.rows,) + shard.shape[1:], shard.dtype)
        self.buf = lax.dynamic_update_slice_in_dim(buf, shard, (self.me + self.n - 1) * self.rows, 0)
        self.pending = (shard, shard)
        self.step = 0

    def steps(self):
        return self.n - 1

    def send(self):
        n, step = self.n, self.step + 1
        from_left, from_right = self.pending
        from_left = lax.ppermute(from_left, self.axis, [(j, j + 1) for j in range(step - 1, n - 1)])
        from_right = lax.ppermute(from_right, self.axis, [(j, j - 1) for j in range(1, n - step + 1)])
        self.pending = (from_left, from_right)
        self.step = step

    def land(self):
        n, step, rows = self.n, self.step, self.rows
        from_left, from_right = self.pending
        self.buf = lax.dynamic_update_slice_in_dim(self.buf, from_left, (self.me - step + n - 1) * rows, 0)
        self.buf = lax.dynamic_update_slice_in_dim(self.buf, from_right, (self.me + step + n - 1) * rows, 0)

    def result(self):
        return self.buf[(self.n - 1) * self.rows : (2 * self.n - 1) * self.rows]


class ScatterSteps:
    def __init__(self, partial, axis, send_dtype):
        self.axis = axis
        self.n = lax.psum(1, axis)
        self.me = lax.axis_index(axis)
        self.rows = partial.shape[0] // self.n
        self.partial = partial
        self.send_dtype = send_dtype
        self.pending = None
        self.step = 0

    def steps(self):
        return self.n - 1

    def block(self, k):
        return lax.dynamic_slice_in_dim(
            self.partial, jnp.clip(k, 0, self.n - 1) * self.rows, self.rows, 0
        )

    def send(self):
        n, me, step = self.n, self.me, self.step + 1
        send_right = self.block(n - step + me)
        send_left = self.block(me + step - n)
        if self.pending is not None:
            send_right = send_right + self.pending[0].astype(jnp.float32)
            send_left = send_left + self.pending[1].astype(jnp.float32)
        recv_right = lax.ppermute(
            send_right.astype(self.send_dtype), self.axis, [(j, j + 1) for j in range(0, step)]
        )
        recv_left = lax.ppermute(
            send_left.astype(self.send_dtype), self.axis, [(j, j - 1) for j in range(n - step, n)]
        )
        self.pending = (recv_right, recv_left)
        self.step = step

    def land(self):
        pass

    def result(self):
        return (
            self.block(self.me)
            + self.pending[0].astype(jnp.float32)
            + self.pending[1].astype(jnp.float32)
        )


class RingGather:
    def __init__(self, shard, axis, absolute=False):
        self.axis = axis
        self.n = lax.psum(1, axis)
        self.me = lax.axis_index(axis)
        self.rows = shard.shape[0]
        self.slots = [shard]
        self.pending = shard
        self.buf = None
        if absolute:
            buf = jnp.zeros((self.n * self.rows,) + shard.shape[1:], shard.dtype)
            self.buf = self.place(buf, shard, 0)

    def place(self, buf, block, slot):
        start = lax.rem(self.me - slot + self.n, self.n) * self.rows
        return lax.dynamic_update_slice_in_dim(buf, block, start, 0)

    def steps(self):
        return self.n - 1

    def send(self):
        n = self.n
        self.pending = lax.ppermute(self.pending, self.axis, [(j, (j + 1) % n) for j in range(n)])

    def land(self):
        self.slots.append(self.pending)
        if self.buf is not None:
            self.buf = self.place(self.buf, self.pending, len(self.slots) - 1)

    def result(self):
        return self.buf


class RingScatter:
    def __init__(self, slots, axis, send_dtype):
        self.axis = axis
        self.n = lax.psum(1, axis)
        self.slots = slots
        self.send_dtype = send_dtype
        self.pending = None
        self.step = 0

    def steps(self):
        return self.n - 1

    def send(self):
        n, step = self.n, self.step + 1
        value = self.slots[step]
        if self.pending is not None:
            value = value + self.pending.astype(jnp.float32)
        self.pending = lax.ppermute(
            value.astype(self.send_dtype), self.axis, [(j, (j + 1) % n) for j in range(n)]
        )
        self.step = step

    def land(self):
        pass

    def result(self):
        return self.slots[0] + self.pending.astype(jnp.float32)


def ring_slots(partial, axis):
    n = lax.psum(1, axis)
    me = lax.axis_index(axis)
    rows = partial.shape[0] // n
    return [
        lax.dynamic_slice_in_dim(partial, lax.rem(me - slot + n, n) * rows, rows, 0)
        for slot in range(n)
    ]


def ring_all_gather(shard, axis):
    chain = RingGather(shard, axis, absolute=True)
    overlap(chain, [])
    return chain.result()


def ring_reduce_scatter(partial, axis, send_dtype):
    chain = RingScatter(ring_slots(partial, axis), axis, send_dtype)
    overlap(chain, [])
    return chain.result()


def overlap(chain, pieces):
    outputs = []
    count = chain.steps()
    for index in range(count):
        chain.send()
        if index < len(pieces):
            value = pieces[index](tuple(outputs))
            chain.pending, value = lax.optimization_barrier((chain.pending, value))
            outputs.append(value)
        else:
            chain.pending = lax.optimization_barrier(chain.pending)
        chain.land()
    for piece in pieces[count:]:
        outputs.append(piece(tuple(outputs)))
    return tuple(outputs)


COL = ("chip", "core")


def col_gather(block, axis):
    return lax.all_gather(block, COL, axis=axis, tiled=True)


def col_scatter(partial, axis):
    low_part = partial.astype(jnp.bfloat16)
    return lax.psum_scatter(low_part, COL, scatter_dimension=axis, tiled=True).astype(jnp.float32)


def layer_norm(inputs):
    center = inputs - jnp.mean(inputs, axis=-1, keepdims=True)
    spread = jnp.mean(center * center, axis=-1, keepdims=True)
    return center * lax.rsqrt(spread + EPSILON)


def norm_back(inputs, grad):
    center = inputs - jnp.mean(inputs, axis=-1, keepdims=True)
    inverse = lax.rsqrt(jnp.mean(center * center, axis=-1, keepdims=True) + EPSILON)
    normed = center * inverse
    return inverse * (
        grad
        - jnp.mean(grad, axis=-1, keepdims=True)
        - normed * jnp.mean(grad * normed, axis=-1, keepdims=True)
    )


def rope_tables():
    positions = jnp.arange(LENGTH, dtype=jnp.float32)
    freqs = jnp.power(jnp.float32(10000.0), -jnp.arange(HD // 2, dtype=jnp.float32) * (2.0 / HD))
    angles = positions[:, None] * freqs[None, :]
    return (jnp.cos(angles)[:, None, :], jnp.sin(angles)[:, None, :])


def rotate(field, cosine, sine):
    half_size = field.shape[-1] // 2
    first_half = field[..., :half_size]
    second_half = field[..., half_size:]
    return jnp.concatenate(
        [first_half * cosine - second_half * sine, second_half * cosine + first_half * sine],
        axis=-1,
    )


def unrotate(field, cosine, sine):
    half_size = field.shape[-1] // 2
    first_half = field[..., :half_size]
    second_half = field[..., half_size:]
    return jnp.concatenate(
        [first_half * cosine + second_half * sine, second_half * cosine - first_half * sine],
        axis=-1,
    )


def piece_mask(starts):
    positions = jnp.arange(LENGTH, dtype=jnp.int32)
    inside = (positions[None, :] >= starts[:, None]) & (
        positions[None, :] < starts[:, None] + PIECE
    )
    shared = jnp.any(inside[:, :, None] & inside[:, None, :], axis=0)
    causal = positions[None, :] <= positions[:, None]
    return causal | shared


def masked_scores(queries, keys_rot, starts):
    scale = 1.0 / math.sqrt(HD)
    scores = (
        jnp.einsum("qhd,khd->hqk", queries, keys_rot, preferred_element_type=jnp.float32) * scale
    )
    return jnp.where(piece_mask(starts)[None], scores, NEGATIVE)


def attend_forward(operands):
    queries, keys_rot, values, starts = operands
    scores = masked_scores(queries, keys_rot, starts)
    row_top = jnp.max(scores, axis=-1, keepdims=True)
    shifted = jnp.exp(scores - row_top)
    row_total = jnp.sum(shifted, axis=-1, keepdims=True)
    probs = (shifted / row_total).astype(jnp.bfloat16)
    mixed = jnp.einsum("hqk,khd->qhd", probs, values, preferred_element_type=jnp.float32)
    return (mixed, row_top + jnp.log(row_total))


def attend_backward(operands):
    queries, keys_rot, values, starts, log_total, grad_mixed = operands
    scale = 1.0 / math.sqrt(HD)
    scores = masked_scores(queries, keys_rot, starts)
    probs = jnp.exp(scores - log_total)
    probs_low = probs.astype(jnp.bfloat16)
    grad_values = jnp.einsum(
        "hqk,qhd->khd", probs_low, grad_mixed, preferred_element_type=jnp.float32
    )
    grad_probs = jnp.einsum("qhd,khd->hqk", grad_mixed, values, preferred_element_type=jnp.float32)
    inner = jnp.sum(probs * grad_probs, axis=-1, keepdims=True)
    grad_scores = (probs * (grad_probs - inner)).astype(jnp.bfloat16)
    grad_queries = (
        jnp.einsum("hqk,khd->qhd", grad_scores, keys_rot, preferred_element_type=jnp.float32)
        * scale
    )
    grad_keys = (
        jnp.einsum("hqk,qhd->khd", grad_scores, queries, preferred_element_type=jnp.float32) * scale
    )
    return (grad_queries, grad_keys, grad_values)


def per_device_body(
    layer_input, w_query, w_key, w_value, w_output, w_gate, w_up, w_down, piece_starts, cotangent
):
    seq_count = piece_starts.shape[0]
    group_rows = seq_count * LENGTH
    width = w_query.shape[1]
    hidden = w_gate.shape[1]
    heads_local = width // HD
    full_qkv = col_gather(jnp.concatenate([w_query, w_key, w_value], axis=1), 0)
    full_output = col_gather(w_output, 1)
    full_gu = col_gather(jnp.concatenate([w_gate, w_up], axis=1), 0)
    full_down = col_gather(w_down, 1)
    cosine, sine = rope_tables()
    inputs = layer_input.astype(jnp.float32)
    normed_first = layer_norm(inputs).astype(jnp.bfloat16)
    first_rows = ring_all_gather(normed_first, "row")

    def split_heads(matrix):
        return matrix.reshape(seq_count, LENGTH, heads_local, HD)

    def merge_heads(field):
        return field.reshape(group_rows, heads_local * HD)

    def project(_):
        qkv_lin = product(first_rows, full_qkv)
        queries = rotate(split_heads(qkv_lin[:, :width]), cosine, sine).astype(jnp.bfloat16)
        keys_rot = rotate(split_heads(qkv_lin[:, width : 2 * width]), cosine, sine).astype(
            jnp.bfloat16
        )
        values = split_heads(qkv_lin[:, 2 * width :]).astype(jnp.bfloat16)
        return dict(queries=queries, keys_rot=keys_rot, values=values)

    def attend(done):
        state = done[0]
        mixed, log_total = lax.map(
            attend_forward, (state["queries"], state["keys_rot"], state["values"], piece_starts)
        )
        return dict(mixed=mixed, log_total=log_total)

    def out_project(done):
        attended = merge_heads(done[1]["mixed"].astype(jnp.bfloat16))
        return dict(attended=attended, attn_partial=product(attended, full_output))

    cot_later, first_rows = lax.optimization_barrier((cotangent, first_rows))
    cot_ring = RingGather(cot_later, "row")
    projected, attention, mixed_out = overlap(cot_ring, [project, attend, out_project])
    cot_slots = cot_ring.slots
    queries, keys_rot = projected["queries"], projected["keys_rot"]
    values = projected["values"]
    log_total, attended = attention["log_total"], mixed_out["attended"]
    attention_sum = ring_reduce_scatter(mixed_out["attn_partial"], "row", jnp.bfloat16)
    middle = inputs + attention_sum
    normed_second = layer_norm(middle).astype(jnp.bfloat16)
    second_ring = RingGather(normed_second, "row")
    slots = second_ring.n

    def ffn_forward(slot):
        def piece(done):
            gu_lin = product(second_ring.slots[slot], full_gu)
            gate_lin = gu_lin[:, :hidden]
            up_lin = gu_lin[:, hidden:]
            activation = (jax.nn.silu(gate_lin) * up_lin).astype(jnp.bfloat16)
            part = product(activation, full_down)
            return (gate_lin, up_lin, activation, part)

        return piece

    ffn = overlap(second_ring, [ffn_forward(slot) for slot in range(slots)])
    second_slots = second_ring.slots
    gate_slots = [item[0] for item in ffn]
    up_slots = [item[1] for item in ffn]
    act_slots = [item[2] for item in ffn]
    ffn_parts = [item[3] for item in ffn]

    def ffn_backward(slot):
        gate_lin, up_lin = gate_slots[slot], up_slots[slot]
        grad_activation = times_transpose(cot_slots[slot], full_down)
        sigma = jax.nn.sigmoid(gate_lin)
        grad_gate = grad_activation * up_lin * sigma * (1.0 + gate_lin * (1.0 - sigma))
        grad_up = grad_activation * gate_lin * sigma
        grad_gu = jnp.concatenate([grad_gate, grad_up], axis=1).astype(jnp.bfloat16)
        return (grad_gu, times_transpose(grad_gu, full_gu))

    second_ring_back = RingScatter([None] * slots, "row", jnp.bfloat16)
    grad_gu_slots = [None] * slots
    order = list(range(1, slots)) + [0]
    grad_gu_slots[order[0]], second_ring_back.slots[order[0]] = ffn_backward(order[0])
    grad_down_w = None
    for index in range(second_ring_back.steps()):
        second_ring_back.send()
        slot = order[index + 1]
        value = ffn_backward(slot)
        if slot == 0:
            grad_down_w = contract_rows(
                jnp.concatenate(act_slots, axis=0), jnp.concatenate(cot_slots, axis=0)
            )
            value = value + (grad_down_w,)
        second_ring_back.pending, value = lax.optimization_barrier(
            (second_ring_back.pending, value)
        )
        grad_gu_slots[slot], second_ring_back.slots[slot] = value[0], value[1]
        if slot == 0:
            grad_down_w = value[2]
    grad_second = second_ring_back.result()
    down_sum = col_scatter(grad_down_w, 1)
    grad_gu = jnp.concatenate(grad_gu_slots, axis=0)
    rows_second = jnp.concatenate(second_slots, axis=0)
    grad_middle = cotangent.astype(jnp.float32) + norm_back(middle, grad_second)
    branch_chain = RingGather(grad_middle.astype(jnp.bfloat16), "row", absolute=True)
    steps = branch_chain.steps()

    def gate_up_weight_grad(_):
        return contract_rows(rows_second, grad_gu)

    tied = overlap(
        branch_chain, [gate_up_weight_grad] + [lambda done: ()] * (steps - 2) + [lambda done: down_sum]
    )
    grad_gu_w, down_sum = tied[0], tied[-1]
    gu_sum = col_scatter(grad_gu_w, 0)
    grad_branch = branch_chain.result()
    ffn_parts, grad_branch = lax.optimization_barrier((ffn_parts, grad_branch))
    ffn_ring = RingScatter(list(ffn_parts), "row", jnp.bfloat16)
    output_sum = col_scatter(contract_rows(attended, grad_branch), 1)
    half = heads_local // 2

    def heads_backward(lo, hi):
        def piece(done):
            grad_mixed = times_transpose(grad_branch, full_output[lo * HD : hi * HD])
            grad_mixed = grad_mixed.astype(jnp.bfloat16).reshape(seq_count, LENGTH, hi - lo, HD)
            return lax.map(
                attend_backward,
                (
                    queries[:, :, lo:hi],
                    keys_rot[:, :, lo:hi],
                    values[:, :, lo:hi],
                    piece_starts,
                    log_total[:, lo:hi],
                    grad_mixed,
                ),
            )

        return piece

    def finish(done):
        parts = [jnp.concatenate([a[k] for a in done], axis=2) for k in range(3)]
        grad_q_rot, grad_k_rot, grad_values = parts
        grad_qkv = jnp.concatenate(
            [
                merge_heads(unrotate(grad_q_rot, cosine, sine)),
                merge_heads(unrotate(grad_k_rot, cosine, sine)),
                merge_heads(grad_values),
            ],
            axis=1,
        ).astype(jnp.bfloat16)
        return (grad_qkv, times_transpose(grad_qkv, full_qkv))

    pieces = [heads_backward(0, half), heads_backward(half, heads_local), finish]
    grad_qkv, first_partial = overlap(ffn_ring, pieces)[-1]
    ffn_sum = ffn_ring.result()
    output = (middle + ffn_sum).astype(jnp.bfloat16)
    qkv_sum = col_scatter(contract_rows(first_rows, grad_qkv), 0)
    first_partial, gu_sum = lax.optimization_barrier((first_partial, gu_sum))
    grad_first = ring_reduce_scatter(first_partial, "row", jnp.bfloat16)
    grad_input = grad_middle + norm_back(inputs, grad_first)
    return (
        output,
        grad_input,
        qkv_sum[:, :width],
        qkv_sum[:, width : 2 * width],
        qkv_sum[:, 2 * width :],
        output_sum,
        gu_sum[:, :hidden],
        gu_sum[:, hidden:],
        down_sum,
    )


def solution(mesh):
    in_specs = (
        P(("chip", "core", "row"), None),
        P(COL, "row"),
        P(COL, "row"),
        P(COL, "row"),
        P("row", COL),
        P(COL, "row"),
        P(COL, "row"),
        P("row", COL),
        P(COL, None),
        P(("chip", "core", "row"), None),
    )
    out_specs = (
        P(("chip", "core", "row"), None),
        P(("chip", "core", "row"), None),
        P(COL, "row"),
        P(COL, "row"),
        P(COL, "row"),
        P("row", COL),
        P(COL, "row"),
        P(COL, "row"),
        P("row", COL),
    )
    devices = mesh.devices
    sub_mesh = Mesh(
        devices.reshape(devices.shape[0], devices.shape[1] // 2, 2), ("row", "chip", "core")
    )
    return jax.shard_map(
        per_device_body, mesh=sub_mesh, in_specs=in_specs, out_specs=out_specs, check_vma=False
    )
```

```python
import math

import jax
import jax.numpy as jnp
from jax import lax
from jax.sharding import Mesh, PartitionSpec as P


HD = 128
LENGTH = 1024
PIECE = 256


EPSILON = 1e-05
NEGATIVE = -1e30


def product(left, right):
    return jnp.dot(left, right, preferred_element_type=jnp.float32)


def contract_rows(left, right):
    return lax.dot_general(
        left, right, (((0,), (0,)), ((), ())), preferred_element_type=jnp.float32
    )


def times_transpose(left, right):
    return lax.dot_general(
        left, right, (((1,), (1,)), ((), ())), preferred_element_type=jnp.float32
    )


class GatherSteps:
    def __init__(self, shard, axis):
        self.axis = axis
        self.n = lax.psum(1, axis)
        self.me = lax.axis_index(axis)
        self.rows = shard.shape[0]
        buf = jnp.zeros(((3 * self.n - 2) * self.rows,) + shard.shape[1:], shard.dtype)
        self.buf = lax.dynamic_update_slice_in_dim(buf, shard, (self.me + self.n - 1) * self.rows, 0)
        self.pending = (shard, shard)
        self.step = 0

    def steps(self):
        return self.n - 1

    def send(self):
        n, step = self.n, self.step + 1
        from_left, from_right = self.pending
        from_left = lax.ppermute(from_left, self.axis, [(j, j + 1) for j in range(step - 1, n - 1)])
        from_right = lax.ppermute(from_right, self.axis, [(j, j - 1) for j in range(1, n - step + 1)])
        self.pending = (from_left, from_right)
        self.step = step

    def land(self):
        n, step, rows = self.n, self.step, self.rows
        from_left, from_right = self.pending
        self.buf = lax.dynamic_update_slice_in_dim(self.buf, from_left, (self.me - step + n - 1) * rows, 0)
        self.buf = lax.dynamic_update_slice_in_dim(self.buf, from_right, (self.me + step + n - 1) * rows, 0)

    def result(self):
        return self.buf[(self.n - 1) * self.rows : (2 * self.n - 1) * self.rows]


class ScatterSteps:
    def __init__(self, partial, axis, send_dtype):
        self.axis = axis
        self.n = lax.psum(1, axis)
        self.me = lax.axis_index(axis)
        self.rows = partial.shape[0] // self.n
        self.partial = partial
        self.send_dtype = send_dtype
        self.pending = None
        self.step = 0

    def steps(self):
        return self.n - 1

    def block(self, k):
        return lax.dynamic_slice_in_dim(
            self.partial, jnp.clip(k, 0, self.n - 1) * self.rows, self.rows, 0
        )

    def send(self):
        n, me, step = self.n, self.me, self.step + 1
        send_right = self.block(n - step + me)
        send_left = self.block(me + step - n)
        if self.pending is not None:
            send_right = send_right + self.pending[0].astype(jnp.float32)
            send_left = send_left + self.pending[1].astype(jnp.float32)
        recv_right = lax.ppermute(
            send_right.astype(self.send_dtype), self.axis, [(j, j + 1) for j in range(0, step)]
        )
        recv_left = lax.ppermute(
            send_left.astype(self.send_dtype), self.axis, [(j, j - 1) for j in range(n - step, n)]
        )
        self.pending = (recv_right, recv_left)
        self.step = step

    def land(self):
        pass

    def result(self):
        return (
            self.block(self.me)
            + self.pending[0].astype(jnp.float32)
            + self.pending[1].astype(jnp.float32)
        )


class RingGather:
    def __init__(self, shard, axis, absolute=False):
        self.axis = axis
        self.n = lax.psum(1, axis)
        self.me = lax.axis_index(axis)
        self.rows = shard.shape[0]
        self.slots = [shard]
        self.pending = shard
        self.buf = None
        if absolute:
            buf = jnp.zeros((self.n * self.rows,) + shard.shape[1:], shard.dtype)
            self.buf = self.place(buf, shard, 0)

    def place(self, buf, block, slot):
        start = lax.rem(self.me - slot + self.n, self.n) * self.rows
        return lax.dynamic_update_slice_in_dim(buf, block, start, 0)

    def steps(self):
        return self.n - 1

    def send(self):
        n = self.n
        self.pending = lax.ppermute(self.pending, self.axis, [(j, (j + 1) % n) for j in range(n)])

    def land(self):
        self.slots.append(self.pending)
        if self.buf is not None:
            self.buf = self.place(self.buf, self.pending, len(self.slots) - 1)

    def result(self):
        return self.buf


class RingScatter:
    def __init__(self, slots, axis, send_dtype):
        self.axis = axis
        self.n = lax.psum(1, axis)
        self.slots = slots
        self.send_dtype = send_dtype
        self.pending = None
        self.step = 0

    def steps(self):
        return self.n - 1

    def send(self):
        n, step = self.n, self.step + 1
        value = self.slots[step]
        if self.pending is not None:
            value = value + self.pending.astype(jnp.float32)
        self.pending = lax.ppermute(
            value.astype(self.send_dtype), self.axis, [(j, (j + 1) % n) for j in range(n)]
        )
        self.step = step

    def land(self):
        pass

    def result(self):
        return self.slots[0] + self.pending.astype(jnp.float32)


def ring_slots(partial, axis):
    n = lax.psum(1, axis)
    me = lax.axis_index(axis)
    rows = partial.shape[0] // n
    return [
        lax.dynamic_slice_in_dim(partial, lax.rem(me - slot + n, n) * rows, rows, 0)
        for slot in range(n)
    ]


def ring_all_gather(shard, axis):
    chain = RingGather(shard, axis, absolute=True)
    overlap(chain, [])
    return chain.result()


def ring_reduce_scatter(partial, axis, send_dtype):
    chain = RingScatter(ring_slots(partial, axis), axis, send_dtype)
    overlap(chain, [])
    return chain.result()


def overlap(chain, pieces):
    outputs = []
    count = chain.steps()
    for index in range(count):
        chain.send()
        if index < len(pieces):
            value = pieces[index](tuple(outputs))
            chain.pending, value = lax.optimization_barrier((chain.pending, value))
            outputs.append(value)
        else:
            chain.pending = lax.optimization_barrier(chain.pending)
        chain.land()
    for piece in pieces[count:]:
        outputs.append(piece(tuple(outputs)))
    return tuple(outputs)


COL = ("chip", "core")


def col_gather(block, axis):
    return lax.all_gather(block, COL, axis=axis, tiled=True)


def col_scatter(partial, axis):
    low_part = partial.astype(jnp.bfloat16)
    return lax.psum_scatter(low_part, COL, scatter_dimension=axis, tiled=True).astype(jnp.float32)


def layer_norm(inputs):
    center = inputs - jnp.mean(inputs, axis=-1, keepdims=True)
    spread = jnp.mean(center * center, axis=-1, keepdims=True)
    return center * lax.rsqrt(spread + EPSILON)


def norm_back(inputs, grad):
    center = inputs - jnp.mean(inputs, axis=-1, keepdims=True)
    inverse = lax.rsqrt(jnp.mean(center * center, axis=-1, keepdims=True) + EPSILON)
    normed = center * inverse
    return inverse * (
        grad
        - jnp.mean(grad, axis=-1, keepdims=True)
        - normed * jnp.mean(grad * normed, axis=-1, keepdims=True)
    )


def rope_tables():
    positions = jnp.arange(LENGTH, dtype=jnp.float32)
    freqs = jnp.power(jnp.float32(10000.0), -jnp.arange(HD // 2, dtype=jnp.float32) * (2.0 / HD))
    angles = positions[:, None] * freqs[None, :]
    return (jnp.cos(angles)[:, None, :], jnp.sin(angles)[:, None, :])


def rotate(field, cosine, sine):
    half_size = field.shape[-1] // 2
    first_half = field[..., :half_size]
    second_half = field[..., half_size:]
    return jnp.concatenate(
        [first_half * cosine - second_half * sine, second_half * cosine + first_half * sine],
        axis=-1,
    )


def unrotate(field, cosine, sine):
    half_size = field.shape[-1] // 2
    first_half = field[..., :half_size]
    second_half = field[..., half_size:]
    return jnp.concatenate(
        [first_half * cosine + second_half * sine, second_half * cosine - first_half * sine],
        axis=-1,
    )


def piece_mask(starts):
    positions = jnp.arange(LENGTH, dtype=jnp.int32)
    inside = (positions[None, :] >= starts[:, None]) & (
        positions[None, :] < starts[:, None] + PIECE
    )
    shared = jnp.any(inside[:, :, None] & inside[:, None, :], axis=0)
    causal = positions[None, :] <= positions[:, None]
    return causal | shared


def masked_scores(queries, keys_rot, starts):
    scale = 1.0 / math.sqrt(HD)
    scores = (
        jnp.einsum("qhd,khd->hqk", queries, keys_rot, preferred_element_type=jnp.float32) * scale
    )
    return jnp.where(piece_mask(starts)[None], scores, NEGATIVE)


def attend_forward(operands):
    queries, keys_rot, values, starts = operands
    scores = masked_scores(queries, keys_rot, starts)
    row_top = jnp.max(scores, axis=-1, keepdims=True)
    shifted = jnp.exp(scores - row_top)
    row_total = jnp.sum(shifted, axis=-1, keepdims=True)
    probs = (shifted / row_total).astype(jnp.bfloat16)
    mixed = jnp.einsum("hqk,khd->qhd", probs, values, preferred_element_type=jnp.float32)
    return (mixed, row_top + jnp.log(row_total))


def attend_backward(operands):
    queries, keys_rot, values, starts, log_total, grad_mixed = operands
    scale = 1.0 / math.sqrt(HD)
    scores = masked_scores(queries, keys_rot, starts)
    probs = jnp.exp(scores - log_total)
    probs_low = probs.astype(jnp.bfloat16)
    grad_values = jnp.einsum(
        "hqk,qhd->khd", probs_low, grad_mixed, preferred_element_type=jnp.float32
    )
    grad_probs = jnp.einsum("qhd,khd->hqk", grad_mixed, values, preferred_element_type=jnp.float32)
    inner = jnp.sum(probs * grad_probs, axis=-1, keepdims=True)
    grad_scores = (probs * (grad_probs - inner)).astype(jnp.bfloat16)
    grad_queries = (
        jnp.einsum("hqk,khd->qhd", grad_scores, keys_rot, preferred_element_type=jnp.float32)
        * scale
    )
    grad_keys = (
        jnp.einsum("hqk,qhd->khd", grad_scores, queries, preferred_element_type=jnp.float32) * scale
    )
    return (grad_queries, grad_keys, grad_values)


def per_device_body(
    layer_input, w_query, w_key, w_value, w_output, w_gate, w_up, w_down, piece_starts, cotangent
):
    seq_count = piece_starts.shape[0]
    group_rows = seq_count * LENGTH
    width = w_query.shape[1]
    hidden = w_gate.shape[1]
    heads_local = width // HD
    full_qkv = col_gather(jnp.concatenate([w_query, w_key, w_value], axis=1), 0)
    full_output = col_gather(w_output, 1)
    full_gu = col_gather(jnp.concatenate([w_gate, w_up], axis=1), 0)
    full_down = col_gather(w_down, 1)
    cosine, sine = rope_tables()
    inputs = layer_input.astype(jnp.float32)
    normed_first = layer_norm(inputs).astype(jnp.bfloat16)
    first_rows = ring_all_gather(normed_first, "row")

    def split_heads(matrix):
        return matrix.reshape(seq_count, LENGTH, heads_local, HD)

    def merge_heads(field):
        return field.reshape(group_rows, heads_local * HD)

    def project(_):
        qkv_lin = product(first_rows, full_qkv)
        queries = rotate(split_heads(qkv_lin[:, :width]), cosine, sine).astype(jnp.bfloat16)
        keys_rot = rotate(split_heads(qkv_lin[:, width : 2 * width]), cosine, sine).astype(
            jnp.bfloat16
        )
        values = split_heads(qkv_lin[:, 2 * width :]).astype(jnp.bfloat16)
        return dict(queries=queries, keys_rot=keys_rot, values=values)

    def attend(done):
        state = done[0]
        mixed, log_total = lax.map(
            attend_forward, (state["queries"], state["keys_rot"], state["values"], piece_starts)
        )
        return dict(mixed=mixed, log_total=log_total)

    def out_project(done):
        attended = merge_heads(done[1]["mixed"].astype(jnp.bfloat16))
        return dict(attended=attended, attn_partial=product(attended, full_output))

    cot_later, first_rows = lax.optimization_barrier((cotangent, first_rows))
    cot_ring = RingGather(cot_later, "row")
    projected, attention, mixed_out = overlap(cot_ring, [project, attend, out_project])
    cot_slots = cot_ring.slots
    queries, keys_rot = projected["queries"], projected["keys_rot"]
    values = projected["values"]
    log_total, attended = attention["log_total"], mixed_out["attended"]
    attn_ring = RingScatter(ring_slots(mixed_out["attn_partial"], "row"), "row", jnp.bfloat16)
    cot_count = len(cot_slots)
    per_step = -(-cot_count // attn_ring.steps())

    def cot_grads(index):
        def piece(done):
            chosen = cot_slots[index * per_step : (index + 1) * per_step]
            return tuple(times_transpose(block, full_down) for block in chosen)

        return piece

    grad_act_parts = overlap(attn_ring, [cot_grads(index) for index in range(attn_ring.steps())])
    grad_act_slots = [block for part in grad_act_parts for block in part]
    attention_sum = attn_ring.result()
    middle = inputs + attention_sum
    normed_second = layer_norm(middle).astype(jnp.bfloat16)
    second_ring = RingGather(normed_second, "row")
    slots = second_ring.n

    def ffn_forward(slot):
        def piece(done):
            gu_lin = product(second_ring.slots[slot], full_gu)
            gate_lin = gu_lin[:, :hidden]
            up_lin = gu_lin[:, hidden:]
            activation = (jax.nn.silu(gate_lin) * up_lin).astype(jnp.bfloat16)
            part = product(activation, full_down)
            return (gate_lin, up_lin, activation, part)

        return piece

    ffn = overlap(second_ring, [ffn_forward(slot) for slot in range(slots)])
    second_slots = second_ring.slots
    gate_slots = [item[0] for item in ffn]
    up_slots = [item[1] for item in ffn]
    act_slots = [item[2] for item in ffn]
    ffn_parts = [item[3] for item in ffn]

    def ffn_backward(slot):
        gate_lin, up_lin = gate_slots[slot], up_slots[slot]
        grad_activation = grad_act_slots[slot]
        sigma = jax.nn.sigmoid(gate_lin)
        grad_gate = grad_activation * up_lin * sigma * (1.0 + gate_lin * (1.0 - sigma))
        grad_up = grad_activation * gate_lin * sigma
        grad_gu = jnp.concatenate([grad_gate, grad_up], axis=1).astype(jnp.bfloat16)
        return (grad_gu, times_transpose(grad_gu, full_gu))

    second_ring_back = RingScatter([None] * slots, "row", jnp.bfloat16)
    grad_gu_slots = [None] * slots
    order = list(range(1, slots)) + [0]
    grad_gu_slots[order[0]], second_ring_back.slots[order[0]] = ffn_backward(order[0])
    grad_down_w = None
    for index in range(second_ring_back.steps()):
        second_ring_back.send()
        slot = order[index + 1]
        value = ffn_backward(slot)
        if slot == 0:
            grad_down_w = contract_rows(
                jnp.concatenate(act_slots, axis=0), jnp.concatenate(cot_slots, axis=0)
            )
            value = value + (grad_down_w,)
        second_ring_back.pending, value = lax.optimization_barrier(
            (second_ring_back.pending, value)
        )
        grad_gu_slots[slot], second_ring_back.slots[slot] = value[0], value[1]
        if slot == 0:
            grad_down_w = value[2]
    grad_second = second_ring_back.result()
    down_sum = col_scatter(grad_down_w, 1)
    grad_gu = jnp.concatenate(grad_gu_slots, axis=0)
    rows_second = jnp.concatenate(second_slots, axis=0)
    grad_middle = cotangent.astype(jnp.float32) + norm_back(middle, grad_second)
    branch_chain = RingGather(grad_middle.astype(jnp.bfloat16), "row", absolute=True)
    steps = branch_chain.steps()

    def gate_up_weight_grad(_):
        return contract_rows(rows_second, grad_gu)

    tied = overlap(
        branch_chain, [gate_up_weight_grad] + [lambda done: ()] * (steps - 2) + [lambda done: down_sum]
    )
    grad_gu_w, down_sum = tied[0], tied[-1]
    gu_sum = col_scatter(grad_gu_w, 0)
    grad_branch = branch_chain.result()
    ffn_parts, grad_branch = lax.optimization_barrier((ffn_parts, grad_branch))
    ffn_ring = RingScatter(list(ffn_parts), "row", jnp.bfloat16)
    output_sum = col_scatter(contract_rows(attended, grad_branch), 1)
    half = heads_local // 2

    def heads_backward(lo, hi):
        def piece(done):
            grad_mixed = times_transpose(grad_branch, full_output[lo * HD : hi * HD])
            grad_mixed = grad_mixed.astype(jnp.bfloat16).reshape(seq_count, LENGTH, hi - lo, HD)
            return lax.map(
                attend_backward,
                (
                    queries[:, :, lo:hi],
                    keys_rot[:, :, lo:hi],
                    values[:, :, lo:hi],
                    piece_starts,
                    log_total[:, lo:hi],
                    grad_mixed,
                ),
            )

        return piece

    def finish(done):
        parts = [jnp.concatenate([a[k] for a in done], axis=2) for k in range(3)]
        grad_q_rot, grad_k_rot, grad_values = parts
        grad_qkv = jnp.concatenate(
            [
                merge_heads(unrotate(grad_q_rot, cosine, sine)),
                merge_heads(unrotate(grad_k_rot, cosine, sine)),
                merge_heads(grad_values),
            ],
            axis=1,
        ).astype(jnp.bfloat16)
        return (grad_qkv, times_transpose(grad_qkv, full_qkv))

    pieces = [heads_backward(0, half), heads_backward(half, heads_local), finish]
    grad_qkv, first_partial = overlap(ffn_ring, pieces)[-1]
    ffn_sum = ffn_ring.result()
    output = (middle + ffn_sum).astype(jnp.bfloat16)
    qkv_sum = col_scatter(contract_rows(first_rows, grad_qkv), 0)
    first_partial, gu_sum = lax.optimization_barrier((first_partial, gu_sum))
    grad_first = ring_reduce_scatter(first_partial, "row", jnp.bfloat16)
    grad_input = grad_middle + norm_back(inputs, grad_first)
    return (
        output,
        grad_input,
        qkv_sum[:, :width],
        qkv_sum[:, width : 2 * width],
        qkv_sum[:, 2 * width :],
        output_sum,
        gu_sum[:, :hidden],
        gu_sum[:, hidden:],
        down_sum,
    )


def solution(mesh):
    in_specs = (
        P(("chip", "core", "row"), None),
        P(COL, "row"),
        P(COL, "row"),
        P(COL, "row"),
        P("row", COL),
        P(COL, "row"),
        P(COL, "row"),
        P("row", COL),
        P(COL, None),
        P(("chip", "core", "row"), None),
    )
    out_specs = (
        P(("chip", "core", "row"), None),
        P(("chip", "core", "row"), None),
        P(COL, "row"),
        P(COL, "row"),
        P(COL, "row"),
        P("row", COL),
        P(COL, "row"),
        P(COL, "row"),
        P("row", COL),
    )
    devices = mesh.devices
    sub_mesh = Mesh(
        devices.reshape(devices.shape[0], devices.shape[1] // 2, 2), ("row", "chip", "core")
    )
    return jax.shard_map(
        per_device_body, mesh=sub_mesh, in_specs=in_specs, out_specs=out_specs, check_vma=False
    )
```

```python
import math

import jax
import jax.numpy as jnp
from jax import lax
from jax.sharding import Mesh, PartitionSpec as P


HD = 128
LENGTH = 1024
PIECE = 256


EPSILON = 1e-05
NEGATIVE = -1e30


def product(left, right):
    return jnp.dot(left, right, preferred_element_type=jnp.float32)


def contract_rows(left, right):
    return lax.dot_general(
        left, right, (((0,), (0,)), ((), ())), preferred_element_type=jnp.float32
    )


def times_transpose(left, right):
    return lax.dot_general(
        left, right, (((1,), (1,)), ((), ())), preferred_element_type=jnp.float32
    )


class GatherSteps:
    def __init__(self, shard, axis):
        self.axis = axis
        self.n = lax.psum(1, axis)
        self.me = lax.axis_index(axis)
        self.rows = shard.shape[0]
        buf = jnp.zeros(((3 * self.n - 2) * self.rows,) + shard.shape[1:], shard.dtype)
        self.buf = lax.dynamic_update_slice_in_dim(buf, shard, (self.me + self.n - 1) * self.rows, 0)
        self.pending = (shard, shard)
        self.step = 0

    def steps(self):
        return self.n - 1

    def send(self):
        n, step = self.n, self.step + 1
        from_left, from_right = self.pending
        from_left = lax.ppermute(from_left, self.axis, [(j, j + 1) for j in range(step - 1, n - 1)])
        from_right = lax.ppermute(from_right, self.axis, [(j, j - 1) for j in range(1, n - step + 1)])
        self.pending = (from_left, from_right)
        self.step = step

    def land(self):
        n, step, rows = self.n, self.step, self.rows
        from_left, from_right = self.pending
        self.buf = lax.dynamic_update_slice_in_dim(self.buf, from_left, (self.me - step + n - 1) * rows, 0)
        self.buf = lax.dynamic_update_slice_in_dim(self.buf, from_right, (self.me + step + n - 1) * rows, 0)

    def result(self):
        return self.buf[(self.n - 1) * self.rows : (2 * self.n - 1) * self.rows]


class ScatterSteps:
    def __init__(self, partial, axis, send_dtype):
        self.axis = axis
        self.n = lax.psum(1, axis)
        self.me = lax.axis_index(axis)
        self.rows = partial.shape[0] // self.n
        self.partial = partial
        self.send_dtype = send_dtype
        self.pending = None
        self.step = 0

    def steps(self):
        return self.n - 1

    def block(self, k):
        return lax.dynamic_slice_in_dim(
            self.partial, jnp.clip(k, 0, self.n - 1) * self.rows, self.rows, 0
        )

    def send(self):
        n, me, step = self.n, self.me, self.step + 1
        send_right = self.block(n - step + me)
        send_left = self.block(me + step - n)
        if self.pending is not None:
            send_right = send_right + self.pending[0].astype(jnp.float32)
            send_left = send_left + self.pending[1].astype(jnp.float32)
        recv_right = lax.ppermute(
            send_right.astype(self.send_dtype), self.axis, [(j, j + 1) for j in range(0, step)]
        )
        recv_left = lax.ppermute(
            send_left.astype(self.send_dtype), self.axis, [(j, j - 1) for j in range(n - step, n)]
        )
        self.pending = (recv_right, recv_left)
        self.step = step

    def land(self):
        pass

    def result(self):
        return (
            self.block(self.me)
            + self.pending[0].astype(jnp.float32)
            + self.pending[1].astype(jnp.float32)
        )


class RingGather:
    def __init__(self, shard, axis, absolute=False):
        self.axis = axis
        self.n = lax.psum(1, axis)
        self.me = lax.axis_index(axis)
        self.rows = shard.shape[0]
        self.slots = [shard]
        self.pending = shard
        self.buf = None
        if absolute:
            buf = jnp.zeros((self.n * self.rows,) + shard.shape[1:], shard.dtype)
            self.buf = self.place(buf, shard, 0)

    def place(self, buf, block, slot):
        start = lax.rem(self.me - slot + self.n, self.n) * self.rows
        return lax.dynamic_update_slice_in_dim(buf, block, start, 0)

    def steps(self):
        return self.n - 1

    def send(self):
        n = self.n
        self.pending = lax.ppermute(self.pending, self.axis, [(j, (j + 1) % n) for j in range(n)])

    def land(self):
        self.slots.append(self.pending)
        if self.buf is not None:
            self.buf = self.place(self.buf, self.pending, len(self.slots) - 1)

    def result(self):
        return self.buf


class RingScatter:
    def __init__(self, slots, axis, send_dtype):
        self.axis = axis
        self.n = lax.psum(1, axis)
        self.slots = slots
        self.send_dtype = send_dtype
        self.pending = None
        self.step = 0

    def steps(self):
        return self.n - 1

    def send(self):
        n, step = self.n, self.step + 1
        value = self.slots[step]
        if self.pending is not None:
            value = value + self.pending.astype(jnp.float32)
        self.pending = lax.ppermute(
            value.astype(self.send_dtype), self.axis, [(j, (j + 1) % n) for j in range(n)]
        )
        self.step = step

    def land(self):
        pass

    def result(self):
        return self.slots[0] + self.pending.astype(jnp.float32)


def ring_slots(partial, axis):
    n = lax.psum(1, axis)
    me = lax.axis_index(axis)
    rows = partial.shape[0] // n
    return [
        lax.dynamic_slice_in_dim(partial, lax.rem(me - slot + n, n) * rows, rows, 0)
        for slot in range(n)
    ]


def ring_all_gather(shard, axis):
    chain = RingGather(shard, axis, absolute=True)
    overlap(chain, [])
    return chain.result()


def ring_reduce_scatter(partial, axis, send_dtype):
    chain = RingScatter(ring_slots(partial, axis), axis, send_dtype)
    overlap(chain, [])
    return chain.result()


def overlap(chain, pieces):
    outputs = []
    count = chain.steps()
    for index in range(count):
        chain.send()
        if index < len(pieces):
            value = pieces[index](tuple(outputs))
            chain.pending, value = lax.optimization_barrier((chain.pending, value))
            outputs.append(value)
        else:
            chain.pending = lax.optimization_barrier(chain.pending)
        chain.land()
    for piece in pieces[count:]:
        outputs.append(piece(tuple(outputs)))
    return tuple(outputs)


COL = ("chip", "core")


def col_gather(block, axis):
    return lax.all_gather(block, COL, axis=axis, tiled=True)


def col_scatter(partial, axis):
    low_part = partial.astype(jnp.bfloat16)
    return lax.psum_scatter(low_part, COL, scatter_dimension=axis, tiled=True).astype(jnp.float32)


def layer_norm(inputs):
    center = inputs - jnp.mean(inputs, axis=-1, keepdims=True)
    spread = jnp.mean(center * center, axis=-1, keepdims=True)
    return center * lax.rsqrt(spread + EPSILON)


def norm_back(inputs, grad):
    center = inputs - jnp.mean(inputs, axis=-1, keepdims=True)
    inverse = lax.rsqrt(jnp.mean(center * center, axis=-1, keepdims=True) + EPSILON)
    normed = center * inverse
    return inverse * (
        grad
        - jnp.mean(grad, axis=-1, keepdims=True)
        - normed * jnp.mean(grad * normed, axis=-1, keepdims=True)
    )


def rope_tables():
    positions = jnp.arange(LENGTH, dtype=jnp.float32)
    freqs = jnp.power(jnp.float32(10000.0), -jnp.arange(HD // 2, dtype=jnp.float32) * (2.0 / HD))
    angles = positions[:, None] * freqs[None, :]
    return (jnp.cos(angles)[:, None, :], jnp.sin(angles)[:, None, :])


def rotate(field, cosine, sine):
    half_size = field.shape[-1] // 2
    first_half = field[..., :half_size]
    second_half = field[..., half_size:]
    return jnp.concatenate(
        [first_half * cosine - second_half * sine, second_half * cosine + first_half * sine],
        axis=-1,
    )


def unrotate(field, cosine, sine):
    half_size = field.shape[-1] // 2
    first_half = field[..., :half_size]
    second_half = field[..., half_size:]
    return jnp.concatenate(
        [first_half * cosine + second_half * sine, second_half * cosine - first_half * sine],
        axis=-1,
    )


def piece_mask(starts):
    positions = jnp.arange(LENGTH, dtype=jnp.int32)
    inside = (positions[None, :] >= starts[:, None]) & (
        positions[None, :] < starts[:, None] + PIECE
    )
    shared = jnp.any(inside[:, :, None] & inside[:, None, :], axis=0)
    causal = positions[None, :] <= positions[:, None]
    return causal | shared


def masked_scores(queries, keys_rot, starts):
    scale = 1.0 / math.sqrt(HD)
    scores = (
        jnp.einsum("qhd,khd->hqk", queries, keys_rot, preferred_element_type=jnp.float32) * scale
    )
    return jnp.where(piece_mask(starts)[None], scores, NEGATIVE)


def attend_forward(operands):
    queries, keys_rot, values, starts = operands
    scores = masked_scores(queries, keys_rot, starts)
    row_top = jnp.max(scores, axis=-1, keepdims=True)
    shifted = jnp.exp(scores - row_top)
    row_total = jnp.sum(shifted, axis=-1, keepdims=True)
    probs = (shifted / row_total).astype(jnp.bfloat16)
    mixed = jnp.einsum("hqk,khd->qhd", probs, values, preferred_element_type=jnp.float32)
    return (mixed, row_top + jnp.log(row_total))


def attend_backward(operands):
    queries, keys_rot, values, starts, log_total, grad_mixed = operands
    scale = 1.0 / math.sqrt(HD)
    scores = masked_scores(queries, keys_rot, starts)
    probs = jnp.exp(scores - log_total)
    probs_low = probs.astype(jnp.bfloat16)
    grad_values = jnp.einsum(
        "hqk,qhd->khd", probs_low, grad_mixed, preferred_element_type=jnp.float32
    )
    grad_probs = jnp.einsum("qhd,khd->hqk", grad_mixed, values, preferred_element_type=jnp.float32)
    inner = jnp.sum(probs * grad_probs, axis=-1, keepdims=True)
    grad_scores = (probs * (grad_probs - inner)).astype(jnp.bfloat16)
    grad_queries = (
        jnp.einsum("hqk,khd->qhd", grad_scores, keys_rot, preferred_element_type=jnp.float32)
        * scale
    )
    grad_keys = (
        jnp.einsum("hqk,qhd->khd", grad_scores, queries, preferred_element_type=jnp.float32) * scale
    )
    return (grad_queries, grad_keys, grad_values)


def per_device_body(
    layer_input, w_query, w_key, w_value, w_output, w_gate, w_up, w_down, piece_starts, cotangent
):
    seq_count = piece_starts.shape[0]
    group_rows = seq_count * LENGTH
    width = w_query.shape[1]
    hidden = w_gate.shape[1]
    heads_local = width // HD
    full_qkv = col_gather(jnp.concatenate([w_query, w_key, w_value], axis=1), 0)
    full_output = col_gather(w_output, 1)
    full_gu = col_gather(jnp.concatenate([w_gate, w_up], axis=1), 0)
    full_down = col_gather(w_down, 1)
    cosine, sine = rope_tables()
    inputs = layer_input.astype(jnp.float32)
    normed_first = layer_norm(inputs).astype(jnp.bfloat16)
    first_rows = ring_all_gather(normed_first, "row")

    def split_heads(matrix):
        return matrix.reshape(seq_count, LENGTH, heads_local, HD)

    def merge_heads(field):
        return field.reshape(group_rows, heads_local * HD)

    def project(_):
        qkv_lin = product(first_rows, full_qkv)
        queries = rotate(split_heads(qkv_lin[:, :width]), cosine, sine).astype(jnp.bfloat16)
        keys_rot = rotate(split_heads(qkv_lin[:, width : 2 * width]), cosine, sine).astype(
            jnp.bfloat16
        )
        values = split_heads(qkv_lin[:, 2 * width :]).astype(jnp.bfloat16)
        return dict(queries=queries, keys_rot=keys_rot, values=values)

    def attend(done):
        state = done[0]
        mixed, log_total = lax.map(
            attend_forward, (state["queries"], state["keys_rot"], state["values"], piece_starts)
        )
        return dict(mixed=mixed, log_total=log_total)

    def out_project(done):
        attended = merge_heads(done[1]["mixed"].astype(jnp.bfloat16))
        return dict(attended=attended, attn_partial=product(attended, full_output))

    cot_later, first_rows = lax.optimization_barrier((cotangent, first_rows))
    cot_ring = RingGather(cot_later, "row")
    projected, attention, mixed_out = overlap(cot_ring, [project, attend, out_project])
    cot_slots = cot_ring.slots
    queries, keys_rot = projected["queries"], projected["keys_rot"]
    values = projected["values"]
    log_total, attended = attention["log_total"], mixed_out["attended"]
    attn_ring = RingScatter(ring_slots(mixed_out["attn_partial"], "row"), "row", jnp.bfloat16)
    cot_count = len(cot_slots)
    per_step = -(-cot_count // attn_ring.steps())

    def cot_grads(index):
        def piece(done):
            chosen = cot_slots[index * per_step : (index + 1) * per_step]
            return tuple(times_transpose(block, full_down) for block in chosen)

        return piece

    grad_act_parts = overlap(attn_ring, [cot_grads(index) for index in range(attn_ring.steps())])
    grad_act_slots = [block for part in grad_act_parts for block in part]
    attention_sum = attn_ring.result()
    middle = inputs + attention_sum
    normed_second = layer_norm(middle).astype(jnp.bfloat16)
    second_ring = RingGather(normed_second, "row")
    slots = second_ring.n

    def ffn_forward(slot):
        def piece(done):
            gu_lin = product(second_ring.slots[slot], full_gu)
            gate_lin = gu_lin[:, :hidden]
            up_lin = gu_lin[:, hidden:]
            activation = (jax.nn.silu(gate_lin) * up_lin).astype(jnp.bfloat16)
            part = product(activation, full_down)
            return (gate_lin, up_lin, activation, part)

        return piece

    ffn = overlap(second_ring, [ffn_forward(slot) for slot in range(slots)])
    second_slots = second_ring.slots
    gate_slots = [item[0] for item in ffn]
    up_slots = [item[1] for item in ffn]
    act_slots = [item[2] for item in ffn]
    ffn_parts = [item[3] for item in ffn]

    def ffn_backward(slot):
        gate_lin, up_lin = gate_slots[slot], up_slots[slot]
        grad_activation = grad_act_slots[slot]
        sigma = jax.nn.sigmoid(gate_lin)
        grad_gate = grad_activation * up_lin * sigma * (1.0 + gate_lin * (1.0 - sigma))
        grad_up = grad_activation * gate_lin * sigma
        grad_gu = jnp.concatenate([grad_gate, grad_up], axis=1).astype(jnp.bfloat16)
        return (grad_gu, times_transpose(grad_gu, full_gu))

    second_ring_back = RingScatter([None] * slots, "row", jnp.bfloat16)
    grad_gu_slots = [None] * slots
    order = list(range(1, slots)) + [0]
    grad_gu_slots[order[0]], second_ring_back.slots[order[0]] = ffn_backward(order[0])
    grad_down_w = None
    for index in range(second_ring_back.steps()):
        second_ring_back.send()
        slot = order[index + 1]
        value = ffn_backward(slot)
        if index == 0:
            grad_down_w = contract_rows(
                jnp.concatenate(act_slots, axis=0), jnp.concatenate(cot_slots, axis=0)
            )
            value = value + (grad_down_w,)
        second_ring_back.pending, value = lax.optimization_barrier(
            (second_ring_back.pending, value)
        )
        grad_gu_slots[slot], second_ring_back.slots[slot] = value[0], value[1]
        if index == 0:
            grad_down_w = value[2]
    grad_second = second_ring_back.result()
    down_sum = col_scatter(grad_down_w, 1)
    grad_gu = jnp.concatenate(grad_gu_slots, axis=0)
    rows_second = jnp.concatenate(second_slots, axis=0)
    grad_middle = cotangent.astype(jnp.float32) + norm_back(middle, grad_second)
    branch_chain = RingGather(grad_middle.astype(jnp.bfloat16), "row", absolute=True)
    steps = branch_chain.steps()

    def gate_up_weight_grad(_):
        return contract_rows(rows_second, grad_gu)

    tied = overlap(
        branch_chain, [gate_up_weight_grad] + [lambda done: ()] * (steps - 2) + [lambda done: down_sum]
    )
    grad_gu_w, down_sum = tied[0], tied[-1]
    gu_sum = col_scatter(grad_gu_w, 0)
    grad_branch = branch_chain.result()
    ffn_parts, grad_branch = lax.optimization_barrier((ffn_parts, grad_branch))
    ffn_ring = RingScatter(list(ffn_parts), "row", jnp.bfloat16)
    output_sum = col_scatter(contract_rows(attended, grad_branch), 1)
    half = heads_local // 2

    def heads_backward(lo, hi):
        def piece(done):
            grad_mixed = times_transpose(grad_branch, full_output[lo * HD : hi * HD])
            grad_mixed = grad_mixed.astype(jnp.bfloat16).reshape(seq_count, LENGTH, hi - lo, HD)
            return lax.map(
                attend_backward,
                (
                    queries[:, :, lo:hi],
                    keys_rot[:, :, lo:hi],
                    values[:, :, lo:hi],
                    piece_starts,
                    log_total[:, lo:hi],
                    grad_mixed,
                ),
            )

        return piece

    def finish(done):
        parts = [jnp.concatenate([a[k] for a in done], axis=2) for k in range(3)]
        grad_q_rot, grad_k_rot, grad_values = parts
        grad_qkv = jnp.concatenate(
            [
                merge_heads(unrotate(grad_q_rot, cosine, sine)),
                merge_heads(unrotate(grad_k_rot, cosine, sine)),
                merge_heads(grad_values),
            ],
            axis=1,
        ).astype(jnp.bfloat16)
        return (grad_qkv, times_transpose(grad_qkv, full_qkv))

    def second_group_and_finish(done):
        return finish(done + (heads_backward(half, heads_local)(done),))

    pieces = [heads_backward(0, half), second_group_and_finish]
    grad_qkv, first_partial = overlap(ffn_ring, pieces)[-1]
    ffn_sum = ffn_ring.result()
    output = (middle + ffn_sum).astype(jnp.bfloat16)
    qkv_sum = col_scatter(contract_rows(first_rows, grad_qkv), 0)
    first_partial, gu_sum = lax.optimization_barrier((first_partial, gu_sum))
    grad_first = ring_reduce_scatter(first_partial, "row", jnp.bfloat16)
    grad_input = grad_middle + norm_back(inputs, grad_first)
    return (
        output,
        grad_input,
        qkv_sum[:, :width],
        qkv_sum[:, width : 2 * width],
        qkv_sum[:, 2 * width :],
        output_sum,
        gu_sum[:, :hidden],
        gu_sum[:, hidden:],
        down_sum,
    )


def solution(mesh):
    in_specs = (
        P(("chip", "core", "row"), None),
        P(COL, "row"),
        P(COL, "row"),
        P(COL, "row"),
        P("row", COL),
        P(COL, "row"),
        P(COL, "row"),
        P("row", COL),
        P(COL, None),
        P(("chip", "core", "row"), None),
    )
    out_specs = (
        P(("chip", "core", "row"), None),
        P(("chip", "core", "row"), None),
        P(COL, "row"),
        P(COL, "row"),
        P(COL, "row"),
        P("row", COL),
        P(COL, "row"),
        P(COL, "row"),
        P("row", COL),
    )
    devices = mesh.devices
    sub_mesh = Mesh(
        devices.reshape(devices.shape[0], devices.shape[1] // 2, 2), ("row", "chip", "core")
    )
    return jax.shard_map(
        per_device_body, mesh=sub_mesh, in_specs=in_specs, out_specs=out_specs, check_vma=False
    )
```

```python
import math

import jax
import jax.numpy as jnp
from jax import lax
from jax.sharding import Mesh, PartitionSpec as P


HD = 128
LENGTH = 1024
PIECE = 256


EPSILON = 1e-05
NEGATIVE = -1e30


def product(left, right):
    return jnp.dot(left, right, preferred_element_type=jnp.float32)


def contract_rows(left, right):
    return lax.dot_general(
        left, right, (((0,), (0,)), ((), ())), preferred_element_type=jnp.float32
    )


def times_transpose(left, right):
    return lax.dot_general(
        left, right, (((1,), (1,)), ((), ())), preferred_element_type=jnp.float32
    )


class GatherSteps:
    def __init__(self, shard, axis):
        self.axis = axis
        self.n = lax.psum(1, axis)
        self.me = lax.axis_index(axis)
        self.rows = shard.shape[0]
        buf = jnp.zeros(((3 * self.n - 2) * self.rows,) + shard.shape[1:], shard.dtype)
        self.buf = lax.dynamic_update_slice_in_dim(buf, shard, (self.me + self.n - 1) * self.rows, 0)
        self.pending = (shard, shard)
        self.step = 0

    def steps(self):
        return self.n - 1

    def send(self):
        n, step = self.n, self.step + 1
        from_left, from_right = self.pending
        from_left = lax.ppermute(from_left, self.axis, [(j, j + 1) for j in range(step - 1, n - 1)])
        from_right = lax.ppermute(from_right, self.axis, [(j, j - 1) for j in range(1, n - step + 1)])
        self.pending = (from_left, from_right)
        self.step = step

    def land(self):
        n, step, rows = self.n, self.step, self.rows
        from_left, from_right = self.pending
        self.buf = lax.dynamic_update_slice_in_dim(self.buf, from_left, (self.me - step + n - 1) * rows, 0)
        self.buf = lax.dynamic_update_slice_in_dim(self.buf, from_right, (self.me + step + n - 1) * rows, 0)

    def result(self):
        return self.buf[(self.n - 1) * self.rows : (2 * self.n - 1) * self.rows]


class ScatterSteps:
    def __init__(self, partial, axis, send_dtype):
        self.axis = axis
        self.n = lax.psum(1, axis)
        self.me = lax.axis_index(axis)
        self.rows = partial.shape[0] // self.n
        self.partial = partial
        self.send_dtype = send_dtype
        self.pending = None
        self.step = 0

    def steps(self):
        return self.n - 1

    def block(self, k):
        return lax.dynamic_slice_in_dim(
            self.partial, jnp.clip(k, 0, self.n - 1) * self.rows, self.rows, 0
        )

    def send(self):
        n, me, step = self.n, self.me, self.step + 1
        send_right = self.block(n - step + me)
        send_left = self.block(me + step - n)
        if self.pending is not None:
            send_right = send_right + self.pending[0].astype(jnp.float32)
            send_left = send_left + self.pending[1].astype(jnp.float32)
        recv_right = lax.ppermute(
            send_right.astype(self.send_dtype), self.axis, [(j, j + 1) for j in range(0, step)]
        )
        recv_left = lax.ppermute(
            send_left.astype(self.send_dtype), self.axis, [(j, j - 1) for j in range(n - step, n)]
        )
        self.pending = (recv_right, recv_left)
        self.step = step

    def land(self):
        pass

    def result(self):
        return (
            self.block(self.me)
            + self.pending[0].astype(jnp.float32)
            + self.pending[1].astype(jnp.float32)
        )


class RingGather:
    def __init__(self, shard, axis, absolute=False):
        self.axis = axis
        self.n = lax.psum(1, axis)
        self.me = lax.axis_index(axis)
        self.rows = shard.shape[0]
        self.slots = [shard]
        self.pending = shard
        self.buf = None
        if absolute:
            buf = jnp.zeros((self.n * self.rows,) + shard.shape[1:], shard.dtype)
            self.buf = self.place(buf, shard, 0)

    def place(self, buf, block, slot):
        start = lax.rem(self.me - slot + self.n, self.n) * self.rows
        return lax.dynamic_update_slice_in_dim(buf, block, start, 0)

    def steps(self):
        return self.n - 1

    def send(self):
        n = self.n
        self.pending = lax.ppermute(self.pending, self.axis, [(j, (j + 1) % n) for j in range(n)])

    def land(self):
        self.slots.append(self.pending)
        if self.buf is not None:
            self.buf = self.place(self.buf, self.pending, len(self.slots) - 1)

    def result(self):
        return self.buf


class RingScatter:
    def __init__(self, slots, axis, send_dtype):
        self.axis = axis
        self.n = lax.psum(1, axis)
        self.slots = slots
        self.send_dtype = send_dtype
        self.pending = None
        self.step = 0

    def steps(self):
        return self.n - 1

    def send(self):
        n, step = self.n, self.step + 1
        value = self.slots[step]
        if self.pending is not None:
            value = value + self.pending.astype(jnp.float32)
        self.pending = lax.ppermute(
            value.astype(self.send_dtype), self.axis, [(j, (j + 1) % n) for j in range(n)]
        )
        self.step = step

    def land(self):
        pass

    def result(self):
        return self.slots[0] + self.pending.astype(jnp.float32)


def ring_slots(partial, axis):
    n = lax.psum(1, axis)
    me = lax.axis_index(axis)
    rows = partial.shape[0] // n
    return [
        lax.dynamic_slice_in_dim(partial, lax.rem(me - slot + n, n) * rows, rows, 0)
        for slot in range(n)
    ]


def ring_all_gather(shard, axis):
    chain = RingGather(shard, axis, absolute=True)
    overlap(chain, [])
    return chain.result()


def ring_reduce_scatter(partial, axis, send_dtype):
    chain = RingScatter(ring_slots(partial, axis), axis, send_dtype)
    overlap(chain, [])
    return chain.result()


def overlap(chain, pieces):
    outputs = []
    count = chain.steps()
    for index in range(count):
        chain.send()
        if index < len(pieces):
            value = pieces[index](tuple(outputs))
            chain.pending, value = lax.optimization_barrier((chain.pending, value))
            outputs.append(value)
        else:
            chain.pending = lax.optimization_barrier(chain.pending)
        chain.land()
    for piece in pieces[count:]:
        outputs.append(piece(tuple(outputs)))
    return tuple(outputs)


COL = ("chip", "core")


def col_gather(block, axis):
    return lax.all_gather(block, COL, axis=axis, tiled=True)


def col_scatter(partial, axis):
    low_part = partial.astype(jnp.bfloat16)
    return lax.psum_scatter(low_part, COL, scatter_dimension=axis, tiled=True).astype(jnp.float32)


def layer_norm(inputs):
    center = inputs - jnp.mean(inputs, axis=-1, keepdims=True)
    spread = jnp.mean(center * center, axis=-1, keepdims=True)
    return center * lax.rsqrt(spread + EPSILON)


def norm_back(inputs, grad):
    center = inputs - jnp.mean(inputs, axis=-1, keepdims=True)
    inverse = lax.rsqrt(jnp.mean(center * center, axis=-1, keepdims=True) + EPSILON)
    normed = center * inverse
    return inverse * (
        grad
        - jnp.mean(grad, axis=-1, keepdims=True)
        - normed * jnp.mean(grad * normed, axis=-1, keepdims=True)
    )


def rope_tables():
    positions = jnp.arange(LENGTH, dtype=jnp.float32)
    freqs = jnp.power(jnp.float32(10000.0), -jnp.arange(HD // 2, dtype=jnp.float32) * (2.0 / HD))
    angles = positions[:, None] * freqs[None, :]
    return (jnp.cos(angles)[:, None, :], jnp.sin(angles)[:, None, :])


def rotate(field, cosine, sine):
    half_size = field.shape[-1] // 2
    first_half = field[..., :half_size]
    second_half = field[..., half_size:]
    return jnp.concatenate(
        [first_half * cosine - second_half * sine, second_half * cosine + first_half * sine],
        axis=-1,
    )


def unrotate(field, cosine, sine):
    half_size = field.shape[-1] // 2
    first_half = field[..., :half_size]
    second_half = field[..., half_size:]
    return jnp.concatenate(
        [first_half * cosine + second_half * sine, second_half * cosine - first_half * sine],
        axis=-1,
    )


def piece_mask(starts):
    positions = jnp.arange(LENGTH, dtype=jnp.int32)
    inside = (positions[None, :] >= starts[:, None]) & (
        positions[None, :] < starts[:, None] + PIECE
    )
    shared = jnp.any(inside[:, :, None] & inside[:, None, :], axis=0)
    causal = positions[None, :] <= positions[:, None]
    return causal | shared


def masked_scores(queries, keys_rot, starts):
    scale = 1.0 / math.sqrt(HD)
    scores = (
        jnp.einsum("qhd,khd->hqk", queries, keys_rot, preferred_element_type=jnp.float32) * scale
    )
    return jnp.where(piece_mask(starts)[None], scores, NEGATIVE)


def attend_forward(operands):
    queries, keys_rot, values, starts = operands
    scores = masked_scores(queries, keys_rot, starts)
    row_top = jnp.max(scores, axis=-1, keepdims=True)
    shifted = jnp.exp(scores - row_top)
    row_total = jnp.sum(shifted, axis=-1, keepdims=True)
    probs = (shifted / row_total).astype(jnp.bfloat16)
    mixed = jnp.einsum("hqk,khd->qhd", probs, values, preferred_element_type=jnp.float32)
    return (mixed, row_top + jnp.log(row_total))


def attend_backward(operands):
    queries, keys_rot, values, starts, log_total, grad_mixed = operands
    scale = 1.0 / math.sqrt(HD)
    scores = masked_scores(queries, keys_rot, starts)
    probs = jnp.exp(scores - log_total)
    probs_low = probs.astype(jnp.bfloat16)
    grad_values = jnp.einsum(
        "hqk,qhd->khd", probs_low, grad_mixed, preferred_element_type=jnp.float32
    )
    grad_probs = jnp.einsum("qhd,khd->hqk", grad_mixed, values, preferred_element_type=jnp.float32)
    inner = jnp.sum(probs * grad_probs, axis=-1, keepdims=True)
    grad_scores = (probs * (grad_probs - inner)).astype(jnp.bfloat16)
    grad_queries = (
        jnp.einsum("hqk,khd->qhd", grad_scores, keys_rot, preferred_element_type=jnp.float32)
        * scale
    )
    grad_keys = (
        jnp.einsum("hqk,qhd->khd", grad_scores, queries, preferred_element_type=jnp.float32) * scale
    )
    return (grad_queries, grad_keys, grad_values)


def per_device_body(
    layer_input, w_query, w_key, w_value, w_output, w_gate, w_up, w_down, piece_starts, cotangent
):
    seq_count = piece_starts.shape[0]
    group_rows = seq_count * LENGTH
    width = w_query.shape[1]
    hidden = w_gate.shape[1]
    heads_local = width // HD
    full_qkv = col_gather(jnp.concatenate([w_query, w_key, w_value], axis=1), 0)
    full_output = col_gather(w_output, 1)
    full_gu = col_gather(jnp.concatenate([w_gate, w_up], axis=1), 0)
    full_down = col_gather(w_down, 1)
    cosine, sine = rope_tables()
    inputs = layer_input.astype(jnp.float32)
    normed_first = layer_norm(inputs).astype(jnp.bfloat16)
    first_rows = ring_all_gather(normed_first, "row")

    def split_heads(matrix):
        return matrix.reshape(seq_count, LENGTH, heads_local, HD)

    def merge_heads(field):
        return field.reshape(group_rows, heads_local * HD)

    def project(_):
        qkv_lin = product(first_rows, full_qkv)
        queries = rotate(split_heads(qkv_lin[:, :width]), cosine, sine).astype(jnp.bfloat16)
        keys_rot = rotate(split_heads(qkv_lin[:, width : 2 * width]), cosine, sine).astype(
            jnp.bfloat16
        )
        values = split_heads(qkv_lin[:, 2 * width :]).astype(jnp.bfloat16)
        return dict(queries=queries, keys_rot=keys_rot, values=values)

    def attend(done):
        state = done[0]
        mixed, log_total = lax.map(
            attend_forward, (state["queries"], state["keys_rot"], state["values"], piece_starts)
        )
        return dict(mixed=mixed, log_total=log_total)

    def out_project(done):
        attended = merge_heads(done[1]["mixed"].astype(jnp.bfloat16))
        return dict(attended=attended, attn_partial=product(attended, full_output))

    cot_later, first_rows = lax.optimization_barrier((cotangent, first_rows))
    cot_ring = RingGather(cot_later, "row")
    projected, attention, mixed_out = overlap(cot_ring, [project, attend, out_project])
    cot_slots = cot_ring.slots
    queries, keys_rot = projected["queries"], projected["keys_rot"]
    values = projected["values"]
    log_total, attended = attention["log_total"], mixed_out["attended"]
    attention_sum = ring_reduce_scatter(mixed_out["attn_partial"], "row", jnp.bfloat16)
    middle = inputs + attention_sum
    normed_second = layer_norm(middle).astype(jnp.bfloat16)
    second_ring = RingGather(normed_second, "row")
    slots = second_ring.n

    def ffn_forward(slot):
        def piece(done):
            gu_lin = product(second_ring.slots[slot], full_gu)
            gate_lin = gu_lin[:, :hidden]
            up_lin = gu_lin[:, hidden:]
            activation = (jax.nn.silu(gate_lin) * up_lin).astype(jnp.bfloat16)
            part = product(activation, full_down)
            return (gate_lin, up_lin, activation, part)

        return piece

    ffn = overlap(second_ring, [ffn_forward(slot) for slot in range(slots)])
    second_slots = second_ring.slots
    gate_slots = [item[0] for item in ffn]
    up_slots = [item[1] for item in ffn]
    act_slots = [item[2] for item in ffn]
    ffn_parts = [item[3] for item in ffn]

    def ffn_backward(group):
        def rows(blocks):
            return jnp.concatenate([blocks[slot] for slot in group], axis=0)

        gate_lin, up_lin = rows(gate_slots), rows(up_slots)
        grad_activation = times_transpose(rows(cot_slots), full_down)
        sigma = jax.nn.sigmoid(gate_lin)
        grad_gate = grad_activation * up_lin * sigma * (1.0 + gate_lin * (1.0 - sigma))
        grad_up = grad_activation * gate_lin * sigma
        grad_gu = jnp.concatenate([grad_gate, grad_up], axis=1).astype(jnp.bfloat16)
        partial = times_transpose(grad_gu, full_gu)
        size = partial.shape[0] // len(group)
        return tuple(
            (grad_gu[k * size : (k + 1) * size], partial[k * size : (k + 1) * size])
            for k in range(len(group))
        )

    second_ring_back = RingScatter([None] * slots, "row", jnp.bfloat16)
    grad_gu_slots = [None] * slots
    order = list(range(1, slots)) + [0]
    groups = [order[k : k + 2] for k in range(0, slots, 2)]
    for slot, item in zip(groups[0], ffn_backward(groups[0])):
        grad_gu_slots[slot], second_ring_back.slots[slot] = item
    grad_down_w = None
    for index in range(second_ring_back.steps()):
        second_ring_back.send()
        value = ()
        if index + 1 < len(groups):
            value = ffn_backward(groups[index + 1])
        fresh = None
        if index == 1 or (index == 0 and len(groups) == 1):
            fresh = contract_rows(
                jnp.concatenate(act_slots, axis=0), jnp.concatenate(cot_slots, axis=0)
            )
        second_ring_back.pending, value, fresh = lax.optimization_barrier(
            (second_ring_back.pending, value, fresh)
        )
        if fresh is not None:
            grad_down_w = fresh
        if index + 1 < len(groups):
            for slot, item in zip(groups[index + 1], value):
                grad_gu_slots[slot], second_ring_back.slots[slot] = item
    grad_second = second_ring_back.result()
    down_sum = col_scatter(grad_down_w, 1)
    grad_gu = jnp.concatenate(grad_gu_slots, axis=0)
    rows_second = jnp.concatenate(second_slots, axis=0)
    grad_middle = cotangent.astype(jnp.float32) + norm_back(middle, grad_second)
    branch_chain = RingGather(grad_middle.astype(jnp.bfloat16), "row", absolute=True)
    steps = branch_chain.steps()

    def gate_up_weight_grad(_):
        return contract_rows(rows_second, grad_gu)

    tied = overlap(
        branch_chain, [gate_up_weight_grad] + [lambda done: ()] * (steps - 2) + [lambda done: down_sum]
    )
    grad_gu_w, down_sum = tied[0], tied[-1]
    gu_sum = col_scatter(grad_gu_w, 0)
    grad_branch = branch_chain.result()
    ffn_parts, grad_branch = lax.optimization_barrier((ffn_parts, grad_branch))
    ffn_ring = RingScatter(list(ffn_parts), "row", jnp.bfloat16)
    output_sum = col_scatter(contract_rows(attended, grad_branch), 1)
    half = heads_local // 2

    def heads_backward(lo, hi):
        def piece(done):
            grad_mixed = times_transpose(grad_branch, full_output[lo * HD : hi * HD])
            grad_mixed = grad_mixed.astype(jnp.bfloat16).reshape(seq_count, LENGTH, hi - lo, HD)
            return lax.map(
                attend_backward,
                (
                    queries[:, :, lo:hi],
                    keys_rot[:, :, lo:hi],
                    values[:, :, lo:hi],
                    piece_starts,
                    log_total[:, lo:hi],
                    grad_mixed,
                ),
            )

        return piece

    def finish(done):
        parts = [jnp.concatenate([a[k] for a in done], axis=2) for k in range(3)]
        grad_q_rot, grad_k_rot, grad_values = parts
        grad_qkv = jnp.concatenate(
            [
                merge_heads(unrotate(grad_q_rot, cosine, sine)),
                merge_heads(unrotate(grad_k_rot, cosine, sine)),
                merge_heads(grad_values),
            ],
            axis=1,
        ).astype(jnp.bfloat16)
        return (grad_qkv, times_transpose(grad_qkv, full_qkv))

    def second_group_and_finish(done):
        return finish(done + (heads_backward(half, heads_local)(done),))

    pieces = [heads_backward(0, half), second_group_and_finish]
    grad_qkv, first_partial = overlap(ffn_ring, pieces)[-1]
    ffn_sum = ffn_ring.result()
    output = (middle + ffn_sum).astype(jnp.bfloat16)
    qkv_sum = col_scatter(contract_rows(first_rows, grad_qkv), 0)
    first_partial, gu_sum = lax.optimization_barrier((first_partial, gu_sum))
    grad_first = ring_reduce_scatter(first_partial, "row", jnp.bfloat16)
    grad_input = grad_middle + norm_back(inputs, grad_first)
    return (
        output,
        grad_input,
        qkv_sum[:, :width],
        qkv_sum[:, width : 2 * width],
        qkv_sum[:, 2 * width :],
        output_sum,
        gu_sum[:, :hidden],
        gu_sum[:, hidden:],
        down_sum,
    )


def solution(mesh):
    in_specs = (
        P(("chip", "core", "row"), None),
        P(COL, "row"),
        P(COL, "row"),
        P(COL, "row"),
        P("row", COL),
        P(COL, "row"),
        P(COL, "row"),
        P("row", COL),
        P(COL, None),
        P(("chip", "core", "row"), None),
    )
    out_specs = (
        P(("chip", "core", "row"), None),
        P(("chip", "core", "row"), None),
        P(COL, "row"),
        P(COL, "row"),
        P(COL, "row"),
        P("row", COL),
        P(COL, "row"),
        P(COL, "row"),
        P("row", COL),
    )
    devices = mesh.devices
    sub_mesh = Mesh(
        devices.reshape(devices.shape[0], devices.shape[1] // 2, 2), ("row", "chip", "core")
    )
    return jax.shard_map(
        per_device_body, mesh=sub_mesh, in_specs=in_specs, out_specs=out_specs, check_vma=False
    )
```

```python
import math

import jax
import jax.numpy as jnp
from jax import lax
from jax.sharding import Mesh, PartitionSpec as P


HD = 128
LENGTH = 1024
PIECE = 256


EPSILON = 1e-05
NEGATIVE = -1e30


def product(left, right):
    return jnp.dot(left, right, preferred_element_type=jnp.float32)


def contract_rows(left, right):
    return lax.dot_general(
        left, right, (((0,), (0,)), ((), ())), preferred_element_type=jnp.float32
    )


def times_transpose(left, right):
    return lax.dot_general(
        left, right, (((1,), (1,)), ((), ())), preferred_element_type=jnp.float32
    )


class GatherSteps:
    def __init__(self, shard, axis):
        self.axis = axis
        self.n = lax.psum(1, axis)
        self.me = lax.axis_index(axis)
        self.rows = shard.shape[0]
        buf = jnp.zeros(((3 * self.n - 2) * self.rows,) + shard.shape[1:], shard.dtype)
        self.buf = lax.dynamic_update_slice_in_dim(buf, shard, (self.me + self.n - 1) * self.rows, 0)
        self.pending = (shard, shard)
        self.step = 0

    def steps(self):
        return self.n - 1

    def send(self):
        n, step = self.n, self.step + 1
        from_left, from_right = self.pending
        from_left = lax.ppermute(from_left, self.axis, [(j, j + 1) for j in range(step - 1, n - 1)])
        from_right = lax.ppermute(from_right, self.axis, [(j, j - 1) for j in range(1, n - step + 1)])
        self.pending = (from_left, from_right)
        self.step = step

    def land(self):
        n, step, rows = self.n, self.step, self.rows
        from_left, from_right = self.pending
        self.buf = lax.dynamic_update_slice_in_dim(self.buf, from_left, (self.me - step + n - 1) * rows, 0)
        self.buf = lax.dynamic_update_slice_in_dim(self.buf, from_right, (self.me + step + n - 1) * rows, 0)

    def result(self):
        return self.buf[(self.n - 1) * self.rows : (2 * self.n - 1) * self.rows]


class ScatterSteps:
    def __init__(self, partial, axis, send_dtype):
        self.axis = axis
        self.n = lax.psum(1, axis)
        self.me = lax.axis_index(axis)
        self.rows = partial.shape[0] // self.n
        self.partial = partial
        self.send_dtype = send_dtype
        self.pending = None
        self.step = 0

    def steps(self):
        return self.n - 1

    def block(self, k):
        return lax.dynamic_slice_in_dim(
            self.partial, jnp.clip(k, 0, self.n - 1) * self.rows, self.rows, 0
        )

    def send(self):
        n, me, step = self.n, self.me, self.step + 1
        send_right = self.block(n - step + me)
        send_left = self.block(me + step - n)
        if self.pending is not None:
            send_right = send_right + self.pending[0].astype(jnp.float32)
            send_left = send_left + self.pending[1].astype(jnp.float32)
        recv_right = lax.ppermute(
            send_right.astype(self.send_dtype), self.axis, [(j, j + 1) for j in range(0, step)]
        )
        recv_left = lax.ppermute(
            send_left.astype(self.send_dtype), self.axis, [(j, j - 1) for j in range(n - step, n)]
        )
        self.pending = (recv_right, recv_left)
        self.step = step

    def land(self):
        pass

    def result(self):
        return (
            self.block(self.me)
            + self.pending[0].astype(jnp.float32)
            + self.pending[1].astype(jnp.float32)
        )


class RingGather:
    def __init__(self, shard, axis, absolute=False):
        self.axis = axis
        self.n = lax.psum(1, axis)
        self.me = lax.axis_index(axis)
        self.rows = shard.shape[0]
        self.slots = [shard]
        self.pending = shard
        self.buf = None
        if absolute:
            buf = jnp.zeros((self.n * self.rows,) + shard.shape[1:], shard.dtype)
            self.buf = self.place(buf, shard, 0)

    def place(self, buf, block, slot):
        start = lax.rem(self.me - slot + self.n, self.n) * self.rows
        return lax.dynamic_update_slice_in_dim(buf, block, start, 0)

    def steps(self):
        return self.n - 1

    def send(self):
        n = self.n
        self.pending = lax.ppermute(self.pending, self.axis, [(j, (j + 1) % n) for j in range(n)])

    def land(self):
        self.slots.append(self.pending)
        if self.buf is not None:
            self.buf = self.place(self.buf, self.pending, len(self.slots) - 1)

    def result(self):
        return self.buf


class RingScatter:
    def __init__(self, slots, axis, send_dtype):
        self.axis = axis
        self.n = lax.psum(1, axis)
        self.slots = slots
        self.send_dtype = send_dtype
        self.pending = None
        self.step = 0

    def steps(self):
        return self.n - 1

    def send(self):
        n, step = self.n, self.step + 1
        value = self.slots[step]
        if self.pending is not None:
            value = value + self.pending.astype(jnp.float32)
        self.pending = lax.ppermute(
            value.astype(self.send_dtype), self.axis, [(j, (j + 1) % n) for j in range(n)]
        )
        self.step = step

    def land(self):
        pass

    def result(self):
        return self.slots[0] + self.pending.astype(jnp.float32)


def ring_slots(partial, axis):
    n = lax.psum(1, axis)
    me = lax.axis_index(axis)
    rows = partial.shape[0] // n
    return [
        lax.dynamic_slice_in_dim(partial, lax.rem(me - slot + n, n) * rows, rows, 0)
        for slot in range(n)
    ]


def ring_all_gather(shard, axis):
    chain = RingGather(shard, axis, absolute=True)
    overlap(chain, [])
    return chain.result()


def ring_reduce_scatter(partial, axis, send_dtype):
    chain = RingScatter(ring_slots(partial, axis), axis, send_dtype)
    overlap(chain, [])
    return chain.result()


def overlap(chain, pieces):
    outputs = []
    count = chain.steps()
    for index in range(count):
        chain.send()
        if index < len(pieces):
            value = pieces[index](tuple(outputs))
            chain.pending, value = lax.optimization_barrier((chain.pending, value))
            outputs.append(value)
        else:
            chain.pending = lax.optimization_barrier(chain.pending)
        chain.land()
    for piece in pieces[count:]:
        outputs.append(piece(tuple(outputs)))
    return tuple(outputs)


COL = ("chip", "core")


def col_gather(block, axis):
    return lax.all_gather(block, COL, axis=axis, tiled=True)


def col_scatter(partial, axis):
    low_part = partial.astype(jnp.bfloat16)
    return lax.psum_scatter(low_part, COL, scatter_dimension=axis, tiled=True).astype(jnp.float32)


def layer_norm(inputs):
    center = inputs - jnp.mean(inputs, axis=-1, keepdims=True)
    spread = jnp.mean(center * center, axis=-1, keepdims=True)
    return center * lax.rsqrt(spread + EPSILON)


def norm_back(inputs, grad):
    center = inputs - jnp.mean(inputs, axis=-1, keepdims=True)
    inverse = lax.rsqrt(jnp.mean(center * center, axis=-1, keepdims=True) + EPSILON)
    normed = center * inverse
    return inverse * (
        grad
        - jnp.mean(grad, axis=-1, keepdims=True)
        - normed * jnp.mean(grad * normed, axis=-1, keepdims=True)
    )


def rope_tables():
    positions = jnp.arange(LENGTH, dtype=jnp.float32)
    freqs = jnp.power(jnp.float32(10000.0), -jnp.arange(HD // 2, dtype=jnp.float32) * (2.0 / HD))
    angles = positions[:, None] * freqs[None, :]
    return (jnp.cos(angles)[:, None, :], jnp.sin(angles)[:, None, :])


def rotate(field, cosine, sine):
    half_size = field.shape[-1] // 2
    first_half = field[..., :half_size]
    second_half = field[..., half_size:]
    return jnp.concatenate(
        [first_half * cosine - second_half * sine, second_half * cosine + first_half * sine],
        axis=-1,
    )


def unrotate(field, cosine, sine):
    half_size = field.shape[-1] // 2
    first_half = field[..., :half_size]
    second_half = field[..., half_size:]
    return jnp.concatenate(
        [first_half * cosine + second_half * sine, second_half * cosine - first_half * sine],
        axis=-1,
    )


def piece_mask(starts):
    positions = jnp.arange(LENGTH, dtype=jnp.int32)
    inside = (positions[None, :] >= starts[:, None]) & (
        positions[None, :] < starts[:, None] + PIECE
    )
    shared = jnp.any(inside[:, :, None] & inside[:, None, :], axis=0)
    causal = positions[None, :] <= positions[:, None]
    return causal | shared


def masked_scores(queries, keys_rot, starts):
    scale = 1.0 / math.sqrt(HD)
    scores = (
        jnp.einsum("qhd,khd->hqk", queries, keys_rot, preferred_element_type=jnp.float32) * scale
    )
    return jnp.where(piece_mask(starts)[None], scores, NEGATIVE)


def attend_forward(operands):
    queries, keys_rot, values, starts = operands
    scores = masked_scores(queries, keys_rot, starts)
    row_top = jnp.max(scores, axis=-1, keepdims=True)
    shifted = jnp.exp(scores - row_top)
    row_total = jnp.sum(shifted, axis=-1, keepdims=True)
    probs = (shifted / row_total).astype(jnp.bfloat16)
    mixed = jnp.einsum("hqk,khd->qhd", probs, values, preferred_element_type=jnp.float32)
    return (mixed, row_top + jnp.log(row_total))


def attend_backward(operands):
    queries, keys_rot, values, starts, log_total, grad_mixed = operands
    scale = 1.0 / math.sqrt(HD)
    scores = masked_scores(queries, keys_rot, starts)
    probs = jnp.exp(scores - log_total)
    probs_low = probs.astype(jnp.bfloat16)
    grad_values = jnp.einsum(
        "hqk,qhd->khd", probs_low, grad_mixed, preferred_element_type=jnp.float32
    )
    grad_probs = jnp.einsum("qhd,khd->hqk", grad_mixed, values, preferred_element_type=jnp.float32)
    inner = jnp.sum(probs * grad_probs, axis=-1, keepdims=True)
    grad_scores = (probs * (grad_probs - inner)).astype(jnp.bfloat16)
    grad_queries = (
        jnp.einsum("hqk,khd->qhd", grad_scores, keys_rot, preferred_element_type=jnp.float32)
        * scale
    )
    grad_keys = (
        jnp.einsum("hqk,qhd->khd", grad_scores, queries, preferred_element_type=jnp.float32) * scale
    )
    return (grad_queries, grad_keys, grad_values)


def per_device_body(
    layer_input, w_query, w_key, w_value, w_output, w_gate, w_up, w_down, piece_starts, cotangent
):
    seq_count = piece_starts.shape[0]
    group_rows = seq_count * LENGTH
    width = w_query.shape[1]
    hidden = w_gate.shape[1]
    heads_local = width // HD
    full_qkvo = col_gather(jnp.concatenate([w_query, w_key, w_value, w_output.T], axis=1), 0)
    full_qkv = full_qkvo[:, : 3 * width]
    output_t = full_qkvo[:, 3 * width :]
    full_gu = col_gather(jnp.concatenate([w_gate, w_up], axis=1), 0)
    full_down = col_gather(w_down, 1)
    cosine, sine = rope_tables()
    inputs = layer_input.astype(jnp.float32)
    normed_first = layer_norm(inputs).astype(jnp.bfloat16)
    first_rows = ring_all_gather(normed_first, "row")

    def split_heads(matrix):
        return matrix.reshape(seq_count, LENGTH, heads_local, HD)

    def merge_heads(field):
        return field.reshape(group_rows, heads_local * HD)

    def project(_):
        qkv_lin = product(first_rows, full_qkv)
        queries = rotate(split_heads(qkv_lin[:, :width]), cosine, sine).astype(jnp.bfloat16)
        keys_rot = rotate(split_heads(qkv_lin[:, width : 2 * width]), cosine, sine).astype(
            jnp.bfloat16
        )
        values = split_heads(qkv_lin[:, 2 * width :]).astype(jnp.bfloat16)
        return dict(queries=queries, keys_rot=keys_rot, values=values)

    def attend(done):
        state = done[0]
        mixed, log_total = lax.map(
            attend_forward, (state["queries"], state["keys_rot"], state["values"], piece_starts)
        )
        return dict(mixed=mixed, log_total=log_total)

    def out_project(done):
        attended = merge_heads(done[1]["mixed"].astype(jnp.bfloat16))
        return dict(attended=attended, attn_partial=times_transpose(attended, output_t))

    cot_later, first_rows = lax.optimization_barrier((cotangent, first_rows))
    cot_ring = RingGather(cot_later, "row")
    projected, attention, mixed_out = overlap(cot_ring, [project, attend, out_project])
    cot_slots = cot_ring.slots
    queries, keys_rot = projected["queries"], projected["keys_rot"]
    values = projected["values"]
    log_total, attended = attention["log_total"], mixed_out["attended"]
    full_down, attn_partial = lax.optimization_barrier((full_down, mixed_out["attn_partial"]))
    attn_ring = RingScatter(ring_slots(attn_partial, "row"), "row", jnp.bfloat16)
    cot_count = len(cot_slots)
    per_step = -(-cot_count // attn_ring.steps())

    def cot_grads(index):
        def piece(done):
            chosen = cot_slots[index * per_step : (index + 1) * per_step]
            return tuple(times_transpose(block, full_down) for block in chosen)

        return piece

    grad_act_parts = overlap(attn_ring, [cot_grads(index) for index in range(attn_ring.steps())])
    grad_act_slots = [block for part in grad_act_parts for block in part]
    attention_sum = attn_ring.result()
    middle = inputs + attention_sum
    normed_second = layer_norm(middle).astype(jnp.bfloat16)
    full_gu, normed_second = lax.optimization_barrier((full_gu, normed_second))
    second_ring = RingGather(normed_second, "row")
    slots = second_ring.n

    def ffn_forward(slot):
        def piece(done):
            gu_lin = product(second_ring.slots[slot], full_gu)
            gate_lin = gu_lin[:, :hidden]
            up_lin = gu_lin[:, hidden:]
            activation = (jax.nn.silu(gate_lin) * up_lin).astype(jnp.bfloat16)
            part = product(activation, full_down)
            return (gate_lin, up_lin, activation, part)

        return piece

    ffn = overlap(second_ring, [ffn_forward(slot) for slot in range(slots)])
    second_slots = second_ring.slots
    gate_slots = [item[0] for item in ffn]
    up_slots = [item[1] for item in ffn]
    act_slots = [item[2] for item in ffn]
    ffn_parts = [item[3] for item in ffn]

    def ffn_backward(slot):
        gate_lin, up_lin = gate_slots[slot], up_slots[slot]
        grad_activation = grad_act_slots[slot]
        sigma = jax.nn.sigmoid(gate_lin)
        grad_gate = grad_activation * up_lin * sigma * (1.0 + gate_lin * (1.0 - sigma))
        grad_up = grad_activation * gate_lin * sigma
        grad_gu = jnp.concatenate([grad_gate, grad_up], axis=1).astype(jnp.bfloat16)
        return (grad_gu, times_transpose(grad_gu, full_gu))

    second_ring_back = RingScatter([None] * slots, "row", jnp.bfloat16)
    grad_gu_slots = [None] * slots
    order = list(range(1, slots)) + [0]
    grad_gu_slots[order[0]], second_ring_back.slots[order[0]] = ffn_backward(order[0])
    grad_down_w = None
    for index in range(second_ring_back.steps()):
        second_ring_back.send()
        slot = order[index + 1]
        value = ffn_backward(slot)
        if index == 0:
            grad_down_w = contract_rows(
                jnp.concatenate(act_slots, axis=0), jnp.concatenate(cot_slots, axis=0)
            )
            value = value + (grad_down_w,)
        second_ring_back.pending, value = lax.optimization_barrier(
            (second_ring_back.pending, value)
        )
        grad_gu_slots[slot], second_ring_back.slots[slot] = value[0], value[1]
        if index == 0:
            grad_down_w = value[2]
    grad_second = second_ring_back.result()
    down_sum = col_scatter(grad_down_w, 1)
    grad_gu = jnp.concatenate(grad_gu_slots, axis=0)
    rows_second = jnp.concatenate(second_slots, axis=0)
    grad_middle = cotangent.astype(jnp.float32) + norm_back(middle, grad_second)
    branch_chain = RingGather(grad_middle.astype(jnp.bfloat16), "row", absolute=True)
    steps = branch_chain.steps()

    def gate_up_weight_grad(_):
        return contract_rows(rows_second, grad_gu)

    tied = overlap(
        branch_chain, [gate_up_weight_grad] + [lambda done: ()] * (steps - 2) + [lambda done: down_sum]
    )
    grad_gu_w, down_sum = tied[0], tied[-1]
    gu_sum = col_scatter(grad_gu_w, 0)
    grad_branch = branch_chain.result()
    ffn_parts, grad_branch = lax.optimization_barrier((ffn_parts, grad_branch))
    ffn_ring = RingScatter(list(ffn_parts), "row", jnp.bfloat16)
    output_sum = col_scatter(contract_rows(attended, grad_branch), 1)
    half = heads_local // 2

    def heads_backward(lo, hi):
        def piece(done):
            grad_mixed = product(grad_branch, output_t[:, lo * HD : hi * HD])
            grad_mixed = grad_mixed.astype(jnp.bfloat16).reshape(seq_count, LENGTH, hi - lo, HD)
            return lax.map(
                attend_backward,
                (
                    queries[:, :, lo:hi],
                    keys_rot[:, :, lo:hi],
                    values[:, :, lo:hi],
                    piece_starts,
                    log_total[:, lo:hi],
                    grad_mixed,
                ),
            )

        return piece

    def finish(done):
        parts = [jnp.concatenate([a[k] for a in done], axis=2) for k in range(3)]
        grad_q_rot, grad_k_rot, grad_values = parts
        grad_qkv = jnp.concatenate(
            [
                merge_heads(unrotate(grad_q_rot, cosine, sine)),
                merge_heads(unrotate(grad_k_rot, cosine, sine)),
                merge_heads(grad_values),
            ],
            axis=1,
        ).astype(jnp.bfloat16)
        return (grad_qkv, times_transpose(grad_qkv, full_qkv))

    def second_group_and_finish(done):
        return finish(done + (heads_backward(half, heads_local)(done),))

    pieces = [heads_backward(0, half), second_group_and_finish]
    grad_qkv, first_partial = overlap(ffn_ring, pieces)[-1]
    ffn_sum = ffn_ring.result()
    output = (middle + ffn_sum).astype(jnp.bfloat16)
    qkv_sum = col_scatter(contract_rows(first_rows, grad_qkv), 0)
    first_partial, gu_sum = lax.optimization_barrier((first_partial, gu_sum))
    grad_first = ring_reduce_scatter(first_partial, "row", jnp.bfloat16)
    grad_input = grad_middle + norm_back(inputs, grad_first)
    return (
        output,
        grad_input,
        qkv_sum[:, :width],
        qkv_sum[:, width : 2 * width],
        qkv_sum[:, 2 * width :],
        output_sum,
        gu_sum[:, :hidden],
        gu_sum[:, hidden:],
        down_sum,
    )


def solution(mesh):
    in_specs = (
        P(("chip", "core", "row"), None),
        P(COL, "row"),
        P(COL, "row"),
        P(COL, "row"),
        P("row", COL),
        P(COL, "row"),
        P(COL, "row"),
        P("row", COL),
        P(COL, None),
        P(("chip", "core", "row"), None),
    )
    out_specs = (
        P(("chip", "core", "row"), None),
        P(("chip", "core", "row"), None),
        P(COL, "row"),
        P(COL, "row"),
        P(COL, "row"),
        P("row", COL),
        P(COL, "row"),
        P(COL, "row"),
        P("row", COL),
    )
    devices = mesh.devices
    sub_mesh = Mesh(
        devices.reshape(devices.shape[0], devices.shape[1] // 2, 2), ("row", "chip", "core")
    )
    return jax.shard_map(
        per_device_body, mesh=sub_mesh, in_specs=in_specs, out_specs=out_specs, check_vma=False
    )
```

```python
import math

import jax
import jax.numpy as jnp
from jax import lax
from jax.sharding import Mesh, PartitionSpec as P


HD = 128
LENGTH = 1024
PIECE = 256


EPSILON = 1e-05
NEGATIVE = -1e30


def product(left, right):
    return jnp.dot(left, right, preferred_element_type=jnp.float32)


def contract_rows(left, right):
    return lax.dot_general(
        left, right, (((0,), (0,)), ((), ())), preferred_element_type=jnp.float32
    )


def times_transpose(left, right):
    return lax.dot_general(
        left, right, (((1,), (1,)), ((), ())), preferred_element_type=jnp.float32
    )


class GatherSteps:
    def __init__(self, shard, axis):
        self.axis = axis
        self.n = lax.psum(1, axis)
        self.me = lax.axis_index(axis)
        self.rows = shard.shape[0]
        buf = jnp.zeros(((3 * self.n - 2) * self.rows,) + shard.shape[1:], shard.dtype)
        self.buf = lax.dynamic_update_slice_in_dim(buf, shard, (self.me + self.n - 1) * self.rows, 0)
        self.pending = (shard, shard)
        self.step = 0

    def steps(self):
        return self.n - 1

    def send(self):
        n, step = self.n, self.step + 1
        from_left, from_right = self.pending
        from_left = lax.ppermute(from_left, self.axis, [(j, j + 1) for j in range(step - 1, n - 1)])
        from_right = lax.ppermute(from_right, self.axis, [(j, j - 1) for j in range(1, n - step + 1)])
        self.pending = (from_left, from_right)
        self.step = step

    def land(self):
        n, step, rows = self.n, self.step, self.rows
        from_left, from_right = self.pending
        self.buf = lax.dynamic_update_slice_in_dim(self.buf, from_left, (self.me - step + n - 1) * rows, 0)
        self.buf = lax.dynamic_update_slice_in_dim(self.buf, from_right, (self.me + step + n - 1) * rows, 0)

    def result(self):
        return self.buf[(self.n - 1) * self.rows : (2 * self.n - 1) * self.rows]


class ScatterSteps:
    def __init__(self, partial, axis, send_dtype):
        self.axis = axis
        self.n = lax.psum(1, axis)
        self.me = lax.axis_index(axis)
        self.rows = partial.shape[0] // self.n
        self.partial = partial
        self.send_dtype = send_dtype
        self.pending = None
        self.step = 0

    def steps(self):
        return self.n - 1

    def block(self, k):
        return lax.dynamic_slice_in_dim(
            self.partial, jnp.clip(k, 0, self.n - 1) * self.rows, self.rows, 0
        )

    def send(self):
        n, me, step = self.n, self.me, self.step + 1
        send_right = self.block(n - step + me)
        send_left = self.block(me + step - n)
        if self.pending is not None:
            send_right = send_right + self.pending[0].astype(jnp.float32)
            send_left = send_left + self.pending[1].astype(jnp.float32)
        recv_right = lax.ppermute(
            send_right.astype(self.send_dtype), self.axis, [(j, j + 1) for j in range(0, step)]
        )
        recv_left = lax.ppermute(
            send_left.astype(self.send_dtype), self.axis, [(j, j - 1) for j in range(n - step, n)]
        )
        self.pending = (recv_right, recv_left)
        self.step = step

    def land(self):
        pass

    def result(self):
        return (
            self.block(self.me)
            + self.pending[0].astype(jnp.float32)
            + self.pending[1].astype(jnp.float32)
        )


class RingGather:
    def __init__(self, shard, axis, absolute=False):
        self.axis = axis
        self.n = lax.psum(1, axis)
        self.me = lax.axis_index(axis)
        self.rows = shard.shape[0]
        self.slots = [shard]
        self.pending = shard
        self.buf = None
        if absolute:
            buf = jnp.zeros((self.n * self.rows,) + shard.shape[1:], shard.dtype)
            self.buf = self.place(buf, shard, 0)

    def place(self, buf, block, slot):
        start = lax.rem(self.me - slot + self.n, self.n) * self.rows
        return lax.dynamic_update_slice_in_dim(buf, block, start, 0)

    def steps(self):
        return self.n - 1

    def send(self):
        n = self.n
        self.pending = lax.ppermute(self.pending, self.axis, [(j, (j + 1) % n) for j in range(n)])

    def land(self):
        self.slots.append(self.pending)
        if self.buf is not None:
            self.buf = self.place(self.buf, self.pending, len(self.slots) - 1)

    def result(self):
        return self.buf


class RingScatter:
    def __init__(self, slots, axis, send_dtype):
        self.axis = axis
        self.n = lax.psum(1, axis)
        self.slots = slots
        self.send_dtype = send_dtype
        self.pending = None
        self.step = 0

    def steps(self):
        return self.n - 1

    def send(self):
        n, step = self.n, self.step + 1
        value = self.slots[step]
        if self.pending is not None:
            value = value + self.pending.astype(jnp.float32)
        self.pending = lax.ppermute(
            value.astype(self.send_dtype), self.axis, [(j, (j + 1) % n) for j in range(n)]
        )
        self.step = step

    def land(self):
        pass

    def result(self):
        return self.slots[0] + self.pending.astype(jnp.float32)


def ring_slots(partial, axis):
    n = lax.psum(1, axis)
    me = lax.axis_index(axis)
    rows = partial.shape[0] // n
    return [
        lax.dynamic_slice_in_dim(partial, lax.rem(me - slot + n, n) * rows, rows, 0)
        for slot in range(n)
    ]


def ring_all_gather(shard, axis):
    chain = RingGather(shard, axis, absolute=True)
    overlap(chain, [])
    return chain.result()


def ring_reduce_scatter(partial, axis, send_dtype):
    chain = RingScatter(ring_slots(partial, axis), axis, send_dtype)
    overlap(chain, [])
    return chain.result()


def overlap(chain, pieces):
    outputs = []
    count = chain.steps()
    for index in range(count):
        chain.send()
        if index < len(pieces):
            value = pieces[index](tuple(outputs))
            chain.pending, value = lax.optimization_barrier((chain.pending, value))
            outputs.append(value)
        else:
            chain.pending = lax.optimization_barrier(chain.pending)
        chain.land()
    for piece in pieces[count:]:
        outputs.append(piece(tuple(outputs)))
    return tuple(outputs)


COL = ("chip", "core")


def col_gather(block, axis):
    return lax.all_gather(block, COL, axis=axis, tiled=True)


def col_scatter(partial, axis):
    low_part = partial.astype(jnp.bfloat16)
    return lax.psum_scatter(low_part, COL, scatter_dimension=axis, tiled=True).astype(jnp.float32)


def layer_norm(inputs):
    center = inputs - jnp.mean(inputs, axis=-1, keepdims=True)
    spread = jnp.mean(center * center, axis=-1, keepdims=True)
    return center * lax.rsqrt(spread + EPSILON)


def norm_back(inputs, grad):
    center = inputs - jnp.mean(inputs, axis=-1, keepdims=True)
    inverse = lax.rsqrt(jnp.mean(center * center, axis=-1, keepdims=True) + EPSILON)
    normed = center * inverse
    return inverse * (
        grad
        - jnp.mean(grad, axis=-1, keepdims=True)
        - normed * jnp.mean(grad * normed, axis=-1, keepdims=True)
    )


def rope_tables():
    positions = jnp.arange(LENGTH, dtype=jnp.float32)
    freqs = jnp.power(jnp.float32(10000.0), -jnp.arange(HD // 2, dtype=jnp.float32) * (2.0 / HD))
    angles = positions[:, None] * freqs[None, :]
    return (jnp.cos(angles)[:, None, :], jnp.sin(angles)[:, None, :])


def rotate(field, cosine, sine):
    half_size = field.shape[-1] // 2
    first_half = field[..., :half_size]
    second_half = field[..., half_size:]
    return jnp.concatenate(
        [first_half * cosine - second_half * sine, second_half * cosine + first_half * sine],
        axis=-1,
    )


def unrotate(field, cosine, sine):
    half_size = field.shape[-1] // 2
    first_half = field[..., :half_size]
    second_half = field[..., half_size:]
    return jnp.concatenate(
        [first_half * cosine + second_half * sine, second_half * cosine - first_half * sine],
        axis=-1,
    )


def piece_mask(starts):
    positions = jnp.arange(LENGTH, dtype=jnp.int32)
    inside = (positions[None, :] >= starts[:, None]) & (
        positions[None, :] < starts[:, None] + PIECE
    )
    shared = jnp.any(inside[:, :, None] & inside[:, None, :], axis=0)
    causal = positions[None, :] <= positions[:, None]
    return causal | shared


def masked_scores(queries, keys_rot, starts):
    scale = 1.0 / math.sqrt(HD)
    scores = (
        jnp.einsum("qhd,khd->hqk", queries, keys_rot, preferred_element_type=jnp.float32) * scale
    )
    return jnp.where(piece_mask(starts)[None], scores, NEGATIVE)


def attend_forward(operands):
    queries, keys_rot, values, starts = operands
    scores = masked_scores(queries, keys_rot, starts)
    row_top = jnp.max(scores, axis=-1, keepdims=True)
    shifted = jnp.exp(scores - row_top)
    row_total = jnp.sum(shifted, axis=-1, keepdims=True)
    probs = (shifted / row_total).astype(jnp.bfloat16)
    mixed = jnp.einsum("hqk,khd->qhd", probs, values, preferred_element_type=jnp.float32)
    return (mixed, row_top + jnp.log(row_total))


def attend_backward(operands):
    queries, keys_rot, values, starts, log_total, grad_mixed = operands
    scale = 1.0 / math.sqrt(HD)
    scores = masked_scores(queries, keys_rot, starts)
    probs = jnp.exp(scores - log_total)
    probs_low = probs.astype(jnp.bfloat16)
    grad_values = jnp.einsum(
        "hqk,qhd->khd", probs_low, grad_mixed, preferred_element_type=jnp.float32
    )
    grad_probs = jnp.einsum("qhd,khd->hqk", grad_mixed, values, preferred_element_type=jnp.float32)
    inner = jnp.sum(probs * grad_probs, axis=-1, keepdims=True)
    grad_scores = (probs * (grad_probs - inner)).astype(jnp.bfloat16)
    grad_queries = (
        jnp.einsum("hqk,khd->qhd", grad_scores, keys_rot, preferred_element_type=jnp.float32)
        * scale
    )
    grad_keys = (
        jnp.einsum("hqk,qhd->khd", grad_scores, queries, preferred_element_type=jnp.float32) * scale
    )
    return (grad_queries, grad_keys, grad_values)


def per_device_body(
    layer_input, w_query, w_key, w_value, w_output, w_gate, w_up, w_down, piece_starts, cotangent
):
    seq_count = piece_starts.shape[0]
    group_rows = seq_count * LENGTH
    width = w_query.shape[1]
    hidden = w_gate.shape[1]
    heads_local = width // HD
    full_qkvo = col_gather(jnp.concatenate([w_query, w_key, w_value, w_output.T], axis=1), 0)
    full_qkv = full_qkvo[:, : 3 * width]
    output_t = full_qkvo[:, 3 * width :]
    full_gu = col_gather(jnp.concatenate([w_gate, w_up], axis=1), 0)
    full_down = col_gather(w_down, 1)
    cosine, sine = rope_tables()
    inputs = layer_input.astype(jnp.float32)
    normed_first = layer_norm(inputs).astype(jnp.bfloat16)
    first_rows = ring_all_gather(normed_first, "row")

    def split_heads(matrix):
        return matrix.reshape(seq_count, LENGTH, heads_local, HD)

    def merge_heads(field):
        return field.reshape(group_rows, heads_local * HD)

    def project(_):
        qkv_lin = product(first_rows, full_qkv)
        queries = rotate(split_heads(qkv_lin[:, :width]), cosine, sine).astype(jnp.bfloat16)
        keys_rot = rotate(split_heads(qkv_lin[:, width : 2 * width]), cosine, sine).astype(
            jnp.bfloat16
        )
        values = split_heads(qkv_lin[:, 2 * width :]).astype(jnp.bfloat16)
        return dict(queries=queries, keys_rot=keys_rot, values=values)

    def attend(done):
        state = done[0]
        mixed, log_total = lax.map(
            attend_forward, (state["queries"], state["keys_rot"], state["values"], piece_starts)
        )
        return dict(mixed=mixed, log_total=log_total)

    cot_later, first_rows = lax.optimization_barrier((cotangent, first_rows))
    cot_ring = RingGather(cot_later, "row")

    def attend_and_project(done):
        attention = attend(done)
        attended = merge_heads(attention["mixed"].astype(jnp.bfloat16))
        return dict(
            log_total=attention["log_total"],
            attended=attended,
            attn_partial=times_transpose(attended, output_t),
        )

    def early_cot_grads(done):
        return tuple(times_transpose(block, full_down) for block in cot_ring.slots)

    projected, mixed_out, early = overlap(cot_ring, [project, attend_and_project, early_cot_grads])
    cot_slots = cot_ring.slots
    queries, keys_rot = projected["queries"], projected["keys_rot"]
    values = projected["values"]
    log_total, attended = mixed_out["log_total"], mixed_out["attended"]
    attn_ring = RingScatter(ring_slots(mixed_out["attn_partial"], "row"), "row", jnp.bfloat16)

    def late_cot_grads(done):
        return tuple(times_transpose(block, full_down) for block in cot_slots[len(early) :])

    (late,) = overlap(attn_ring, [late_cot_grads])
    grad_act_slots = list(early) + list(late)
    attention_sum = attn_ring.result()
    middle = inputs + attention_sum
    normed_second = layer_norm(middle).astype(jnp.bfloat16)
    full_gu, normed_second = lax.optimization_barrier((full_gu, normed_second))
    second_ring = RingGather(normed_second, "row")
    slots = second_ring.n

    def ffn_forward(slot):
        def piece(done):
            gu_lin = product(second_ring.slots[slot], full_gu)
            gate_lin = gu_lin[:, :hidden]
            up_lin = gu_lin[:, hidden:]
            activation = (jax.nn.silu(gate_lin) * up_lin).astype(jnp.bfloat16)
            part = product(activation, full_down)
            return (gate_lin, up_lin, activation, part)

        return piece

    ffn = overlap(second_ring, [ffn_forward(slot) for slot in range(slots)])
    second_slots = second_ring.slots
    gate_slots = [item[0] for item in ffn]
    up_slots = [item[1] for item in ffn]
    act_slots = [item[2] for item in ffn]
    ffn_parts = [item[3] for item in ffn]

    def ffn_backward(slot):
        gate_lin, up_lin = gate_slots[slot], up_slots[slot]
        grad_activation = grad_act_slots[slot]
        sigma = jax.nn.sigmoid(gate_lin)
        grad_gate = grad_activation * up_lin * sigma * (1.0 + gate_lin * (1.0 - sigma))
        grad_up = grad_activation * gate_lin * sigma
        grad_gu = jnp.concatenate([grad_gate, grad_up], axis=1).astype(jnp.bfloat16)
        return (grad_gu, times_transpose(grad_gu, full_gu))

    second_ring_back = RingScatter([None] * slots, "row", jnp.bfloat16)
    grad_gu_slots = [None] * slots
    order = list(range(1, slots)) + [0]
    grad_gu_slots[order[0]], second_ring_back.slots[order[0]] = ffn_backward(order[0])
    grad_down_w = None
    for index in range(second_ring_back.steps()):
        second_ring_back.send()
        slot = order[index + 1]
        value = ffn_backward(slot)
        if index == 0:
            grad_down_w = contract_rows(
                jnp.concatenate(act_slots, axis=0), jnp.concatenate(cot_slots, axis=0)
            )
            value = value + (grad_down_w,)
        second_ring_back.pending, value = lax.optimization_barrier(
            (second_ring_back.pending, value)
        )
        grad_gu_slots[slot], second_ring_back.slots[slot] = value[0], value[1]
        if index == 0:
            grad_down_w = value[2]
    grad_second = second_ring_back.result()
    down_sum = col_scatter(grad_down_w, 1)
    grad_gu = jnp.concatenate(grad_gu_slots, axis=0)
    rows_second = jnp.concatenate(second_slots, axis=0)
    grad_middle = cotangent.astype(jnp.float32) + norm_back(middle, grad_second)
    branch_chain = RingGather(grad_middle.astype(jnp.bfloat16), "row", absolute=True)
    steps = branch_chain.steps()

    def gate_up_weight_grad(_):
        return contract_rows(rows_second, grad_gu)

    tied = overlap(
        branch_chain, [gate_up_weight_grad] + [lambda done: ()] * (steps - 2) + [lambda done: down_sum]
    )
    grad_gu_w, down_sum = tied[0], tied[-1]
    gu_sum = col_scatter(grad_gu_w, 0)
    grad_branch = branch_chain.result()
    ffn_parts, grad_branch = lax.optimization_barrier((ffn_parts, grad_branch))
    ffn_ring = RingScatter(list(ffn_parts), "row", jnp.bfloat16)
    output_sum = col_scatter(contract_rows(attended, grad_branch), 1)
    half = heads_local // 2

    def heads_backward(lo, hi):
        def piece(done):
            grad_mixed = product(grad_branch, output_t[:, lo * HD : hi * HD])
            grad_mixed = grad_mixed.astype(jnp.bfloat16).reshape(seq_count, LENGTH, hi - lo, HD)
            return lax.map(
                attend_backward,
                (
                    queries[:, :, lo:hi],
                    keys_rot[:, :, lo:hi],
                    values[:, :, lo:hi],
                    piece_starts,
                    log_total[:, lo:hi],
                    grad_mixed,
                ),
            )

        return piece

    def finish(done):
        parts = [jnp.concatenate([a[k] for a in done], axis=2) for k in range(3)]
        grad_q_rot, grad_k_rot, grad_values = parts
        grad_qkv = jnp.concatenate(
            [
                merge_heads(unrotate(grad_q_rot, cosine, sine)),
                merge_heads(unrotate(grad_k_rot, cosine, sine)),
                merge_heads(grad_values),
            ],
            axis=1,
        ).astype(jnp.bfloat16)
        return (grad_qkv, times_transpose(grad_qkv, full_qkv))

    def second_group_and_finish(done):
        return finish(done + (heads_backward(half, heads_local)(done),))

    pieces = [heads_backward(0, half), second_group_and_finish]
    grad_qkv, first_partial = overlap(ffn_ring, pieces)[-1]
    ffn_sum = ffn_ring.result()
    output = (middle + ffn_sum).astype(jnp.bfloat16)
    qkv_sum = col_scatter(contract_rows(first_rows, grad_qkv), 0)
    first_partial, gu_sum = lax.optimization_barrier((first_partial, gu_sum))
    grad_first = ring_reduce_scatter(first_partial, "row", jnp.bfloat16)
    grad_input = grad_middle + norm_back(inputs, grad_first)
    return (
        output,
        grad_input,
        qkv_sum[:, :width],
        qkv_sum[:, width : 2 * width],
        qkv_sum[:, 2 * width :],
        output_sum,
        gu_sum[:, :hidden],
        gu_sum[:, hidden:],
        down_sum,
    )


def solution(mesh):
    in_specs = (
        P(("chip", "core", "row"), None),
        P(COL, "row"),
        P(COL, "row"),
        P(COL, "row"),
        P("row", COL),
        P(COL, "row"),
        P(COL, "row"),
        P("row", COL),
        P(COL, None),
        P(("chip", "core", "row"), None),
    )
    out_specs = (
        P(("chip", "core", "row"), None),
        P(("chip", "core", "row"), None),
        P(COL, "row"),
        P(COL, "row"),
        P(COL, "row"),
        P("row", COL),
        P(COL, "row"),
        P(COL, "row"),
        P("row", COL),
    )
    devices = mesh.devices
    sub_mesh = Mesh(
        devices.reshape(devices.shape[0], devices.shape[1] // 2, 2), ("row", "chip", "core")
    )
    return jax.shard_map(
        per_device_body, mesh=sub_mesh, in_specs=in_specs, out_specs=out_specs, check_vma=False
    )
```

```python
import math

import jax
import jax.numpy as jnp
from jax import lax
from jax.sharding import Mesh, PartitionSpec as P


HD = 128
LENGTH = 1024
PIECE = 256


EPSILON = 1e-05
NEGATIVE = -1e30


def product(left, right):
    return jnp.dot(left, right, preferred_element_type=jnp.float32)


def contract_rows(left, right):
    return lax.dot_general(
        left, right, (((0,), (0,)), ((), ())), preferred_element_type=jnp.float32
    )


def times_transpose(left, right):
    return lax.dot_general(
        left, right, (((1,), (1,)), ((), ())), preferred_element_type=jnp.float32
    )


class GatherSteps:
    def __init__(self, shard, axis):
        self.axis = axis
        self.n = lax.psum(1, axis)
        self.me = lax.axis_index(axis)
        self.rows = shard.shape[0]
        buf = jnp.zeros(((3 * self.n - 2) * self.rows,) + shard.shape[1:], shard.dtype)
        self.buf = lax.dynamic_update_slice_in_dim(buf, shard, (self.me + self.n - 1) * self.rows, 0)
        self.pending = (shard, shard)
        self.step = 0

    def steps(self):
        return self.n - 1

    def send(self):
        n, step = self.n, self.step + 1
        from_left, from_right = self.pending
        from_left = lax.ppermute(from_left, self.axis, [(j, j + 1) for j in range(step - 1, n - 1)])
        from_right = lax.ppermute(from_right, self.axis, [(j, j - 1) for j in range(1, n - step + 1)])
        self.pending = (from_left, from_right)
        self.step = step

    def land(self):
        n, step, rows = self.n, self.step, self.rows
        from_left, from_right = self.pending
        self.buf = lax.dynamic_update_slice_in_dim(self.buf, from_left, (self.me - step + n - 1) * rows, 0)
        self.buf = lax.dynamic_update_slice_in_dim(self.buf, from_right, (self.me + step + n - 1) * rows, 0)

    def result(self):
        return self.buf[(self.n - 1) * self.rows : (2 * self.n - 1) * self.rows]


class ScatterSteps:
    def __init__(self, partial, axis, send_dtype):
        self.axis = axis
        self.n = lax.psum(1, axis)
        self.me = lax.axis_index(axis)
        self.rows = partial.shape[0] // self.n
        self.partial = partial
        self.send_dtype = send_dtype
        self.pending = None
        self.step = 0

    def steps(self):
        return self.n - 1

    def block(self, k):
        return lax.dynamic_slice_in_dim(
            self.partial, jnp.clip(k, 0, self.n - 1) * self.rows, self.rows, 0
        )

    def send(self):
        n, me, step = self.n, self.me, self.step + 1
        send_right = self.block(n - step + me)
        send_left = self.block(me + step - n)
        if self.pending is not None:
            send_right = send_right + self.pending[0].astype(jnp.float32)
            send_left = send_left + self.pending[1].astype(jnp.float32)
        recv_right = lax.ppermute(
            send_right.astype(self.send_dtype), self.axis, [(j, j + 1) for j in range(0, step)]
        )
        recv_left = lax.ppermute(
            send_left.astype(self.send_dtype), self.axis, [(j, j - 1) for j in range(n - step, n)]
        )
        self.pending = (recv_right, recv_left)
        self.step = step

    def land(self):
        pass

    def result(self):
        return (
            self.block(self.me)
            + self.pending[0].astype(jnp.float32)
            + self.pending[1].astype(jnp.float32)
        )


class RingGather:
    def __init__(self, shard, axis, absolute=False):
        self.axis = axis
        self.n = lax.psum(1, axis)
        self.me = lax.axis_index(axis)
        self.rows = shard.shape[0]
        self.slots = [shard]
        self.pending = shard
        self.buf = None
        if absolute:
            buf = jnp.zeros((self.n * self.rows,) + shard.shape[1:], shard.dtype)
            self.buf = self.place(buf, shard, 0)

    def place(self, buf, block, slot):
        start = lax.rem(self.me - slot + self.n, self.n) * self.rows
        return lax.dynamic_update_slice_in_dim(buf, block, start, 0)

    def steps(self):
        return self.n - 1

    def send(self):
        n = self.n
        self.pending = lax.ppermute(self.pending, self.axis, [(j, (j + 1) % n) for j in range(n)])

    def land(self):
        self.slots.append(self.pending)
        if self.buf is not None:
            self.buf = self.place(self.buf, self.pending, len(self.slots) - 1)

    def result(self):
        return self.buf


class RingScatter:
    def __init__(self, slots, axis, send_dtype):
        self.axis = axis
        self.n = lax.psum(1, axis)
        self.slots = slots
        self.send_dtype = send_dtype
        self.pending = None
        self.step = 0

    def steps(self):
        return self.n - 1

    def send(self):
        n, step = self.n, self.step + 1
        value = self.slots[step]
        if self.pending is not None:
            value = value + self.pending.astype(jnp.float32)
        self.pending = lax.ppermute(
            value.astype(self.send_dtype), self.axis, [(j, (j + 1) % n) for j in range(n)]
        )
        self.step = step

    def land(self):
        pass

    def result(self):
        return self.slots[0] + self.pending.astype(jnp.float32)


def ring_slots(partial, axis):
    n = lax.psum(1, axis)
    me = lax.axis_index(axis)
    rows = partial.shape[0] // n
    return [
        lax.dynamic_slice_in_dim(partial, lax.rem(me - slot + n, n) * rows, rows, 0)
        for slot in range(n)
    ]


def ring_all_gather(shard, axis):
    chain = RingGather(shard, axis, absolute=True)
    overlap(chain, [])
    return chain.result()


def ring_reduce_scatter(partial, axis, send_dtype):
    chain = RingScatter(ring_slots(partial, axis), axis, send_dtype)
    overlap(chain, [])
    return chain.result()


def overlap(chain, pieces):
    outputs = []
    count = chain.steps()
    for index in range(count):
        chain.send()
        if index < len(pieces):
            value = pieces[index](tuple(outputs))
            chain.pending, value = lax.optimization_barrier((chain.pending, value))
            outputs.append(value)
        else:
            chain.pending = lax.optimization_barrier(chain.pending)
        chain.land()
    for piece in pieces[count:]:
        outputs.append(piece(tuple(outputs)))
    return tuple(outputs)


COL = ("chip", "core")


def col_gather(block, axis):
    return lax.all_gather(block, COL, axis=axis, tiled=True)


def col_scatter(partial, axis):
    low_part = partial.astype(jnp.bfloat16)
    return lax.psum_scatter(low_part, COL, scatter_dimension=axis, tiled=True).astype(jnp.float32)


def layer_norm(inputs):
    center = inputs - jnp.mean(inputs, axis=-1, keepdims=True)
    spread = jnp.mean(center * center, axis=-1, keepdims=True)
    return center * lax.rsqrt(spread + EPSILON)


def norm_back(inputs, grad):
    center = inputs - jnp.mean(inputs, axis=-1, keepdims=True)
    inverse = lax.rsqrt(jnp.mean(center * center, axis=-1, keepdims=True) + EPSILON)
    normed = center * inverse
    return inverse * (
        grad
        - jnp.mean(grad, axis=-1, keepdims=True)
        - normed * jnp.mean(grad * normed, axis=-1, keepdims=True)
    )


def rope_tables():
    positions = jnp.arange(LENGTH, dtype=jnp.float32)
    freqs = jnp.power(jnp.float32(10000.0), -jnp.arange(HD // 2, dtype=jnp.float32) * (2.0 / HD))
    angles = positions[:, None] * freqs[None, :]
    return (jnp.cos(angles)[:, None, :], jnp.sin(angles)[:, None, :])


def rotate(field, cosine, sine):
    half_size = field.shape[-1] // 2
    first_half = field[..., :half_size]
    second_half = field[..., half_size:]
    return jnp.concatenate(
        [first_half * cosine - second_half * sine, second_half * cosine + first_half * sine],
        axis=-1,
    )


def unrotate(field, cosine, sine):
    half_size = field.shape[-1] // 2
    first_half = field[..., :half_size]
    second_half = field[..., half_size:]
    return jnp.concatenate(
        [first_half * cosine + second_half * sine, second_half * cosine - first_half * sine],
        axis=-1,
    )


def piece_mask(starts):
    positions = jnp.arange(LENGTH, dtype=jnp.int32)
    inside = (positions[None, :] >= starts[:, None]) & (
        positions[None, :] < starts[:, None] + PIECE
    )
    shared = jnp.any(inside[:, :, None] & inside[:, None, :], axis=0)
    causal = positions[None, :] <= positions[:, None]
    return causal | shared


def masked_scores(queries, keys_rot, starts):
    scale = 1.0 / math.sqrt(HD)
    scores = (
        jnp.einsum("qhd,khd->hqk", queries, keys_rot, preferred_element_type=jnp.float32) * scale
    )
    return jnp.where(piece_mask(starts)[None], scores, NEGATIVE)


def attend_forward(operands):
    queries, keys_rot, values, starts = operands
    scores = masked_scores(queries, keys_rot, starts)
    row_top = jnp.max(scores, axis=-1, keepdims=True)
    shifted = jnp.exp(scores - row_top)
    row_total = jnp.sum(shifted, axis=-1, keepdims=True)
    probs = (shifted / row_total).astype(jnp.bfloat16)
    mixed = jnp.einsum("hqk,khd->qhd", probs, values, preferred_element_type=jnp.float32)
    return (mixed, row_top + jnp.log(row_total))


def attend_backward(operands):
    queries, keys_rot, values, starts, log_total, grad_mixed = operands
    scale = 1.0 / math.sqrt(HD)
    scores = masked_scores(queries, keys_rot, starts)
    probs = jnp.exp(scores - log_total)
    probs_low = probs.astype(jnp.bfloat16)
    grad_values = jnp.einsum(
        "hqk,qhd->khd", probs_low, grad_mixed, preferred_element_type=jnp.float32
    )
    grad_probs = jnp.einsum("qhd,khd->hqk", grad_mixed, values, preferred_element_type=jnp.float32)
    inner = jnp.sum(probs * grad_probs, axis=-1, keepdims=True)
    grad_scores = (probs * (grad_probs - inner)).astype(jnp.bfloat16)
    grad_queries = (
        jnp.einsum("hqk,khd->qhd", grad_scores, keys_rot, preferred_element_type=jnp.float32)
        * scale
    )
    grad_keys = (
        jnp.einsum("hqk,qhd->khd", grad_scores, queries, preferred_element_type=jnp.float32) * scale
    )
    return (grad_queries, grad_keys, grad_values)


def per_device_body(
    layer_input, w_query, w_key, w_value, w_output, w_gate, w_up, w_down, piece_starts, cotangent
):
    seq_count = piece_starts.shape[0]
    group_rows = seq_count * LENGTH
    width = w_query.shape[1]
    hidden = w_gate.shape[1]
    heads_local = width // HD
    full_qkv = col_gather(jnp.concatenate([w_query, w_key, w_value], axis=1), 0)
    full_output = col_gather(w_output, 1)
    full_gu = col_gather(jnp.concatenate([w_gate, w_up], axis=1), 0)
    full_down = col_gather(w_down, 1)
    cosine, sine = rope_tables()
    inputs = layer_input.astype(jnp.float32)
    normed_first = layer_norm(inputs).astype(jnp.bfloat16)
    first_rows = ring_all_gather(normed_first, "row")

    def split_heads(matrix):
        return matrix.reshape(seq_count, LENGTH, heads_local, HD)

    def merge_heads(field):
        return field.reshape(group_rows, heads_local * HD)

    def project(_):
        qkv_lin = product(first_rows, full_qkv)
        queries = rotate(split_heads(qkv_lin[:, :width]), cosine, sine).astype(jnp.bfloat16)
        keys_rot = rotate(split_heads(qkv_lin[:, width : 2 * width]), cosine, sine).astype(
            jnp.bfloat16
        )
        values = split_heads(qkv_lin[:, 2 * width :]).astype(jnp.bfloat16)
        return dict(queries=queries, keys_rot=keys_rot, values=values)

    def attend(done):
        state = done[0]
        mixed, log_total = lax.map(
            attend_forward, (state["queries"], state["keys_rot"], state["values"], piece_starts)
        )
        return dict(mixed=mixed, log_total=log_total)

    def out_project(done):
        attended = merge_heads(done[1]["mixed"].astype(jnp.bfloat16))
        return dict(attended=attended, attn_partial=product(attended, full_output))

    cot_later, first_rows = lax.optimization_barrier((cotangent, first_rows))
    cot_ring = RingGather(cot_later, "row")
    projected, attention, mixed_out = overlap(cot_ring, [project, attend, out_project])
    cot_slots = cot_ring.slots
    queries, keys_rot = projected["queries"], projected["keys_rot"]
    values = projected["values"]
    log_total, attended = attention["log_total"], mixed_out["attended"]
    attn_ring = RingScatter(ring_slots(mixed_out["attn_partial"], "row"), "row", jnp.bfloat16)
    cot_count = len(cot_slots)
    per_step = -(-cot_count // attn_ring.steps())

    def cot_grads(index):
        def piece(done):
            chosen = cot_slots[index * per_step : (index + 1) * per_step]
            return tuple(times_transpose(block, full_down) for block in chosen)

        return piece

    grad_act_parts = overlap(attn_ring, [cot_grads(index) for index in range(attn_ring.steps())])
    grad_act_slots = [block for part in grad_act_parts for block in part]
    attention_sum = attn_ring.result()
    middle = inputs + attention_sum
    normed_second = layer_norm(middle).astype(jnp.bfloat16)
    second_ring = RingGather(normed_second, "row")
    slots = second_ring.n

    def ffn_forward(slot):
        def piece(done):
            gu_lin = product(second_ring.slots[slot], full_gu)
            gate_lin = gu_lin[:, :hidden]
            up_lin = gu_lin[:, hidden:]
            activation = (jax.nn.silu(gate_lin) * up_lin).astype(jnp.bfloat16)
            part = product(activation, full_down)
            return (gate_lin, up_lin, activation, part)

        return piece

    ffn = overlap(second_ring, [ffn_forward(slot) for slot in range(slots)])
    second_slots = second_ring.slots
    gate_slots = [item[0] for item in ffn]
    up_slots = [item[1] for item in ffn]
    act_slots = [item[2] for item in ffn]
    ffn_parts = [item[3] for item in ffn]

    def ffn_backward(slot):
        gate_lin, up_lin = gate_slots[slot], up_slots[slot]
        grad_activation = grad_act_slots[slot]
        sigma = jax.nn.sigmoid(gate_lin)
        grad_gate = grad_activation * up_lin * sigma * (1.0 + gate_lin * (1.0 - sigma))
        grad_up = grad_activation * gate_lin * sigma
        grad_gu = jnp.concatenate([grad_gate, grad_up], axis=1).astype(jnp.bfloat16)
        return (grad_gu, times_transpose(grad_gu, full_gu))

    second_ring_back = RingScatter([None] * slots, "row", jnp.bfloat16)
    grad_gu_slots = [None] * slots
    order = list(range(1, slots)) + [0]
    grad_gu_slots[order[0]], second_ring_back.slots[order[0]] = ffn_backward(order[0])
    grad_down_w = None
    for index in range(second_ring_back.steps()):
        second_ring_back.send()
        slot = order[index + 1]
        value = ffn_backward(slot)
        if index == 0:
            grad_down_w = contract_rows(
                jnp.concatenate(act_slots, axis=0), jnp.concatenate(cot_slots, axis=0)
            )
            value = value + (grad_down_w,)
        second_ring_back.pending, value = lax.optimization_barrier(
            (second_ring_back.pending, value)
        )
        grad_gu_slots[slot], second_ring_back.slots[slot] = value[0], value[1]
        if index == 0:
            grad_down_w = value[2]
    grad_second = second_ring_back.result()
    down_sum = col_scatter(grad_down_w, 1)
    grad_gu = jnp.concatenate(grad_gu_slots, axis=0)
    rows_second = jnp.concatenate(second_slots, axis=0)
    grad_middle = cotangent.astype(jnp.float32) + norm_back(middle, grad_second)
    branch_chain = RingGather(grad_middle.astype(jnp.bfloat16), "row", absolute=True)
    steps = branch_chain.steps()

    def gate_up_weight_grad(_):
        return contract_rows(rows_second, grad_gu)

    tied = overlap(
        branch_chain, [gate_up_weight_grad] + [lambda done: ()] * (steps - 2) + [lambda done: down_sum]
    )
    grad_gu_w, down_sum = tied[0], tied[-1]
    gu_sum = col_scatter(grad_gu_w, 0)
    grad_branch = branch_chain.result()
    ffn_parts, grad_branch = lax.optimization_barrier((ffn_parts, grad_branch))
    ffn_ring = RingScatter(list(ffn_parts), "row", jnp.bfloat16)
    output_sum = col_scatter(contract_rows(attended, grad_branch), 1)

    def heads_backward(lo, hi):
        def piece(done):
            grad_mixed = times_transpose(grad_branch, full_output[lo * HD : hi * HD])
            grad_mixed = grad_mixed.astype(jnp.bfloat16).reshape(seq_count, LENGTH, hi - lo, HD)
            return lax.map(
                attend_backward,
                (
                    queries[:, :, lo:hi],
                    keys_rot[:, :, lo:hi],
                    values[:, :, lo:hi],
                    piece_starts,
                    log_total[:, lo:hi],
                    grad_mixed,
                ),
            )

        return piece

    def finish(done):
        parts = [jnp.concatenate([a[k] for a in done], axis=2) for k in range(3)]
        grad_q_rot, grad_k_rot, grad_values = parts
        grad_qkv = jnp.concatenate(
            [
                merge_heads(unrotate(grad_q_rot, cosine, sine)),
                merge_heads(unrotate(grad_k_rot, cosine, sine)),
                merge_heads(grad_values),
            ],
            axis=1,
        ).astype(jnp.bfloat16)
        return (grad_qkv, times_transpose(grad_qkv, full_qkv))

    pieces = [heads_backward(0, heads_local), finish]
    grad_qkv, first_partial = overlap(ffn_ring, pieces)[-1]
    ffn_sum = ffn_ring.result()
    output = (middle + ffn_sum).astype(jnp.bfloat16)
    qkv_sum = col_scatter(contract_rows(first_rows, grad_qkv), 0)
    first_partial, gu_sum = lax.optimization_barrier((first_partial, gu_sum))
    grad_first = ring_reduce_scatter(first_partial, "row", jnp.bfloat16)
    grad_input = grad_middle + norm_back(inputs, grad_first)
    return (
        output,
        grad_input,
        qkv_sum[:, :width],
        qkv_sum[:, width : 2 * width],
        qkv_sum[:, 2 * width :],
        output_sum,
        gu_sum[:, :hidden],
        gu_sum[:, hidden:],
        down_sum,
    )


def solution(mesh):
    in_specs = (
        P(("chip", "core", "row"), None),
        P(COL, "row"),
        P(COL, "row"),
        P(COL, "row"),
        P("row", COL),
        P(COL, "row"),
        P(COL, "row"),
        P("row", COL),
        P(COL, None),
        P(("chip", "core", "row"), None),
    )
    out_specs = (
        P(("chip", "core", "row"), None),
        P(("chip", "core", "row"), None),
        P(COL, "row"),
        P(COL, "row"),
        P(COL, "row"),
        P("row", COL),
        P(COL, "row"),
        P(COL, "row"),
        P("row", COL),
    )
    devices = mesh.devices
    sub_mesh = Mesh(
        devices.reshape(devices.shape[0], devices.shape[1] // 2, 2), ("row", "chip", "core")
    )
    return jax.shard_map(
        per_device_body, mesh=sub_mesh, in_specs=in_specs, out_specs=out_specs, check_vma=False
    )
```

```python
import math

import jax
import jax.numpy as jnp
from jax import lax
from jax.sharding import Mesh, PartitionSpec as P


HD = 128
LENGTH = 1024
PIECE = 256


EPSILON = 1e-05
NEGATIVE = -1e30


def product(left, right):
    return jnp.dot(left, right, preferred_element_type=jnp.float32)


def contract_rows(left, right):
    return lax.dot_general(
        left, right, (((0,), (0,)), ((), ())), preferred_element_type=jnp.float32
    )


def times_transpose(left, right):
    return lax.dot_general(
        left, right, (((1,), (1,)), ((), ())), preferred_element_type=jnp.float32
    )


class GatherSteps:
    def __init__(self, shard, axis):
        self.axis = axis
        self.n = lax.psum(1, axis)
        self.me = lax.axis_index(axis)
        self.rows = shard.shape[0]
        buf = jnp.zeros(((3 * self.n - 2) * self.rows,) + shard.shape[1:], shard.dtype)
        self.buf = lax.dynamic_update_slice_in_dim(buf, shard, (self.me + self.n - 1) * self.rows, 0)
        self.pending = (shard, shard)
        self.step = 0

    def steps(self):
        return self.n - 1

    def send(self):
        n, step = self.n, self.step + 1
        from_left, from_right = self.pending
        from_left = lax.ppermute(from_left, self.axis, [(j, j + 1) for j in range(step - 1, n - 1)])
        from_right = lax.ppermute(from_right, self.axis, [(j, j - 1) for j in range(1, n - step + 1)])
        self.pending = (from_left, from_right)
        self.step = step

    def land(self):
        n, step, rows = self.n, self.step, self.rows
        from_left, from_right = self.pending
        self.buf = lax.dynamic_update_slice_in_dim(self.buf, from_left, (self.me - step + n - 1) * rows, 0)
        self.buf = lax.dynamic_update_slice_in_dim(self.buf, from_right, (self.me + step + n - 1) * rows, 0)

    def result(self):
        return self.buf[(self.n - 1) * self.rows : (2 * self.n - 1) * self.rows]


class ScatterSteps:
    def __init__(self, partial, axis, send_dtype):
        self.axis = axis
        self.n = lax.psum(1, axis)
        self.me = lax.axis_index(axis)
        self.rows = partial.shape[0] // self.n
        self.partial = partial
        self.send_dtype = send_dtype
        self.pending = None
        self.step = 0

    def steps(self):
        return self.n - 1

    def block(self, k):
        return lax.dynamic_slice_in_dim(
            self.partial, jnp.clip(k, 0, self.n - 1) * self.rows, self.rows, 0
        )

    def send(self):
        n, me, step = self.n, self.me, self.step + 1
        send_right = self.block(n - step + me)
        send_left = self.block(me + step - n)
        if self.pending is not None:
            send_right = send_right + self.pending[0].astype(jnp.float32)
            send_left = send_left + self.pending[1].astype(jnp.float32)
        recv_right = lax.ppermute(
            send_right.astype(self.send_dtype), self.axis, [(j, j + 1) for j in range(0, step)]
        )
        recv_left = lax.ppermute(
            send_left.astype(self.send_dtype), self.axis, [(j, j - 1) for j in range(n - step, n)]
        )
        self.pending = (recv_right, recv_left)
        self.step = step

    def land(self):
        pass

    def result(self):
        return (
            self.block(self.me)
            + self.pending[0].astype(jnp.float32)
            + self.pending[1].astype(jnp.float32)
        )


class RingGather:
    def __init__(self, shard, axis, absolute=False):
        self.axis = axis
        self.n = lax.psum(1, axis)
        self.me = lax.axis_index(axis)
        self.rows = shard.shape[0]
        self.slots = [shard]
        self.pending = shard
        self.absolute = absolute
        self.buf = None

    def place(self, buf, block, slot):
        start = lax.rem(self.me - slot + self.n, self.n) * self.rows
        return lax.dynamic_update_slice_in_dim(buf, block, start, 0)

    def steps(self):
        return self.n - 1

    def send(self):
        n = self.n
        self.pending = lax.ppermute(self.pending, self.axis, [(j, (j + 1) % n) for j in range(n)])

    def land(self):
        self.slots.append(self.pending)
        if self.absolute:
            if self.buf is None:
                shard = self.slots[0]
                buf = jnp.zeros((self.n * self.rows,) + shard.shape[1:], shard.dtype)
                self.buf = self.place(buf, shard, 0)
            self.buf = self.place(self.buf, self.pending, len(self.slots) - 1)

    def result(self):
        return self.buf


class RingScatter:
    def __init__(self, slots, axis, send_dtype):
        self.axis = axis
        self.n = lax.psum(1, axis)
        self.slots = slots
        self.send_dtype = send_dtype
        self.pending = None
        self.step = 0

    def steps(self):
        return self.n - 1

    def send(self):
        n, step = self.n, self.step + 1
        value = self.slots[step]
        if self.pending is not None:
            value = value + self.pending.astype(jnp.float32)
        self.pending = lax.ppermute(
            value.astype(self.send_dtype), self.axis, [(j, (j + 1) % n) for j in range(n)]
        )
        self.step = step

    def land(self):
        pass

    def result(self):
        return self.slots[0] + self.pending.astype(jnp.float32)


def ring_slots(partial, axis):
    n = lax.psum(1, axis)
    me = lax.axis_index(axis)
    rows = partial.shape[0] // n
    return [
        lax.dynamic_slice_in_dim(partial, lax.rem(me - slot + n, n) * rows, rows, 0)
        for slot in range(n)
    ]


def ring_all_gather(shard, axis):
    chain = RingGather(shard, axis, absolute=True)
    overlap(chain, [])
    return chain.result()


def ring_reduce_scatter(partial, axis, send_dtype):
    chain = RingScatter(ring_slots(partial, axis), axis, send_dtype)
    overlap(chain, [])
    return chain.result()


def overlap(chain, pieces):
    outputs = []
    count = chain.steps()
    for index in range(count):
        chain.send()
        if index < len(pieces):
            value = pieces[index](tuple(outputs))
            chain.pending, value = lax.optimization_barrier((chain.pending, value))
            outputs.append(value)
        else:
            chain.pending = lax.optimization_barrier(chain.pending)
        chain.land()
    for piece in pieces[count:]:
        outputs.append(piece(tuple(outputs)))
    return tuple(outputs)


COL = ("chip", "core")


def col_gather(block, axis):
    return lax.all_gather(block, COL, axis=axis, tiled=True)


def col_scatter(partial, axis):
    low_part = partial.astype(jnp.bfloat16)
    return lax.psum_scatter(low_part, COL, scatter_dimension=axis, tiled=True).astype(jnp.float32)


def layer_norm(inputs):
    center = inputs - jnp.mean(inputs, axis=-1, keepdims=True)
    spread = jnp.mean(center * center, axis=-1, keepdims=True)
    return center * lax.rsqrt(spread + EPSILON)


def norm_back(inputs, grad):
    center = inputs - jnp.mean(inputs, axis=-1, keepdims=True)
    inverse = lax.rsqrt(jnp.mean(center * center, axis=-1, keepdims=True) + EPSILON)
    normed = center * inverse
    return inverse * (
        grad
        - jnp.mean(grad, axis=-1, keepdims=True)
        - normed * jnp.mean(grad * normed, axis=-1, keepdims=True)
    )


def rope_tables():
    positions = jnp.arange(LENGTH, dtype=jnp.float32)
    freqs = jnp.power(jnp.float32(10000.0), -jnp.arange(HD // 2, dtype=jnp.float32) * (2.0 / HD))
    angles = positions[:, None] * freqs[None, :]
    return (jnp.cos(angles)[:, None, :], jnp.sin(angles)[:, None, :])


def rotate(field, cosine, sine):
    half_size = field.shape[-1] // 2
    first_half = field[..., :half_size]
    second_half = field[..., half_size:]
    return jnp.concatenate(
        [first_half * cosine - second_half * sine, second_half * cosine + first_half * sine],
        axis=-1,
    )


def unrotate(field, cosine, sine):
    half_size = field.shape[-1] // 2
    first_half = field[..., :half_size]
    second_half = field[..., half_size:]
    return jnp.concatenate(
        [first_half * cosine + second_half * sine, second_half * cosine - first_half * sine],
        axis=-1,
    )


def piece_mask(starts):
    positions = jnp.arange(LENGTH, dtype=jnp.int32)
    inside = (positions[None, :] >= starts[:, None]) & (
        positions[None, :] < starts[:, None] + PIECE
    )
    shared = jnp.any(inside[:, :, None] & inside[:, None, :], axis=0)
    causal = positions[None, :] <= positions[:, None]
    return causal | shared


def masked_scores(queries, keys_rot, starts):
    scale = 1.0 / math.sqrt(HD)
    scores = (
        jnp.einsum("qhd,khd->hqk", queries, keys_rot, preferred_element_type=jnp.float32) * scale
    )
    return jnp.where(piece_mask(starts)[None], scores, NEGATIVE)


def attend_forward(operands):
    queries, keys_rot, values, starts = operands
    scores = masked_scores(queries, keys_rot, starts)
    row_top = jnp.max(scores, axis=-1, keepdims=True)
    shifted = jnp.exp(scores - row_top)
    row_total = jnp.sum(shifted, axis=-1, keepdims=True)
    probs = (shifted / row_total).astype(jnp.bfloat16)
    mixed = jnp.einsum("hqk,khd->qhd", probs, values, preferred_element_type=jnp.float32)
    return (mixed, row_top + jnp.log(row_total))


def attend_backward(operands):
    queries, keys_rot, values, starts, log_total, grad_mixed = operands
    scale = 1.0 / math.sqrt(HD)
    scores = masked_scores(queries, keys_rot, starts)
    probs = jnp.exp(scores - log_total)
    probs_low = probs.astype(jnp.bfloat16)
    grad_values = jnp.einsum(
        "hqk,qhd->khd", probs_low, grad_mixed, preferred_element_type=jnp.float32
    )
    grad_probs = jnp.einsum("qhd,khd->hqk", grad_mixed, values, preferred_element_type=jnp.float32)
    inner = jnp.sum(probs * grad_probs, axis=-1, keepdims=True)
    grad_scores = (probs * (grad_probs - inner)).astype(jnp.bfloat16)
    grad_queries = (
        jnp.einsum("hqk,khd->qhd", grad_scores, keys_rot, preferred_element_type=jnp.float32)
        * scale
    )
    grad_keys = (
        jnp.einsum("hqk,qhd->khd", grad_scores, queries, preferred_element_type=jnp.float32) * scale
    )
    return (grad_queries, grad_keys, grad_values)


def per_device_body(
    layer_input, w_query, w_key, w_value, w_output, w_gate, w_up, w_down, piece_starts, cotangent
):
    seq_count = piece_starts.shape[0]
    group_rows = seq_count * LENGTH
    width = w_query.shape[1]
    hidden = w_gate.shape[1]
    heads_local = width // HD
    full_qkv = col_gather(jnp.concatenate([w_query, w_key, w_value], axis=1), 0)
    full_output = col_gather(w_output, 1)
    full_gu = col_gather(jnp.concatenate([w_gate, w_up], axis=1), 0)
    full_down = col_gather(w_down, 1)
    cosine, sine = rope_tables()
    inputs = layer_input.astype(jnp.float32)
    normed_first = layer_norm(inputs).astype(jnp.bfloat16)
    first_rows = ring_all_gather(normed_first, "row")

    def split_heads(matrix):
        return matrix.reshape(seq_count, LENGTH, heads_local, HD)

    def merge_heads(field):
        return field.reshape(group_rows, heads_local * HD)

    def project(_):
        qkv_lin = product(first_rows, full_qkv)
        queries = rotate(split_heads(qkv_lin[:, :width]), cosine, sine).astype(jnp.bfloat16)
        keys_rot = rotate(split_heads(qkv_lin[:, width : 2 * width]), cosine, sine).astype(
            jnp.bfloat16
        )
        values = split_heads(qkv_lin[:, 2 * width :]).astype(jnp.bfloat16)
        return dict(queries=queries, keys_rot=keys_rot, values=values)

    def attend(done):
        state = done[0]
        mixed, log_total = lax.map(
            attend_forward, (state["queries"], state["keys_rot"], state["values"], piece_starts)
        )
        return dict(mixed=mixed, log_total=log_total)

    def out_project(done):
        attended = merge_heads(done[1]["mixed"].astype(jnp.bfloat16))
        return dict(attended=attended, attn_partial=product(attended, full_output))

    cot_later, first_rows = lax.optimization_barrier((cotangent, first_rows))
    cot_ring = RingGather(cot_later, "row")
    projected, attention, mixed_out = overlap(cot_ring, [project, attend, out_project])
    cot_slots = cot_ring.slots
    queries, keys_rot = projected["queries"], projected["keys_rot"]
    values = projected["values"]
    log_total, attended = attention["log_total"], mixed_out["attended"]
    attn_ring = RingScatter(ring_slots(mixed_out["attn_partial"], "row"), "row", jnp.bfloat16)
    cot_count = len(cot_slots)
    per_step = -(-cot_count // attn_ring.steps())

    def cot_grads(index):
        def piece(done):
            chosen = cot_slots[index * per_step : (index + 1) * per_step]
            return tuple(times_transpose(block, full_down) for block in chosen)

        return piece

    grad_act_parts = overlap(attn_ring, [cot_grads(index) for index in range(attn_ring.steps())])
    grad_act_slots = [block for part in grad_act_parts for block in part]
    attention_sum = attn_ring.result()
    middle = inputs + attention_sum
    normed_second = layer_norm(middle).astype(jnp.bfloat16)
    second_ring = RingGather(normed_second, "row")
    slots = second_ring.n

    def ffn_forward(slot):
        def piece(done):
            gu_lin = product(second_ring.slots[slot], full_gu)
            gate_lin = gu_lin[:, :hidden]
            up_lin = gu_lin[:, hidden:]
            activation = (jax.nn.silu(gate_lin) * up_lin).astype(jnp.bfloat16)
            part = product(activation, full_down)
            return (gate_lin, up_lin, activation, part)

        return piece

    ffn = overlap(second_ring, [ffn_forward(slot) for slot in range(slots)])
    second_slots = second_ring.slots
    gate_slots = [item[0] for item in ffn]
    up_slots = [item[1] for item in ffn]
    act_slots = [item[2] for item in ffn]
    ffn_parts = [item[3] for item in ffn]

    def ffn_backward(slot):
        gate_lin, up_lin = gate_slots[slot], up_slots[slot]
        grad_activation = grad_act_slots[slot]
        sigma = jax.nn.sigmoid(gate_lin)
        grad_gate = grad_activation * up_lin * sigma * (1.0 + gate_lin * (1.0 - sigma))
        grad_up = grad_activation * gate_lin * sigma
        grad_gu = jnp.concatenate([grad_gate, grad_up], axis=1).astype(jnp.bfloat16)
        return (grad_gu, times_transpose(grad_gu, full_gu))

    second_ring_back = RingScatter([None] * slots, "row", jnp.bfloat16)
    grad_gu_slots = [None] * slots
    order = list(range(1, slots)) + [0]
    grad_gu_slots[order[0]], second_ring_back.slots[order[0]] = ffn_backward(order[0])
    grad_down_w = None
    for index in range(second_ring_back.steps()):
        second_ring_back.send()
        slot = order[index + 1]
        value = ffn_backward(slot)
        if index == 0:
            grad_down_w = contract_rows(
                jnp.concatenate(act_slots, axis=0), jnp.concatenate(cot_slots, axis=0)
            )
            value = value + (grad_down_w,)
        second_ring_back.pending, value = lax.optimization_barrier(
            (second_ring_back.pending, value)
        )
        grad_gu_slots[slot], second_ring_back.slots[slot] = value[0], value[1]
        if index == 0:
            grad_down_w = value[2]
    grad_second = second_ring_back.result()
    down_sum = col_scatter(grad_down_w, 1)
    grad_gu = jnp.concatenate(grad_gu_slots, axis=0)
    rows_second = jnp.concatenate(second_slots, axis=0)
    grad_middle = cotangent.astype(jnp.float32) + norm_back(middle, grad_second)
    branch_chain = RingGather(grad_middle.astype(jnp.bfloat16), "row", absolute=True)
    steps = branch_chain.steps()

    def gate_up_weight_grad(_):
        return contract_rows(rows_second, grad_gu)

    tied = overlap(
        branch_chain, [gate_up_weight_grad] + [lambda done: ()] * (steps - 2) + [lambda done: down_sum]
    )
    grad_gu_w, down_sum = tied[0], tied[-1]
    gu_sum = col_scatter(grad_gu_w, 0)
    grad_branch = branch_chain.result()
    ffn_parts, grad_branch = lax.optimization_barrier((ffn_parts, grad_branch))
    ffn_ring = RingScatter(list(ffn_parts), "row", jnp.bfloat16)
    output_sum = col_scatter(contract_rows(attended, grad_branch), 1)
    half = heads_local // 2

    def heads_backward(lo, hi):
        def piece(done):
            grad_mixed = times_transpose(grad_branch, full_output[lo * HD : hi * HD])
            grad_mixed = grad_mixed.astype(jnp.bfloat16).reshape(seq_count, LENGTH, hi - lo, HD)
            return lax.map(
                attend_backward,
                (
                    queries[:, :, lo:hi],
                    keys_rot[:, :, lo:hi],
                    values[:, :, lo:hi],
                    piece_starts,
                    log_total[:, lo:hi],
                    grad_mixed,
                ),
            )

        return piece

    def finish(done):
        parts = [jnp.concatenate([a[k] for a in done], axis=2) for k in range(3)]
        grad_q_rot, grad_k_rot, grad_values = parts
        grad_qkv = jnp.concatenate(
            [
                merge_heads(unrotate(grad_q_rot, cosine, sine)),
                merge_heads(unrotate(grad_k_rot, cosine, sine)),
                merge_heads(grad_values),
            ],
            axis=1,
        ).astype(jnp.bfloat16)
        return (grad_qkv, times_transpose(grad_qkv, full_qkv))

    def second_group_and_finish(done):
        return finish(done + (heads_backward(half, heads_local)(done),))

    pieces = [heads_backward(0, half), second_group_and_finish]
    grad_qkv, first_partial = overlap(ffn_ring, pieces)[-1]
    ffn_sum = ffn_ring.result()
    output = (middle + ffn_sum).astype(jnp.bfloat16)
    qkv_sum = col_scatter(contract_rows(first_rows, grad_qkv), 0)
    first_partial, gu_sum = lax.optimization_barrier((first_partial, gu_sum))
    grad_first = ring_reduce_scatter(first_partial, "row", jnp.bfloat16)
    grad_input = grad_middle + norm_back(inputs, grad_first)
    return (
        output,
        grad_input,
        qkv_sum[:, :width],
        qkv_sum[:, width : 2 * width],
        qkv_sum[:, 2 * width :],
        output_sum,
        gu_sum[:, :hidden],
        gu_sum[:, hidden:],
        down_sum,
    )


def solution(mesh):
    in_specs = (
        P(("chip", "core", "row"), None),
        P(COL, "row"),
        P(COL, "row"),
        P(COL, "row"),
        P("row", COL),
        P(COL, "row"),
        P(COL, "row"),
        P("row", COL),
        P(COL, None),
        P(("chip", "core", "row"), None),
    )
    out_specs = (
        P(("chip", "core", "row"), None),
        P(("chip", "core", "row"), None),
        P(COL, "row"),
        P(COL, "row"),
        P(COL, "row"),
        P("row", COL),
        P(COL, "row"),
        P(COL, "row"),
        P("row", COL),
    )
    devices = mesh.devices
    sub_mesh = Mesh(
        devices.reshape(devices.shape[0], devices.shape[1] // 2, 2), ("row", "chip", "core")
    )
    return jax.shard_map(
        per_device_body, mesh=sub_mesh, in_specs=in_specs, out_specs=out_specs, check_vma=False
    )
```

```python
import math

import jax
import jax.numpy as jnp
from jax import lax
from jax.sharding import Mesh, PartitionSpec as P


HD = 128
LENGTH = 1024
PIECE = 256


EPSILON = 1e-05
NEGATIVE = -1e30


def product(left, right):
    return jnp.dot(left, right, preferred_element_type=jnp.float32)


def contract_rows(left, right):
    return lax.dot_general(
        left, right, (((0,), (0,)), ((), ())), preferred_element_type=jnp.float32
    )


def times_transpose(left, right):
    return lax.dot_general(
        left, right, (((1,), (1,)), ((), ())), preferred_element_type=jnp.float32
    )


class GatherSteps:
    def __init__(self, shard, axis):
        self.axis = axis
        self.n = lax.psum(1, axis)
        self.me = lax.axis_index(axis)
        self.rows = shard.shape[0]
        buf = jnp.zeros(((3 * self.n - 2) * self.rows,) + shard.shape[1:], shard.dtype)
        self.buf = lax.dynamic_update_slice_in_dim(buf, shard, (self.me + self.n - 1) * self.rows, 0)
        self.pending = (shard, shard)
        self.step = 0

    def steps(self):
        return self.n - 1

    def send(self):
        n, step = self.n, self.step + 1
        from_left, from_right = self.pending
        from_left = lax.ppermute(from_left, self.axis, [(j, j + 1) for j in range(step - 1, n - 1)])
        from_right = lax.ppermute(from_right, self.axis, [(j, j - 1) for j in range(1, n - step + 1)])
        self.pending = (from_left, from_right)
        self.step = step

    def land(self):
        n, step, rows = self.n, self.step, self.rows
        from_left, from_right = self.pending
        self.buf = lax.dynamic_update_slice_in_dim(self.buf, from_left, (self.me - step + n - 1) * rows, 0)
        self.buf = lax.dynamic_update_slice_in_dim(self.buf, from_right, (self.me + step + n - 1) * rows, 0)

    def result(self):
        return self.buf[(self.n - 1) * self.rows : (2 * self.n - 1) * self.rows]


class ScatterSteps:
    def __init__(self, partial, axis, send_dtype):
        self.axis = axis
        self.n = lax.psum(1, axis)
        self.me = lax.axis_index(axis)
        self.rows = partial.shape[0] // self.n
        self.partial = partial
        self.send_dtype = send_dtype
        self.pending = None
        self.step = 0

    def steps(self):
        return self.n - 1

    def block(self, k):
        return lax.dynamic_slice_in_dim(
            self.partial, jnp.clip(k, 0, self.n - 1) * self.rows, self.rows, 0
        )

    def send(self):
        n, me, step = self.n, self.me, self.step + 1
        send_right = self.block(n - step + me)
        send_left = self.block(me + step - n)
        if self.pending is not None:
            send_right = send_right + self.pending[0].astype(jnp.float32)
            send_left = send_left + self.pending[1].astype(jnp.float32)
        recv_right = lax.ppermute(
            send_right.astype(self.send_dtype), self.axis, [(j, j + 1) for j in range(0, step)]
        )
        recv_left = lax.ppermute(
            send_left.astype(self.send_dtype), self.axis, [(j, j - 1) for j in range(n - step, n)]
        )
        self.pending = (recv_right, recv_left)
        self.step = step

    def land(self):
        pass

    def result(self):
        return (
            self.block(self.me)
            + self.pending[0].astype(jnp.float32)
            + self.pending[1].astype(jnp.float32)
        )


class RingGather:
    def __init__(self, shard, axis, absolute=False):
        self.axis = axis
        self.n = lax.psum(1, axis)
        self.me = lax.axis_index(axis)
        self.rows = shard.shape[0]
        self.slots = [shard]
        self.pending = shard
        self.buf = None
        if absolute:
            buf = jnp.zeros((self.n * self.rows,) + shard.shape[1:], shard.dtype)
            self.buf = self.place(buf, shard, 0)

    def place(self, buf, block, slot):
        start = lax.rem(self.me - slot + self.n, self.n) * self.rows
        return lax.dynamic_update_slice_in_dim(buf, block, start, 0)

    def steps(self):
        return self.n - 1

    def send(self):
        n = self.n
        self.pending = lax.ppermute(self.pending, self.axis, [(j, (j + 1) % n) for j in range(n)])

    def land(self):
        self.slots.append(self.pending)
        if self.buf is not None:
            self.buf = self.place(self.buf, self.pending, len(self.slots) - 1)

    def result(self):
        return self.buf


class RingScatter:
    def __init__(self, slots, axis, send_dtype):
        self.axis = axis
        self.n = lax.psum(1, axis)
        self.slots = slots
        self.send_dtype = send_dtype
        self.pending = None
        self.step = 0

    def steps(self):
        return self.n - 1

    def send(self):
        n, step = self.n, self.step + 1
        value = self.slots[step].astype(jnp.float32)
        if self.pending is not None:
            value = value + self.pending.astype(jnp.float32)
        self.pending = lax.ppermute(
            value.astype(self.send_dtype), self.axis, [(j, (j + 1) % n) for j in range(n)]
        )
        self.step = step

    def land(self):
        pass

    def result(self):
        return self.slots[0].astype(jnp.float32) + self.pending.astype(jnp.float32)


def ring_slots(partial, axis):
    n = lax.psum(1, axis)
    me = lax.axis_index(axis)
    rows = partial.shape[0] // n
    return [
        lax.dynamic_slice_in_dim(partial, lax.rem(me - slot + n, n) * rows, rows, 0)
        for slot in range(n)
    ]


def ring_all_gather(shard, axis):
    chain = RingGather(shard, axis, absolute=True)
    overlap(chain, [])
    return chain.result()


def ring_reduce_scatter(partial, axis, send_dtype):
    chain = RingScatter(ring_slots(partial, axis), axis, send_dtype)
    overlap(chain, [])
    return chain.result()


def overlap(chain, pieces):
    outputs = []
    count = chain.steps()
    for index in range(count):
        chain.send()
        if index < len(pieces):
            value = pieces[index](tuple(outputs))
            chain.pending, value = lax.optimization_barrier((chain.pending, value))
            outputs.append(value)
        else:
            chain.pending = lax.optimization_barrier(chain.pending)
        chain.land()
    for piece in pieces[count:]:
        outputs.append(piece(tuple(outputs)))
    return tuple(outputs)


COL = ("chip", "core")


def col_gather(block, axis):
    return lax.all_gather(block, COL, axis=axis, tiled=True)


def col_scatter(partial, axis):
    low_part = partial.astype(jnp.bfloat16)
    return lax.psum_scatter(low_part, COL, scatter_dimension=axis, tiled=True).astype(jnp.float32)


def layer_norm(inputs):
    center = inputs - jnp.mean(inputs, axis=-1, keepdims=True)
    spread = jnp.mean(center * center, axis=-1, keepdims=True)
    return center * lax.rsqrt(spread + EPSILON)


def norm_back(inputs, grad):
    center = inputs - jnp.mean(inputs, axis=-1, keepdims=True)
    inverse = lax.rsqrt(jnp.mean(center * center, axis=-1, keepdims=True) + EPSILON)
    normed = center * inverse
    return inverse * (
        grad
        - jnp.mean(grad, axis=-1, keepdims=True)
        - normed * jnp.mean(grad * normed, axis=-1, keepdims=True)
    )


def rope_tables():
    positions = jnp.arange(LENGTH, dtype=jnp.float32)
    freqs = jnp.power(jnp.float32(10000.0), -jnp.arange(HD // 2, dtype=jnp.float32) * (2.0 / HD))
    angles = positions[:, None] * freqs[None, :]
    return (jnp.cos(angles)[:, None, :], jnp.sin(angles)[:, None, :])


def rotate(field, cosine, sine):
    half_size = field.shape[-1] // 2
    first_half = field[..., :half_size]
    second_half = field[..., half_size:]
    return jnp.concatenate(
        [first_half * cosine - second_half * sine, second_half * cosine + first_half * sine],
        axis=-1,
    )


def unrotate(field, cosine, sine):
    half_size = field.shape[-1] // 2
    first_half = field[..., :half_size]
    second_half = field[..., half_size:]
    return jnp.concatenate(
        [first_half * cosine + second_half * sine, second_half * cosine - first_half * sine],
        axis=-1,
    )


def piece_mask(starts):
    positions = jnp.arange(LENGTH, dtype=jnp.int32)
    inside = (positions[None, :] >= starts[:, None]) & (
        positions[None, :] < starts[:, None] + PIECE
    )
    shared = jnp.any(inside[:, :, None] & inside[:, None, :], axis=0)
    causal = positions[None, :] <= positions[:, None]
    return causal | shared


def masked_scores(queries, keys_rot, starts):
    scale = 1.0 / math.sqrt(HD)
    scores = (
        jnp.einsum("qhd,khd->hqk", queries, keys_rot, preferred_element_type=jnp.float32) * scale
    )
    return jnp.where(piece_mask(starts)[None], scores, NEGATIVE)


def attend_forward(operands):
    queries, keys_rot, values, starts = operands
    scores = masked_scores(queries, keys_rot, starts)
    row_top = jnp.max(scores, axis=-1, keepdims=True)
    shifted = jnp.exp(scores - row_top)
    row_total = jnp.sum(shifted, axis=-1, keepdims=True)
    probs = (shifted / row_total).astype(jnp.bfloat16)
    mixed = jnp.einsum("hqk,khd->qhd", probs, values, preferred_element_type=jnp.float32)
    return (mixed, row_top + jnp.log(row_total))


def attend_backward(operands):
    queries, keys_rot, values, starts, log_total, grad_mixed = operands
    scale = 1.0 / math.sqrt(HD)
    scores = masked_scores(queries, keys_rot, starts)
    probs = jnp.exp(scores - log_total)
    probs_low = probs.astype(jnp.bfloat16)
    grad_values = jnp.einsum(
        "hqk,qhd->khd", probs_low, grad_mixed, preferred_element_type=jnp.float32
    )
    grad_probs = jnp.einsum("qhd,khd->hqk", grad_mixed, values, preferred_element_type=jnp.float32)
    inner = jnp.sum(probs * grad_probs, axis=-1, keepdims=True)
    grad_scores = (probs * (grad_probs - inner)).astype(jnp.bfloat16)
    grad_queries = (
        jnp.einsum("hqk,khd->qhd", grad_scores, keys_rot, preferred_element_type=jnp.float32)
        * scale
    )
    grad_keys = (
        jnp.einsum("hqk,qhd->khd", grad_scores, queries, preferred_element_type=jnp.float32) * scale
    )
    return (grad_queries, grad_keys, grad_values)


def per_device_body(
    layer_input, w_query, w_key, w_value, w_output, w_gate, w_up, w_down, piece_starts, cotangent
):
    seq_count = piece_starts.shape[0]
    group_rows = seq_count * LENGTH
    width = w_query.shape[1]
    hidden = w_gate.shape[1]
    heads_local = width // HD
    full_qkv = col_gather(jnp.concatenate([w_query, w_key, w_value], axis=1), 0)
    full_output = col_gather(w_output, 1)
    full_gu = col_gather(jnp.concatenate([w_gate, w_up], axis=1), 0)
    full_down = col_gather(w_down, 1)
    cosine, sine = rope_tables()
    inputs = layer_input.astype(jnp.float32)
    normed_first = layer_norm(inputs).astype(jnp.bfloat16)
    first_rows = ring_all_gather(normed_first, "row")

    def split_heads(matrix):
        return matrix.reshape(seq_count, LENGTH, heads_local, HD)

    def merge_heads(field):
        return field.reshape(group_rows, heads_local * HD)

    def project(_):
        qkv_lin = product(first_rows, full_qkv)
        queries = rotate(split_heads(qkv_lin[:, :width]), cosine, sine).astype(jnp.bfloat16)
        keys_rot = rotate(split_heads(qkv_lin[:, width : 2 * width]), cosine, sine).astype(
            jnp.bfloat16
        )
        values = split_heads(qkv_lin[:, 2 * width :]).astype(jnp.bfloat16)
        return dict(queries=queries, keys_rot=keys_rot, values=values)

    def attend(done):
        state = done[0]
        mixed, log_total = lax.map(
            attend_forward, (state["queries"], state["keys_rot"], state["values"], piece_starts)
        )
        return dict(mixed=mixed, log_total=log_total)

    def out_project(done):
        attended = merge_heads(done[1]["mixed"].astype(jnp.bfloat16))
        return dict(
            attended=attended, attn_partial=product(attended, full_output).astype(jnp.bfloat16)
        )

    cot_later, first_rows = lax.optimization_barrier((cotangent, first_rows))
    cot_ring = RingGather(cot_later, "row")
    projected, attention, mixed_out = overlap(cot_ring, [project, attend, out_project])
    cot_slots = cot_ring.slots
    queries, keys_rot = projected["queries"], projected["keys_rot"]
    values = projected["values"]
    log_total, attended = attention["log_total"], mixed_out["attended"]
    attn_ring = RingScatter(ring_slots(mixed_out["attn_partial"], "row"), "row", jnp.bfloat16)
    cot_count = len(cot_slots)
    per_step = -(-cot_count // attn_ring.steps())

    def cot_grads(index):
        def piece(done):
            chosen = cot_slots[index * per_step : (index + 1) * per_step]
            return tuple(times_transpose(block, full_down) for block in chosen)

        return piece

    grad_act_parts = overlap(attn_ring, [cot_grads(index) for index in range(attn_ring.steps())])
    grad_act_slots = [block for part in grad_act_parts for block in part]
    attention_sum = attn_ring.result()
    middle = inputs + attention_sum
    normed_second = layer_norm(middle).astype(jnp.bfloat16)
    second_ring = RingGather(normed_second, "row")
    slots = second_ring.n

    def ffn_forward(slot):
        def piece(done):
            gu_lin = product(second_ring.slots[slot], full_gu)
            gate_lin = gu_lin[:, :hidden]
            up_lin = gu_lin[:, hidden:]
            activation = (jax.nn.silu(gate_lin) * up_lin).astype(jnp.bfloat16)
            part = product(activation, full_down).astype(jnp.bfloat16)
            return (gate_lin, up_lin, activation, part)

        return piece

    ffn = overlap(second_ring, [ffn_forward(slot) for slot in range(slots)])
    second_slots = second_ring.slots
    gate_slots = [item[0] for item in ffn]
    up_slots = [item[1] for item in ffn]
    act_slots = [item[2] for item in ffn]
    ffn_parts = [item[3] for item in ffn]

    def ffn_backward(slot):
        gate_lin, up_lin = gate_slots[slot], up_slots[slot]
        grad_activation = grad_act_slots[slot]
        sigma = jax.nn.sigmoid(gate_lin)
        grad_gate = grad_activation * up_lin * sigma * (1.0 + gate_lin * (1.0 - sigma))
        grad_up = grad_activation * gate_lin * sigma
        grad_gu = jnp.concatenate([grad_gate, grad_up], axis=1).astype(jnp.bfloat16)
        return (grad_gu, times_transpose(grad_gu, full_gu).astype(jnp.bfloat16))

    second_ring_back = RingScatter([None] * slots, "row", jnp.bfloat16)
    grad_gu_slots = [None] * slots
    order = list(range(1, slots)) + [0]
    grad_gu_slots[order[0]], second_ring_back.slots[order[0]] = ffn_backward(order[0])
    grad_down_w = None
    for index in range(second_ring_back.steps()):
        second_ring_back.send()
        slot = order[index + 1]
        value = ffn_backward(slot)
        if index == 0:
            grad_down_w = contract_rows(
                jnp.concatenate(act_slots, axis=0), jnp.concatenate(cot_slots, axis=0)
            )
            value = value + (grad_down_w,)
        second_ring_back.pending, value = lax.optimization_barrier(
            (second_ring_back.pending, value)
        )
        grad_gu_slots[slot], second_ring_back.slots[slot] = value[0], value[1]
        if index == 0:
            grad_down_w = value[2]
    grad_second = second_ring_back.result()
    down_sum = col_scatter(grad_down_w, 1)
    grad_gu = jnp.concatenate(grad_gu_slots, axis=0)
    rows_second = jnp.concatenate(second_slots, axis=0)
    grad_middle = cotangent.astype(jnp.float32) + norm_back(middle, grad_second)
    branch_chain = RingGather(grad_middle.astype(jnp.bfloat16), "row", absolute=True)
    steps = branch_chain.steps()

    def gate_up_weight_grad(_):
        return contract_rows(rows_second, grad_gu)

    tied = overlap(
        branch_chain, [gate_up_weight_grad] + [lambda done: ()] * (steps - 2) + [lambda done: down_sum]
    )
    grad_gu_w, down_sum = tied[0], tied[-1]
    gu_sum = col_scatter(grad_gu_w, 0)
    grad_branch = branch_chain.result()
    ffn_parts, grad_branch = lax.optimization_barrier((ffn_parts, grad_branch))
    ffn_ring = RingScatter(list(ffn_parts), "row", jnp.bfloat16)
    output_sum = col_scatter(contract_rows(attended, grad_branch), 1)
    half = heads_local // 2

    def heads_backward(lo, hi):
        def piece(done):
            grad_mixed = times_transpose(grad_branch, full_output[lo * HD : hi * HD])
            grad_mixed = grad_mixed.astype(jnp.bfloat16).reshape(seq_count, LENGTH, hi - lo, HD)
            return lax.map(
                attend_backward,
                (
                    queries[:, :, lo:hi],
                    keys_rot[:, :, lo:hi],
                    values[:, :, lo:hi],
                    piece_starts,
                    log_total[:, lo:hi],
                    grad_mixed,
                ),
            )

        return piece

    def finish(done):
        parts = [jnp.concatenate([a[k] for a in done], axis=2) for k in range(3)]
        grad_q_rot, grad_k_rot, grad_values = parts
        grad_qkv = jnp.concatenate(
            [
                merge_heads(unrotate(grad_q_rot, cosine, sine)),
                merge_heads(unrotate(grad_k_rot, cosine, sine)),
                merge_heads(grad_values),
            ],
            axis=1,
        ).astype(jnp.bfloat16)
        return (grad_qkv, times_transpose(grad_qkv, full_qkv).astype(jnp.bfloat16))

    def second_group_and_finish(done):
        return finish(done + (heads_backward(half, heads_local)(done),))

    pieces = [heads_backward(0, half), second_group_and_finish]
    grad_qkv, first_partial = overlap(ffn_ring, pieces)[-1]
    ffn_sum = ffn_ring.result()
    output = (middle + ffn_sum).astype(jnp.bfloat16)
    qkv_sum = col_scatter(contract_rows(first_rows, grad_qkv), 0)
    first_partial, gu_sum = lax.optimization_barrier((first_partial, gu_sum))
    grad_first = ring_reduce_scatter(first_partial, "row", jnp.bfloat16)
    grad_input = grad_middle + norm_back(inputs, grad_first)
    return (
        output,
        grad_input,
        qkv_sum[:, :width],
        qkv_sum[:, width : 2 * width],
        qkv_sum[:, 2 * width :],
        output_sum,
        gu_sum[:, :hidden],
        gu_sum[:, hidden:],
        down_sum,
    )


def solution(mesh):
    in_specs = (
        P(("chip", "core", "row"), None),
        P(COL, "row"),
        P(COL, "row"),
        P(COL, "row"),
        P("row", COL),
        P(COL, "row"),
        P(COL, "row"),
        P("row", COL),
        P(COL, None),
        P(("chip", "core", "row"), None),
    )
    out_specs = (
        P(("chip", "core", "row"), None),
        P(("chip", "core", "row"), None),
        P(COL, "row"),
        P(COL, "row"),
        P(COL, "row"),
        P("row", COL),
        P(COL, "row"),
        P(COL, "row"),
        P("row", COL),
    )
    devices = mesh.devices
    sub_mesh = Mesh(
        devices.reshape(devices.shape[0], devices.shape[1] // 2, 2), ("row", "chip", "core")
    )
    return jax.shard_map(
        per_device_body, mesh=sub_mesh, in_specs=in_specs, out_specs=out_specs, check_vma=False
    )
```

```python
import math

import jax
import jax.numpy as jnp
from jax import lax
from jax.sharding import Mesh, PartitionSpec as P


HD = 128
LENGTH = 1024
PIECE = 256


EPSILON = 1e-05
NEGATIVE = -1e30


def product(left, right):
    return jnp.dot(left, right, preferred_element_type=jnp.float32)


def contract_rows(left, right):
    return lax.dot_general(
        left, right, (((0,), (0,)), ((), ())), preferred_element_type=jnp.float32
    )


def times_transpose(left, right):
    return lax.dot_general(
        left, right, (((1,), (1,)), ((), ())), preferred_element_type=jnp.float32
    )


class GatherSteps:
    def __init__(self, shard, axis):
        self.axis = axis
        self.n = lax.psum(1, axis)
        self.me = lax.axis_index(axis)
        self.rows = shard.shape[0]
        buf = jnp.zeros(((3 * self.n - 2) * self.rows,) + shard.shape[1:], shard.dtype)
        self.buf = lax.dynamic_update_slice_in_dim(buf, shard, (self.me + self.n - 1) * self.rows, 0)
        self.pending = (shard, shard)
        self.step = 0

    def steps(self):
        return self.n - 1

    def send(self):
        n, step = self.n, self.step + 1
        from_left, from_right = self.pending
        from_left = lax.ppermute(from_left, self.axis, [(j, j + 1) for j in range(step - 1, n - 1)])
        from_right = lax.ppermute(from_right, self.axis, [(j, j - 1) for j in range(1, n - step + 1)])
        self.pending = (from_left, from_right)
        self.step = step

    def land(self):
        n, step, rows = self.n, self.step, self.rows
        from_left, from_right = self.pending
        self.buf = lax.dynamic_update_slice_in_dim(self.buf, from_left, (self.me - step + n - 1) * rows, 0)
        self.buf = lax.dynamic_update_slice_in_dim(self.buf, from_right, (self.me + step + n - 1) * rows, 0)

    def result(self):
        return self.buf[(self.n - 1) * self.rows : (2 * self.n - 1) * self.rows]


class ScatterSteps:
    def __init__(self, partial, axis, send_dtype):
        self.axis = axis
        self.n = lax.psum(1, axis)
        self.me = lax.axis_index(axis)
        self.rows = partial.shape[0] // self.n
        self.partial = partial
        self.send_dtype = send_dtype
        self.pending = None
        self.step = 0

    def steps(self):
        return self.n - 1

    def block(self, k):
        return lax.dynamic_slice_in_dim(
            self.partial, jnp.clip(k, 0, self.n - 1) * self.rows, self.rows, 0
        )

    def send(self):
        n, me, step = self.n, self.me, self.step + 1
        send_right = self.block(n - step + me)
        send_left = self.block(me + step - n)
        if self.pending is not None:
            send_right = send_right + self.pending[0].astype(jnp.float32)
            send_left = send_left + self.pending[1].astype(jnp.float32)
        recv_right = lax.ppermute(
            send_right.astype(self.send_dtype), self.axis, [(j, j + 1) for j in range(0, step)]
        )
        recv_left = lax.ppermute(
            send_left.astype(self.send_dtype), self.axis, [(j, j - 1) for j in range(n - step, n)]
        )
        self.pending = (recv_right, recv_left)
        self.step = step

    def land(self):
        pass

    def result(self):
        return (
            self.block(self.me)
            + self.pending[0].astype(jnp.float32)
            + self.pending[1].astype(jnp.float32)
        )


class RingGather:
    def __init__(self, shard, axis, absolute=False):
        self.axis = axis
        self.n = lax.psum(1, axis)
        self.me = lax.axis_index(axis)
        self.rows = shard.shape[0]
        self.slots = [shard]
        self.pending = shard
        self.absolute = absolute
        self.buf = None

    def place(self, buf, block, slot):
        start = lax.rem(self.me - slot + self.n, self.n) * self.rows
        return lax.dynamic_update_slice_in_dim(buf, block, start, 0)

    def steps(self):
        return self.n - 1

    def send(self):
        n = self.n
        self.pending = lax.ppermute(self.pending, self.axis, [(j, (j + 1) % n) for j in range(n)])

    def land(self):
        self.slots.append(self.pending)
        if self.absolute:
            if self.buf is None:
                shard = self.slots[0]
                buf = jnp.zeros((self.n * self.rows,) + shard.shape[1:], shard.dtype)
                self.buf = self.place(buf, shard, 0)
            self.buf = self.place(self.buf, self.pending, len(self.slots) - 1)

    def result(self):
        return self.buf


class RingScatter:
    def __init__(self, slots, axis, send_dtype):
        self.axis = axis
        self.n = lax.psum(1, axis)
        self.slots = slots
        self.send_dtype = send_dtype
        self.pending = None
        self.step = 0

    def steps(self):
        return self.n - 1

    def send(self):
        n, step = self.n, self.step + 1
        value = self.slots[step].astype(jnp.float32)
        if self.pending is not None:
            value = value + self.pending.astype(jnp.float32)
        self.pending = lax.ppermute(
            value.astype(self.send_dtype), self.axis, [(j, (j + 1) % n) for j in range(n)]
        )
        self.step = step

    def land(self):
        pass

    def result(self):
        return self.slots[0].astype(jnp.float32) + self.pending.astype(jnp.float32)


def ring_slots(partial, axis):
    n = lax.psum(1, axis)
    me = lax.axis_index(axis)
    rows = partial.shape[0] // n
    return [
        lax.dynamic_slice_in_dim(partial, lax.rem(me - slot + n, n) * rows, rows, 0)
        for slot in range(n)
    ]


def ring_all_gather(shard, axis):
    chain = RingGather(shard, axis, absolute=True)
    overlap(chain, [])
    return chain.result()


def ring_reduce_scatter(partial, axis, send_dtype):
    chain = RingScatter(ring_slots(partial, axis), axis, send_dtype)
    overlap(chain, [])
    return chain.result()


def overlap(chain, pieces):
    outputs = []
    count = chain.steps()
    for index in range(count):
        chain.send()
        if index < len(pieces):
            value = pieces[index](tuple(outputs))
            chain.pending, value = lax.optimization_barrier((chain.pending, value))
            outputs.append(value)
        else:
            chain.pending = lax.optimization_barrier(chain.pending)
        chain.land()
    for piece in pieces[count:]:
        outputs.append(piece(tuple(outputs)))
    return tuple(outputs)


COL = ("chip", "core")


def col_gather(block, axis):
    return lax.all_gather(block, COL, axis=axis, tiled=True)


def col_scatter(partial, axis):
    low_part = partial.astype(jnp.bfloat16)
    return lax.psum_scatter(low_part, COL, scatter_dimension=axis, tiled=True).astype(jnp.float32)


def layer_norm(inputs):
    center = inputs - jnp.mean(inputs, axis=-1, keepdims=True)
    spread = jnp.mean(center * center, axis=-1, keepdims=True)
    return center * lax.rsqrt(spread + EPSILON)


def norm_back(inputs, grad):
    center = inputs - jnp.mean(inputs, axis=-1, keepdims=True)
    inverse = lax.rsqrt(jnp.mean(center * center, axis=-1, keepdims=True) + EPSILON)
    normed = center * inverse
    return inverse * (
        grad
        - jnp.mean(grad, axis=-1, keepdims=True)
        - normed * jnp.mean(grad * normed, axis=-1, keepdims=True)
    )


def rope_tables():
    positions = jnp.arange(LENGTH, dtype=jnp.float32)
    freqs = jnp.power(jnp.float32(10000.0), -jnp.arange(HD // 2, dtype=jnp.float32) * (2.0 / HD))
    angles = positions[:, None] * freqs[None, :]
    return (jnp.cos(angles)[:, None, :], jnp.sin(angles)[:, None, :])


def rotate(field, cosine, sine):
    half_size = field.shape[-1] // 2
    first_half = field[..., :half_size]
    second_half = field[..., half_size:]
    return jnp.concatenate(
        [first_half * cosine - second_half * sine, second_half * cosine + first_half * sine],
        axis=-1,
    )


def unrotate(field, cosine, sine):
    half_size = field.shape[-1] // 2
    first_half = field[..., :half_size]
    second_half = field[..., half_size:]
    return jnp.concatenate(
        [first_half * cosine + second_half * sine, second_half * cosine - first_half * sine],
        axis=-1,
    )


def piece_mask(starts):
    positions = jnp.arange(LENGTH, dtype=jnp.int32)
    inside = (positions[None, :] >= starts[:, None]) & (
        positions[None, :] < starts[:, None] + PIECE
    )
    shared = jnp.any(inside[:, :, None] & inside[:, None, :], axis=0)
    causal = positions[None, :] <= positions[:, None]
    return causal | shared


def masked_scores(queries, keys_rot, starts):
    scale = 1.0 / math.sqrt(HD)
    scores = (
        jnp.einsum("qhd,khd->hqk", queries, keys_rot, preferred_element_type=jnp.float32) * scale
    )
    return jnp.where(piece_mask(starts)[None], scores, NEGATIVE)


def attend_forward(operands):
    queries, keys_rot, values, starts = operands
    scores = masked_scores(queries, keys_rot, starts)
    row_top = jnp.max(scores, axis=-1, keepdims=True)
    shifted = jnp.exp(scores - row_top)
    row_total = jnp.sum(shifted, axis=-1, keepdims=True)
    probs = (shifted / row_total).astype(jnp.bfloat16)
    mixed = jnp.einsum("hqk,khd->qhd", probs, values, preferred_element_type=jnp.float32)
    return (mixed, row_top + jnp.log(row_total))


def attend_backward(operands):
    queries, keys_rot, values, starts, log_total, grad_mixed = operands
    scale = 1.0 / math.sqrt(HD)
    scores = masked_scores(queries, keys_rot, starts)
    probs = jnp.exp(scores - log_total)
    probs_low = probs.astype(jnp.bfloat16)
    grad_values = jnp.einsum(
        "hqk,qhd->khd", probs_low, grad_mixed, preferred_element_type=jnp.float32
    )
    grad_probs = jnp.einsum("qhd,khd->hqk", grad_mixed, values, preferred_element_type=jnp.float32)
    inner = jnp.sum(probs * grad_probs, axis=-1, keepdims=True)
    grad_scores = (probs * (grad_probs - inner)).astype(jnp.bfloat16)
    grad_queries = (
        jnp.einsum("hqk,khd->qhd", grad_scores, keys_rot, preferred_element_type=jnp.float32)
        * scale
    )
    grad_keys = (
        jnp.einsum("hqk,qhd->khd", grad_scores, queries, preferred_element_type=jnp.float32) * scale
    )
    return (grad_queries, grad_keys, grad_values)


def per_device_body(
    layer_input, w_query, w_key, w_value, w_output, w_gate, w_up, w_down, piece_starts, cotangent
):
    seq_count = piece_starts.shape[0]
    group_rows = seq_count * LENGTH
    width = w_query.shape[1]
    hidden = w_gate.shape[1]
    heads_local = width // HD
    full_qkv = col_gather(jnp.concatenate([w_query, w_key, w_value], axis=1), 0)
    full_output = col_gather(w_output, 1)
    full_gu = col_gather(jnp.concatenate([w_gate, w_up], axis=1), 0)
    full_down = col_gather(w_down, 1)
    cosine, sine = rope_tables()
    inputs = layer_input.astype(jnp.float32)
    normed_first = layer_norm(inputs).astype(jnp.bfloat16)
    first_rows = ring_all_gather(normed_first, "row")

    def split_heads(matrix):
        return matrix.reshape(seq_count, LENGTH, heads_local, HD)

    def merge_heads(field):
        return field.reshape(group_rows, heads_local * HD)

    def project(_):
        qkv_lin = product(first_rows, full_qkv)
        queries = rotate(split_heads(qkv_lin[:, :width]), cosine, sine).astype(jnp.bfloat16)
        keys_rot = rotate(split_heads(qkv_lin[:, width : 2 * width]), cosine, sine).astype(
            jnp.bfloat16
        )
        values = split_heads(qkv_lin[:, 2 * width :]).astype(jnp.bfloat16)
        return dict(queries=queries, keys_rot=keys_rot, values=values)

    def attend(done):
        state = done[0]
        mixed, log_total = lax.map(
            attend_forward, (state["queries"], state["keys_rot"], state["values"], piece_starts)
        )
        return dict(mixed=mixed, log_total=log_total)

    def out_project(done):
        attended = merge_heads(done[1]["mixed"].astype(jnp.bfloat16))
        return dict(
            attended=attended, attn_partial=product(attended, full_output).astype(jnp.bfloat16)
        )

    cot_later, first_rows = lax.optimization_barrier((cotangent, first_rows))
    cot_ring = RingGather(cot_later, "row")
    projected, attention, mixed_out = overlap(cot_ring, [project, attend, out_project])
    cot_slots = cot_ring.slots
    queries, keys_rot = projected["queries"], projected["keys_rot"]
    values = projected["values"]
    log_total, attended = attention["log_total"], mixed_out["attended"]
    attn_ring = RingScatter(ring_slots(mixed_out["attn_partial"], "row"), "row", jnp.bfloat16)
    cot_count = len(cot_slots)
    per_step = -(-cot_count // attn_ring.steps())

    def cot_grads(index):
        def piece(done):
            chosen = cot_slots[index * per_step : (index + 1) * per_step]
            return tuple(times_transpose(block, full_down) for block in chosen)

        return piece

    grad_act_parts = overlap(attn_ring, [cot_grads(index) for index in range(attn_ring.steps())])
    grad_act_slots = [block for part in grad_act_parts for block in part]
    attention_sum = attn_ring.result()
    middle = inputs + attention_sum
    normed_second = layer_norm(middle).astype(jnp.bfloat16)
    second_ring = RingGather(normed_second, "row")
    slots = second_ring.n

    def ffn_forward(slot):
        def piece(done):
            gu_lin = product(second_ring.slots[slot], full_gu)
            gate_lin = gu_lin[:, :hidden]
            up_lin = gu_lin[:, hidden:]
            activation = (jax.nn.silu(gate_lin) * up_lin).astype(jnp.bfloat16)
            part = product(activation, full_down).astype(jnp.bfloat16)
            return (gate_lin, up_lin, activation, part)

        return piece

    ffn = overlap(second_ring, [ffn_forward(slot) for slot in range(slots)])
    second_slots = second_ring.slots
    gate_slots = [item[0] for item in ffn]
    up_slots = [item[1] for item in ffn]
    act_slots = [item[2] for item in ffn]
    ffn_parts = [item[3] for item in ffn]

    def ffn_backward(slot):
        gate_lin, up_lin = gate_slots[slot], up_slots[slot]
        grad_activation = grad_act_slots[slot]
        sigma = jax.nn.sigmoid(gate_lin)
        grad_gate = grad_activation * up_lin * sigma * (1.0 + gate_lin * (1.0 - sigma))
        grad_up = grad_activation * gate_lin * sigma
        grad_gu = jnp.concatenate([grad_gate, grad_up], axis=1).astype(jnp.bfloat16)
        return (grad_gu, times_transpose(grad_gu, full_gu).astype(jnp.bfloat16))

    second_ring_back = RingScatter([None] * slots, "row", jnp.bfloat16)
    grad_gu_slots = [None] * slots
    order = list(range(1, slots)) + [0]
    grad_gu_slots[order[0]], second_ring_back.slots[order[0]] = ffn_backward(order[0])
    grad_down_w = None
    for index in range(second_ring_back.steps()):
        second_ring_back.send()
        slot = order[index + 1]
        value = ffn_backward(slot)
        if index == 0:
            grad_down_w = contract_rows(
                jnp.concatenate(act_slots, axis=0), jnp.concatenate(cot_slots, axis=0)
            )
            value = value + (grad_down_w,)
        second_ring_back.pending, value = lax.optimization_barrier(
            (second_ring_back.pending, value)
        )
        grad_gu_slots[slot], second_ring_back.slots[slot] = value[0], value[1]
        if index == 0:
            grad_down_w = value[2]
    grad_second = second_ring_back.result()
    down_sum = col_scatter(grad_down_w, 1)
    grad_gu = jnp.concatenate(grad_gu_slots, axis=0)
    rows_second = jnp.concatenate(second_slots, axis=0)
    grad_middle = cotangent.astype(jnp.float32) + norm_back(middle, grad_second)
    branch_chain = RingGather(grad_middle.astype(jnp.bfloat16), "row", absolute=True)
    steps = branch_chain.steps()

    def gate_up_weight_grad(_):
        return contract_rows(rows_second, grad_gu)

    tied = overlap(
        branch_chain, [gate_up_weight_grad] + [lambda done: ()] * (steps - 2) + [lambda done: down_sum]
    )
    grad_gu_w, down_sum = tied[0], tied[-1]
    gu_sum = col_scatter(grad_gu_w, 0)
    grad_branch = branch_chain.result()
    ffn_parts, grad_branch = lax.optimization_barrier((ffn_parts, grad_branch))
    ffn_ring = RingScatter(list(ffn_parts), "row", jnp.bfloat16)
    output_sum = col_scatter(contract_rows(attended, grad_branch), 1)
    half = heads_local // 2

    def heads_backward(lo, hi):
        def piece(done):
            grad_mixed = times_transpose(grad_branch, full_output[lo * HD : hi * HD])
            grad_mixed = grad_mixed.astype(jnp.bfloat16).reshape(seq_count, LENGTH, hi - lo, HD)
            return lax.map(
                attend_backward,
                (
                    queries[:, :, lo:hi],
                    keys_rot[:, :, lo:hi],
                    values[:, :, lo:hi],
                    piece_starts,
                    log_total[:, lo:hi],
                    grad_mixed,
                ),
            )

        return piece

    def finish(done):
        parts = [jnp.concatenate([a[k] for a in done], axis=2) for k in range(3)]
        grad_q_rot, grad_k_rot, grad_values = parts
        grad_qkv = jnp.concatenate(
            [
                merge_heads(unrotate(grad_q_rot, cosine, sine)),
                merge_heads(unrotate(grad_k_rot, cosine, sine)),
                merge_heads(grad_values),
            ],
            axis=1,
        ).astype(jnp.bfloat16)
        return (grad_qkv, times_transpose(grad_qkv, full_qkv).astype(jnp.bfloat16))

    def second_group_and_finish(done):
        return finish(done + (heads_backward(half, heads_local)(done),))

    pieces = [heads_backward(0, half), second_group_and_finish]
    grad_qkv, first_partial = overlap(ffn_ring, pieces)[-1]
    ffn_sum = ffn_ring.result()
    output = (middle + ffn_sum).astype(jnp.bfloat16)
    qkv_sum = col_scatter(contract_rows(first_rows, grad_qkv), 0)
    first_partial, gu_sum = lax.optimization_barrier((first_partial, gu_sum))
    grad_first = ring_reduce_scatter(first_partial, "row", jnp.bfloat16)
    grad_input = grad_middle + norm_back(inputs, grad_first)
    return (
        output,
        grad_input,
        qkv_sum[:, :width],
        qkv_sum[:, width : 2 * width],
        qkv_sum[:, 2 * width :],
        output_sum,
        gu_sum[:, :hidden],
        gu_sum[:, hidden:],
        down_sum,
    )


def solution(mesh):
    in_specs = (
        P(("chip", "core", "row"), None),
        P(COL, "row"),
        P(COL, "row"),
        P(COL, "row"),
        P("row", COL),
        P(COL, "row"),
        P(COL, "row"),
        P("row", COL),
        P(COL, None),
        P(("chip", "core", "row"), None),
    )
    out_specs = (
        P(("chip", "core", "row"), None),
        P(("chip", "core", "row"), None),
        P(COL, "row"),
        P(COL, "row"),
        P(COL, "row"),
        P("row", COL),
        P(COL, "row"),
        P(COL, "row"),
        P("row", COL),
    )
    devices = mesh.devices
    sub_mesh = Mesh(
        devices.reshape(devices.shape[0], devices.shape[1] // 2, 2), ("row", "chip", "core")
    )
    return jax.shard_map(
        per_device_body, mesh=sub_mesh, in_specs=in_specs, out_specs=out_specs, check_vma=False
    )
```
